32 devices in a mesh: dp: 8 (over y, x, core), tensor: 4 (over z).
Axes of the slice: x: 2, y: 2, z: 4, core: 2. Of those that a mesh axis runs over, the one named last changes fastest.
Arguments:
- inputs: bfloat16 [16384, 768], P(('dp', 'tensor')), may hold values from -6 to 6
- cotangent: bfloat16 [16384, 768], P(('dp', 'tensor')), may hold values from -6 to 6
- lengths: int32 [128], P('dp'), may hold values from 25 to 128
- block_kind: int32 [32], P('dp'), may hold values from 0 to 1
- w_qkv: bfloat16 [2, 3, 768, 768], P(None, None, None, 'tensor'), may hold values from -0.3125 to 0.3125
- qv_bias: bfloat16 [2, 2, 768], P(None, None, 'tensor'), may hold values from -3 to 3
- w_out: bfloat16 [2, 768, 768], P(None, 'tensor'), may hold values from -0.625 to 0.625
- resid_bias: bfloat16 [2, 2, 768], replicated, may hold values from -3 to 3
- norm_gain: bfloat16 [2, 2, 768], replicated, may hold values from 0.5 to 1.5
- norm_shift: bfloat16 [2, 2, 768], replicated, may hold values from -2 to 2
- w_up: bfloat16 [2, 768, 3072], P(None, None, 'tensor'), may hold values from -0.21875 to 0.21875
- up_bias: bfloat16 [2, 3072], P(None, 'tensor'), may hold values from -3 to 3
- w_down: bfloat16 [2, 3072, 768], P(None, 'tensor'), may hold values from -0.15625 to 0.15625
Outputs:
- layer_out: bfloat16 [16384, 768], P(('dp', 'tensor'))
- input_grad: float32 [16384, 768], P(('dp', 'tensor'))
- grad_w_qkv: float32 [2, 3, 768, 768], P(None, None, None, 'tensor')
- grad_qv_bias: float32 [2, 2, 768], P(None, None, 'tensor')
- grad_w_out: float32 [2, 768, 768], P(None, 'tensor')
- grad_resid_bias: float32 [2, 2, 768], replicated
- grad_norm_gain: float32 [2, 2, 768], replicated
- grad_norm_shift: float32 [2, 2, 768], replicated
- grad_w_up: float32 [2, 768, 3072], P(None, None, 'tensor')
- grad_up_bias: float32 [2, 3072], P(None, 'tensor')
- grad_w_down: float32 [2, 3072, 768], P(None, 'tensor')
The draws below stay inside these ranges and needn't reach their ends.
Inputs may be any that keep to these rules, and one draw needn't show every extreme that they name: lengths[s] is the number of real tokens of chain s; positions from lengths[s] on are padding and are never attended to. `block_kind`: block b holds chains b * 4 to (b+1) * 4 - 1, all heavy (0) or all light (1).
All inputs are finite; a program needn't handle non-finite values.
Results may differ from the reference program's by a relative error of at most 0.019.
The reference program's roundings to bfloat16 on the way count: a program that leaves them out, or rounds other values in their place, can miss the bound.
Values may be sent and summed in bfloat16 or wider, within the bound.
No kernel may reach another device: no remote copies, remote signals or barrier semaphores. Data moves between devices by JAX's collectives and lax.ppermute only.
A program may use at most 128 MiB of HBM per device.

```python
import jax
import jax.numpy as jnp
from jax import lax

D = 768
HEADS = 12
HEAD_DIM = 64
FF = 3072
CHAIN = 128
BLOCK_SEQS = 4
TYPES = 2
TOKENS = 16384
SEQS = 128
BLOCKS = 32


def plant(drawn, key, smallest, largest):
    shape = drawn.shape
    place = [jax.random.randint(jax.random.fold_in(key, axis), (), 0, shape[axis]) for axis in range(len(shape))]
    drawn = drawn.at[tuple(place)].set(smallest)
    longest = shape.index(max(shape))
    place[longest] = (place[longest] + 1) % shape[longest]
    return drawn.at[tuple(place)].set(largest)


def level_of(stream_key, extent, cuts, least, high):
    factor_of = 1.0
    for dim, blocks in cuts:
        draws = jax.random.uniform(jax.random.fold_in(jax.random.fold_in(stream_key, 6), dim), (blocks,), jnp.float32, least / len(cuts), high / len(cuts))
        factor_of = factor_of * jnp.repeat(jnp.exp(draws), extent[dim] // blocks).reshape((-1,) + (1,) * (len(extent) - 1 - dim))
    return factor_of


def scatter_about(own_key, extent, width, limit, split=(), dtype=jnp.bfloat16):
    drawn = jax.random.normal(own_key, extent, jnp.float32) * width
    if len(split) > 0:
        drawn = level_of(own_key, extent, split, -0.22, 0.18) * drawn
    return jnp.clip(drawn, min=-limit, max=limit).astype(dtype)


def setup_inputs(seed: int = 0) -> dict:
    key_list = jax.random.split(jax.random.key(seed), 14)
    return {
        "inputs": scatter_about(key_list[0], (TOKENS, D), 1.0, 6.0, ((0, 32),)),
        "cotangent": scatter_about(key_list[1], (TOKENS, D), 1.0, 6.0, ((0, 32),)),
        "lengths": plant(jax.random.randint(key_list[2], (SEQS,), max(1, CHAIN // 5), CHAIN + 1), jax.random.fold_in(key_list[2], 1), max(1, CHAIN // 5), CHAIN).astype(jnp.int32),
        "block_kind": plant(jax.random.randint(key_list[3], (BLOCKS,), 0, 2), jax.random.fold_in(key_list[3], 1), 0, 1).astype(jnp.int32),
        "w_qkv": scatter_about(key_list[4], (TYPES, 3, D, D), (D // 2) ** -0.5, 0.3125, ((3, 4),)),
        "qv_bias": scatter_about(key_list[5], (TYPES, 2, D), 0.5, 3.0, ((2, 4),)),
        "w_out": scatter_about(key_list[6], (TYPES, D, D), (D // 8) ** -0.5, 0.625, ((1, 4),)),
        "resid_bias": scatter_about(key_list[7], (TYPES, 2, D), 0.5, 3.0),
        "norm_gain": jnp.clip(1.0 + 0.1 * jax.random.normal(key_list[8], (TYPES, 2, D), jnp.float32), 0.5, 1.5).astype(jnp.bfloat16),
        "norm_shift": scatter_about(key_list[9], (TYPES, 2, D), 0.3, 2.0),
        "w_up": scatter_about(key_list[10], (TYPES, D, FF), D ** -0.5, 0.21875, ((2, 4),)),
        "up_bias": scatter_about(key_list[11], (TYPES, FF), 0.5, 3.0, ((1, 4),)),
        "w_down": scatter_about(key_list[12], (TYPES, FF, D), (FF // 2) ** -0.5, 0.15625, ((1, 4),)),
    }


@jax.custom_vjp
def low(v):
    return lax.optimization_barrier(v.astype(jnp.bfloat16)).astype(jnp.float32)

@jax.custom_vjp
def low_back(v):
    return v

def low_keep(v):
    return (low(v), None)

def low_pass(kept, grad):
    return (grad,)

def back_keep(v):
    return (v, None)

def back_low(kept, grad):
    return (low(grad),)
low.defvjp(low_keep, low_pass)
low_back.defvjp(back_keep, back_low)

def matmul(left_mat, right_mat):
    return jnp.dot(left_mat, right_mat, precision=lax.Precision.HIGHEST)

def heads_of(row_data):
    return row_data.reshape(BLOCK_SEQS, CHAIN, HEADS, HEAD_DIM)

def layer_norm(row_data, gain_row, shift_row):
    mean_row = lax.optimization_barrier(jnp.mean(row_data, axis=-1, keepdims=True))
    centred = row_data - mean_row
    var_row = lax.optimization_barrier(jnp.mean(centred * centred, axis=-1, keepdims=True))
    return centred * lax.rsqrt(var_row + 1e-05) * gain_row + shift_row

def block_forward(params, row_data, seq_lens, block_type):
    w_qkv, qv_bias, w_out, resid_bias, norm_gain, norm_shift, w_up, up_bias, w_down = [param[block_type] for param in params]
    query_rows = low_back(low(matmul(row_data, w_qkv[0]) + qv_bias[0]))
    key_rows = low_back(low(matmul(row_data, w_qkv[1])))
    value_rows = low_back(low(matmul(row_data, w_qkv[2]) + qv_bias[1]))
    raw_scores = jnp.einsum('sqhd,skhd->shqk', heads_of(query_rows), heads_of(key_rows), precision=lax.Precision.HIGHEST) * HEAD_DIM ** (-0.5)
    key_valid = jnp.arange(CHAIN)[None, :] < seq_lens[:, None]
    scores = low_back(jnp.where(key_valid[:, None, None, :], raw_scores, -1e+30))
    attn_probs = jax.nn.softmax(scores, axis=-1)
    mixed = jnp.einsum('shqk,skhd->sqhd', low(attn_probs), heads_of(value_rows), precision=lax.Precision.HIGHEST)
    mixed = low_back(low(mixed.reshape(row_data.shape[0], D)))
    attn_out = low_back(matmul(mixed, w_out))
    hidden_one = row_data + attn_out + resid_bias[0]
    normed = layer_norm(hidden_one, norm_gain[0], norm_shift[0])
    pre_act = low_back(matmul(low(normed), w_up) + up_bias)
    activ = low_back(low(jax.nn.gelu(pre_act, approximate=False)))
    ffn_out = low_back(matmul(activ, w_down))
    hidden_two = normed + ffn_out + resid_bias[1]
    return layer_norm(hidden_two, norm_gain[1], norm_shift[1])

def reference(inputs, cotangent, lengths, block_kind, w_qkv, qv_bias, w_out, resid_bias, norm_gain, norm_shift, w_up, up_bias, w_down):
    params = tuple((param.astype(jnp.float32) for param in (w_qkv, qv_bias, w_out, resid_bias, norm_gain, norm_shift, w_up, up_bias, w_down)))
    row_data = inputs.astype(jnp.float32).reshape(BLOCKS, BLOCK_SEQS * CHAIN, D)
    seq_lens = lengths.reshape(BLOCKS, BLOCK_SEQS)

    def forward(weights, data):

        def one_block(packed):
            return block_forward(weights, packed[0], packed[1], packed[2])
        return lax.map(jax.checkpoint(one_block), (data, seq_lens, block_kind))
    layer_out, pullback = jax.vjp(forward, params, row_data)
    weight_grads, input_grad = pullback(cotangent.astype(jnp.float32).reshape(BLOCKS, BLOCK_SEQS * CHAIN, D))
    return (layer_out.reshape(TOKENS, D).astype(jnp.bfloat16), input_grad.reshape(TOKENS, D), weight_grads[0], weight_grads[1], weight_grads[2], weight_grads[3], weight_grads[4], weight_grads[5], weight_grads[6], weight_grads[7], weight_grads[8])
```

```python
import jax
import jax.numpy as jnp
from jax import lax
from jax.sharding import PartitionSpec as P

HEAD_DIM = 64
CHAIN = 128
BLOCK_SEQS = 4


EPSILON = 1e-05
SQRT_HALF = 0.7071067811865476
INV_ROOT_TWO_PI = 0.3989422804014327


def norm_forward(row_data, gain_rows, shift_rows):
    mean_row = jnp.mean(row_data, axis=-1, keepdims=True)
    centred = row_data - mean_row
    var_row = jnp.mean(centred * centred, axis=-1, keepdims=True)
    inv_std = lax.rsqrt(var_row + EPSILON)
    unit_rows = centred * inv_std
    return (unit_rows * gain_rows + shift_rows, unit_rows, inv_std)


def norm_backward(grad_rows, gain_rows, unit_rows, inv_std):
    scaled = grad_rows * gain_rows
    mean_first = jnp.mean(scaled, axis=-1, keepdims=True)
    mean_second = jnp.mean(scaled * unit_rows, axis=-1, keepdims=True)
    return inv_std * (scaled - mean_first - unit_rows * mean_second)


def type_sum(kind_hot, values):
    return jnp.einsum("rt,rd->td", kind_hot, values, precision=lax.Precision.HIGHEST)


def gelu_slope(values):
    return 0.5 * (1.0 + lax.erf(values * SQRT_HALF)) + values * INV_ROOT_TWO_PI * jnp.exp(
        -0.5 * values * values
    )


def split_heads(row_data, heads_here):
    return row_data.reshape(BLOCK_SEQS, CHAIN, heads_here, HEAD_DIM)


def ffn_apply(up_w, ubias_w, down_w, row_blocks, kinds):

    def step(carry, packed):
        row_data, block_type = packed
        pre_act = jnp.dot(row_data, up_w[block_type], preferred_element_type=jnp.float32) + ubias_w[
            block_type
        ].astype(jnp.float32)
        activ = jax.nn.gelu(pre_act, approximate=False).astype(jnp.bfloat16)
        return (
            carry,
            (
                pre_act,
                activ,
                jnp.dot(activ, down_w[block_type], preferred_element_type=jnp.float32),
            ),
        )

    return lax.scan(step, 0, (row_blocks, kinds))[1]


def ffn_grad(up_w, ubias_w, down_w, row_blocks, grad_blocks, pre_blocks, activ_blocks, kinds):

    def step(accums, packed):
        acc_up, acc_ubias, acc_down = accums
        row_data, grad_rows, pre_act, activ, block_type = packed
        acc_down = acc_down.at[block_type].add(
            jnp.einsum("rf,rd->fd", activ, grad_rows, preferred_element_type=jnp.float32)
        )
        d_activ = jnp.einsum(
            "rd,fd->rf", grad_rows, down_w[block_type], preferred_element_type=jnp.float32
        ).astype(jnp.bfloat16)
        d_pre = (d_activ.astype(jnp.float32) * gelu_slope(pre_act)).astype(jnp.bfloat16)
        acc_up = acc_up.at[block_type].add(
            jnp.einsum("rd,rf->df", row_data, d_pre, preferred_element_type=jnp.float32)
        )
        acc_ubias = acc_ubias.at[block_type].add(jnp.sum(d_pre.astype(jnp.float32), axis=0))
        partial_back = jnp.einsum(
            "rf,df->rd", d_pre, up_w[block_type], preferred_element_type=jnp.float32
        )
        return ((acc_up, acc_ubias, acc_down), partial_back)

    zeros_ffn = (
        jnp.zeros(up_w.shape, jnp.float32),
        jnp.zeros(ubias_w.shape, jnp.float32),
        jnp.zeros(down_w.shape, jnp.float32),
    )
    return lax.scan(step, zeros_ffn, (row_blocks, grad_blocks, pre_blocks, activ_blocks, kinds))


def local(
    inputs,
    cotangent,
    lengths,
    block_kind,
    w_qkv,
    qv_bias,
    w_out,
    resid_bias,
    norm_gain,
    norm_shift,
    w_up,
    up_bias,
    w_down,
):
    tok_dev = inputs.shape[0]
    group_rows = tok_dev * lax.axis_size("tensor")
    block_rows = BLOCK_SEQS * CHAIN
    n_blocks = group_rows // block_rows
    heads_here = w_qkv.shape[3] // HEAD_DIM
    score_scale = HEAD_DIM ** (-0.5)
    highest = lax.Precision.HIGHEST
    row_block = (lax.axis_index("tensor") * tok_dev + jnp.arange(tok_dev)) // block_rows
    block_hot = row_block[:, None] == jnp.arange(n_blocks)[None, :]
    row_kind = jnp.sum(jnp.where(block_hot, block_kind[None, :], 0), axis=1)
    kind_hot = (row_kind[:, None] == jnp.arange(2)[None, :]).astype(jnp.float32)

    def pick(kind_table):
        return jnp.dot(kind_hot, kind_table.astype(jnp.float32), precision=highest)

    key_valid = jnp.arange(CHAIN)[None, :] < lengths[:, None]
    valid_blocks = key_valid.reshape(n_blocks, BLOCK_SEQS, CHAIN)

    def scores_of(query_rows, key_rows, valid_keys):
        raw_scores = (
            jnp.einsum(
                "sqhd,skhd->shqk",
                split_heads(query_rows, heads_here),
                split_heads(key_rows, heads_here),
                preferred_element_type=jnp.float32,
            )
            * score_scale
        )
        return jnp.where(valid_keys[:, None, None, :], raw_scores, -1e30)

    gathered = lax.all_gather(inputs, "tensor", axis=0, tiled=True)
    input_blocks = gathered.reshape(n_blocks, block_rows, -1)

    def attend_forward(accums, packed):
        row_data, valid_keys, block_type = packed
        projected = jnp.einsum(
            "rd,jde->jre", row_data, w_qkv[block_type], preferred_element_type=jnp.float32
        )
        bias_pair = qv_bias[block_type].astype(jnp.float32)
        query_rows = (projected[0] + bias_pair[0]).astype(jnp.bfloat16)
        key_rows = projected[1].astype(jnp.bfloat16)
        value_rows = (projected[2] + bias_pair[1]).astype(jnp.bfloat16)
        scores = scores_of(query_rows, key_rows, valid_keys)
        row_max = jnp.max(scores, axis=-1, keepdims=True)
        log_total = row_max[..., 0] + jnp.log(jnp.sum(jnp.exp(scores - row_max), axis=-1))
        attn_probs = jnp.exp(scores - log_total[..., None]).astype(jnp.bfloat16)
        mixed = jnp.einsum(
            "shqk,skhd->sqhd",
            attn_probs,
            split_heads(value_rows, heads_here),
            preferred_element_type=jnp.float32,
        )
        mixed = mixed.reshape(block_rows, -1).astype(jnp.bfloat16)
        partial_out = jnp.dot(mixed, w_out[block_type], preferred_element_type=jnp.float32)
        return (
            accums,
            (jnp.stack([query_rows, key_rows, value_rows]), log_total, mixed, partial_out),
        )

    unused, (kept_proj, kept_total, kept_mixed, attn_parts) = lax.scan(
        attend_forward, 0, (input_blocks, valid_blocks, block_kind)
    )
    attn_rows = lax.psum_scatter(
        attn_parts.reshape(group_rows, -1), "tensor", scatter_dimension=0, tiled=True
    )
    hidden_one = inputs.astype(jnp.float32) + attn_rows + pick(resid_bias[:, 0])
    gain_one = pick(norm_gain[:, 0])
    normed, unit_one, inv_one = norm_forward(hidden_one, gain_one, pick(norm_shift[:, 0]))
    normed_low = normed.astype(jnp.bfloat16)
    gathered_norm = lax.all_gather(normed_low, "tensor", axis=0, tiled=True)
    norm_blocks = gathered_norm.reshape(n_blocks, block_rows, -1)
    kept_pre, kept_activ, ffn_parts = ffn_apply(w_up, up_bias, w_down, norm_blocks, block_kind)
    ffn_rows = lax.psum_scatter(
        ffn_parts.reshape(group_rows, -1).astype(jnp.bfloat16),
        "tensor",
        scatter_dimension=0,
        tiled=True,
    ).astype(jnp.float32)
    hidden_two = normed + ffn_rows + pick(resid_bias[:, 1])
    gain_two = pick(norm_gain[:, 1])
    output_rows, unit_two, inv_two = norm_forward(hidden_two, gain_two, pick(norm_shift[:, 1]))
    layer_out = output_rows.astype(jnp.bfloat16)
    grad_out = cotangent.astype(jnp.float32)
    d_two = norm_backward(grad_out, gain_two, unit_two, inv_two)
    d_two_low = d_two.astype(jnp.bfloat16)
    gathered_two = lax.all_gather(d_two_low, "tensor", axis=0, tiled=True)
    two_blocks = gathered_two.reshape(n_blocks, block_rows, -1)
    (acc_up, acc_ubias, acc_down), ffn_back_parts = ffn_grad(
        w_up, up_bias, w_down, norm_blocks, two_blocks, kept_pre, kept_activ, block_kind
    )
    d_normed = (
        lax.psum_scatter(
            ffn_back_parts.reshape(group_rows, -1).astype(jnp.bfloat16),
            "tensor",
            scatter_dimension=0,
            tiled=True,
        ).astype(jnp.float32)
        + d_two
    )
    up_total, ubias_total, down_total = (acc_up, acc_ubias, acc_down)
    d_one = norm_backward(d_normed, gain_one, unit_one, inv_one)
    gain_grads = jnp.stack(
        [type_sum(kind_hot, d_normed * unit_one), type_sum(kind_hot, grad_out * unit_two)], axis=1
    )
    shift_grads = jnp.stack([type_sum(kind_hot, d_normed), type_sum(kind_hot, grad_out)], axis=1)
    rbias_grads = jnp.stack([type_sum(kind_hot, d_one), type_sum(kind_hot, d_two)], axis=1)
    gathered_one = lax.all_gather(d_one.astype(jnp.bfloat16), "tensor", axis=0, tiled=True)
    one_blocks = gathered_one.reshape(n_blocks, block_rows, -1)

    def attend_backward(accums, packed):
        acc_qkv, acc_qv, acc_out = accums
        row_data, grad_rows, valid_keys, kept_rows, log_total, mixed, block_type = packed
        acc_out = acc_out.at[block_type].add(
            jnp.einsum("re,rd->ed", mixed, grad_rows, preferred_element_type=jnp.float32)
        )
        d_mixed = jnp.einsum(
            "rd,ed->re", grad_rows, w_out[block_type], preferred_element_type=jnp.float32
        ).astype(jnp.bfloat16)
        scores = scores_of(kept_rows[0], kept_rows[1], valid_keys)
        attn_probs = jnp.exp(scores - log_total[..., None])
        d_mixed_heads = split_heads(d_mixed, heads_here)
        d_value = jnp.einsum(
            "shqk,sqhd->skhd",
            attn_probs.astype(jnp.bfloat16),
            d_mixed_heads,
            preferred_element_type=jnp.float32,
        )
        d_value = d_value.reshape(block_rows, -1).astype(jnp.bfloat16)
        d_probs = jnp.einsum(
            "sqhd,skhd->shqk",
            d_mixed_heads,
            split_heads(kept_rows[2], heads_here),
            preferred_element_type=jnp.float32,
        )
        prob_dot = jnp.sum(attn_probs * d_probs, axis=-1, keepdims=True)
        d_scores = (attn_probs * (d_probs - prob_dot)).astype(jnp.bfloat16)
        d_query = (
            jnp.einsum(
                "shqk,skhd->sqhd",
                d_scores,
                split_heads(kept_rows[1], heads_here),
                preferred_element_type=jnp.float32,
            )
            * score_scale
        )
        d_key = (
            jnp.einsum(
                "shqk,sqhd->skhd",
                d_scores,
                split_heads(kept_rows[0], heads_here),
                preferred_element_type=jnp.float32,
            )
            * score_scale
        )
        d_query = d_query.reshape(block_rows, -1).astype(jnp.bfloat16)
        d_key = d_key.reshape(block_rows, -1).astype(jnp.bfloat16)
        d_proj = jnp.stack([d_query, d_key, d_value])
        acc_qkv = acc_qkv.at[block_type].add(
            jnp.einsum("rd,jre->jde", row_data, d_proj, preferred_element_type=jnp.float32)
        )
        bias_sums = jnp.stack(
            [
                jnp.sum(d_query.astype(jnp.float32), axis=0),
                jnp.sum(d_value.astype(jnp.float32), axis=0),
            ]
        )
        acc_qv = acc_qv.at[block_type].add(bias_sums)
        partial_back = jnp.einsum(
            "jre,jde->rd", d_proj, w_qkv[block_type], preferred_element_type=jnp.float32
        )
        return ((acc_qkv, acc_qv, acc_out), partial_back)

    zeros_attn = (
        jnp.zeros(w_qkv.shape, jnp.float32),
        jnp.zeros(qv_bias.shape, jnp.float32),
        jnp.zeros(w_out.shape, jnp.float32),
    )
    (acc_qkv, acc_qv, acc_out), qkv_back_parts = lax.scan(
        attend_backward,
        zeros_attn,
        (input_blocks, one_blocks, valid_blocks, kept_proj, kept_total, kept_mixed, block_kind),
    )
    input_grad = (
        lax.psum_scatter(
            qkv_back_parts.reshape(group_rows, -1).astype(jnp.bfloat16),
            "tensor",
            scatter_dimension=0,
            tiled=True,
        ).astype(jnp.float32)
        + d_one
    )
    qkv_low, out_low, up_low, down_low = lax.psum(
        tuple(v.astype(jnp.bfloat16) for v in (acc_qkv, acc_out, up_total, down_total)), "dp"
    )
    qkv_total, out_total, up_total, down_total = (
        v.astype(jnp.float32) for v in (qkv_low, out_low, up_low, down_low)
    )
    small_grads = jnp.sum(
        lax.all_gather(jnp.stack([rbias_grads, gain_grads, shift_grads]), "tensor"), axis=0
    )
    qv_total, ubias_total, small_total = lax.psum((acc_qv, ubias_total, small_grads), "dp")
    rbias_total, gain_total, shift_total = small_total[0], small_total[1], small_total[2]
    return (
        layer_out,
        input_grad,
        qkv_total,
        qv_total,
        out_total,
        rbias_total,
        gain_total,
        shift_total,
        up_total,
        ubias_total,
        down_total,
    )


def solution(mesh):
    return jax.shard_map(
        local,
        mesh=mesh,
        in_specs=(
            P(("dp", "tensor"), None),
            P(("dp", "tensor"), None),
            P("dp"),
            P("dp"),
            P(None, None, None, "tensor"),
            P(None, None, "tensor"),
            P(None, "tensor", None),
            P(),
            P(),
            P(),
            P(None, None, "tensor"),
            P(None, "tensor"),
            P(None, "tensor", None),
        ),
        out_specs=(
            P(("dp", "tensor"), None),
            P(("dp", "tensor"), None),
            P(None, None, None, "tensor"),
            P(None, None, "tensor"),
            P(None, "tensor", None),
            P(),
            P(),
            P(),
            P(None, None, "tensor"),
            P(None, "tensor"),
            P(None, "tensor", None),
        ),
        check_vma=False,
    )
```

```python
import jax
import jax.numpy as jnp
from jax import lax
from jax.sharding import PartitionSpec as P

HEAD_DIM = 64
CHAIN = 128
BLOCK_SEQS = 4
STREAMS = 2


EPSILON = 1e-05
SQRT_HALF = 0.7071067811865476
INV_ROOT_TWO_PI = 0.3989422804014327


def norm_forward(row_data, gain_rows, shift_rows):
    mean_row = jnp.mean(row_data, axis=-1, keepdims=True)
    centred = row_data - mean_row
    var_row = jnp.mean(centred * centred, axis=-1, keepdims=True)
    inv_std = lax.rsqrt(var_row + EPSILON)
    unit_rows = centred * inv_std
    return (unit_rows * gain_rows + shift_rows, unit_rows, inv_std)


def norm_backward(grad_rows, gain_rows, unit_rows, inv_std):
    scaled = grad_rows * gain_rows
    mean_first = jnp.mean(scaled, axis=-1, keepdims=True)
    mean_second = jnp.mean(scaled * unit_rows, axis=-1, keepdims=True)
    return inv_std * (scaled - mean_first - unit_rows * mean_second)


def type_sum(kind_hot, values):
    return jnp.einsum("rt,rd->td", kind_hot, values, precision=lax.Precision.HIGHEST)


def gelu_slope(values):
    return 0.5 * (1.0 + lax.erf(values * SQRT_HALF)) + values * INV_ROOT_TWO_PI * jnp.exp(
        -0.5 * values * values
    )


def gather_rows(local_rows):
    return lax.all_gather(local_rows, "tensor", axis=0, tiled=False)


def scatter_sum(seg_parts):
    n_seg, seg_rows, width = seg_parts.shape
    summed = lax.psum_scatter(
        seg_parts.reshape(n_seg * seg_rows, width).astype(jnp.bfloat16),
        "tensor",
        scatter_dimension=0,
        tiled=True,
    )
    return summed.astype(jnp.float32)


def masked(seg_rows, seg_hot):
    return seg_rows[:, None] * seg_hot[:, :, None, None].astype(seg_rows.dtype)


def kind_sums(seg_hot, seg_totals):
    return jnp.einsum(
        "st,se->te", seg_hot, seg_totals, precision=lax.Precision.HIGHEST
    )


def stream(
    inputs,
    cotangent,
    seg_kind,
    seg_lens,
    row_kind,
    w_qkv,
    qv_bias,
    w_out,
    resid_bias,
    norm_gain,
    norm_shift,
    w_up,
    up_bias,
    w_down,
):
    n_seg, chains = seg_lens.shape
    seg_rows = chains * CHAIN
    heads_here = w_qkv.shape[3] // HEAD_DIM
    score_scale = HEAD_DIM ** (-0.5)
    highest = lax.Precision.HIGHEST
    seg_hot = (seg_kind[:, None] == jnp.arange(2)[None, :]).astype(jnp.float32)
    kind_hot = (row_kind[:, None] == jnp.arange(2)[None, :]).astype(jnp.float32)

    def pick(kind_table):
        return jnp.dot(kind_hot, kind_table.astype(jnp.float32), precision=highest)

    def heads(rows):
        return rows.reshape(n_seg, chains, CHAIN, heads_here, HEAD_DIM)

    key_valid = jnp.arange(CHAIN)[None, None, :] < seg_lens[:, :, None]

    qkv_sel = w_qkv[seg_kind]
    qvb_sel = qv_bias[seg_kind].astype(jnp.float32)
    out_sel = w_out[seg_kind]
    up_sel = w_up[seg_kind]
    ubias_sel = up_bias[seg_kind].astype(jnp.float32)
    down_sel = w_down[seg_kind]

    input_segs = gather_rows(inputs)
    projected = jnp.einsum(
        "srd,sjde->jsre", input_segs, qkv_sel, preferred_element_type=jnp.float32
    )
    query_rows = (projected[0] + qvb_sel[:, None, 0]).astype(jnp.bfloat16)
    key_rows = projected[1].astype(jnp.bfloat16)
    value_rows = (projected[2] + qvb_sel[:, None, 1]).astype(jnp.bfloat16)

    def probs_of():
        raw_scores = (
            jnp.einsum(
                "scqhd,sckhd->schqk",
                heads(query_rows),
                heads(key_rows),
                preferred_element_type=jnp.float32,
            )
            * score_scale
        )
        return jnp.where(key_valid[:, :, None, None, :], raw_scores, -1e30)

    scores = probs_of()
    row_max = jnp.max(scores, axis=-1, keepdims=True)
    log_total = row_max[..., 0] + jnp.log(jnp.sum(jnp.exp(scores - row_max), axis=-1))
    attn_probs = jnp.exp(scores - log_total[..., None])
    probs_low = attn_probs.astype(jnp.bfloat16)
    mixed = jnp.einsum(
        "schqk,sckhd->scqhd", probs_low, heads(value_rows), preferred_element_type=jnp.float32
    )
    mixed = mixed.reshape(n_seg, seg_rows, -1).astype(jnp.bfloat16)
    attn_parts = jnp.einsum("sre,sed->srd", mixed, out_sel, preferred_element_type=jnp.float32)
    attn_rows = scatter_sum(attn_parts)

    hidden_one = inputs.astype(jnp.float32) + attn_rows + pick(resid_bias[:, 0])
    gain_one = pick(norm_gain[:, 0])
    normed, unit_one, inv_one = norm_forward(hidden_one, gain_one, pick(norm_shift[:, 0]))
    normed_low = normed.astype(jnp.bfloat16)
    norm_segs = gather_rows(normed_low)
    pre_act = (
        jnp.einsum("srd,sdf->srf", norm_segs, up_sel, preferred_element_type=jnp.float32)
        + ubias_sel[:, None]
    )
    activ = jax.nn.gelu(pre_act, approximate=False).astype(jnp.bfloat16)
    ffn_parts = jnp.einsum("srf,sfd->srd", activ, down_sel, preferred_element_type=jnp.float32)
    ffn_rows = scatter_sum(ffn_parts)

    hidden_two = normed + ffn_rows + pick(resid_bias[:, 1])
    gain_two = pick(norm_gain[:, 1])
    output_rows, unit_two, inv_two = norm_forward(hidden_two, gain_two, pick(norm_shift[:, 1]))
    layer_out = output_rows.astype(jnp.bfloat16)
    grad_out = cotangent.astype(jnp.float32)
    d_two = norm_backward(grad_out, gain_two, unit_two, inv_two)
    two_segs = gather_rows(d_two.astype(jnp.bfloat16))

    grad_down = jnp.einsum(
        "strf,srd->tfd", masked(activ, seg_hot), two_segs, preferred_element_type=jnp.float32
    )
    d_activ = jnp.einsum(
        "srd,sfd->srf", two_segs, down_sel, preferred_element_type=jnp.float32
    ).astype(jnp.bfloat16)
    d_pre = (d_activ.astype(jnp.float32) * gelu_slope(pre_act)).astype(jnp.bfloat16)
    grad_up = jnp.einsum(
        "strd,srf->tdf", masked(norm_segs, seg_hot), d_pre, preferred_element_type=jnp.float32
    )
    grad_ubias = kind_sums(seg_hot, jnp.sum(d_pre.astype(jnp.float32), axis=1))
    ffn_back = jnp.einsum("srf,sdf->srd", d_pre, up_sel, preferred_element_type=jnp.float32)
    d_normed = scatter_sum(ffn_back) + d_two

    d_one = norm_backward(d_normed, gain_one, unit_one, inv_one)
    gain_grads = jnp.stack(
        [type_sum(kind_hot, d_normed * unit_one), type_sum(kind_hot, grad_out * unit_two)], axis=1
    )
    shift_grads = jnp.stack([type_sum(kind_hot, d_normed), type_sum(kind_hot, grad_out)], axis=1)
    rbias_grads = jnp.stack([type_sum(kind_hot, d_one), type_sum(kind_hot, d_two)], axis=1)
    one_segs = gather_rows(d_one.astype(jnp.bfloat16))

    grad_out_w = jnp.einsum(
        "stre,srd->ted", masked(mixed, seg_hot), one_segs, preferred_element_type=jnp.float32
    )
    d_mixed = jnp.einsum(
        "srd,sed->sre", one_segs, out_sel, preferred_element_type=jnp.float32
    ).astype(jnp.bfloat16)
    d_mixed_heads = heads(d_mixed)
    d_value = jnp.einsum(
        "schqk,scqhd->sckhd", probs_low, d_mixed_heads, preferred_element_type=jnp.float32
    )
    d_value = d_value.reshape(n_seg, seg_rows, -1).astype(jnp.bfloat16)
    d_probs = jnp.einsum(
        "scqhd,sckhd->schqk", d_mixed_heads, heads(value_rows), preferred_element_type=jnp.float32
    )
    prob_dot = jnp.sum(attn_probs * d_probs, axis=-1, keepdims=True)
    d_scores = (attn_probs * (d_probs - prob_dot)).astype(jnp.bfloat16)
    d_query = (
        jnp.einsum(
            "schqk,sckhd->scqhd", d_scores, heads(key_rows), preferred_element_type=jnp.float32
        )
        * score_scale
    )
    d_key = (
        jnp.einsum(
            "schqk,scqhd->sckhd", d_scores, heads(query_rows), preferred_element_type=jnp.float32
        )
        * score_scale
    )
    d_query = d_query.reshape(n_seg, seg_rows, -1).astype(jnp.bfloat16)
    d_key = d_key.reshape(n_seg, seg_rows, -1).astype(jnp.bfloat16)
    d_proj = jnp.stack([d_query, d_key, d_value])
    grad_qkv = jnp.einsum(
        "strd,jsre->tjde", masked(input_segs, seg_hot), d_proj, preferred_element_type=jnp.float32
    )
    grad_qv = jnp.stack(
        [
            kind_sums(seg_hot, jnp.sum(d_query.astype(jnp.float32), axis=1)),
            kind_sums(seg_hot, jnp.sum(d_value.astype(jnp.float32), axis=1)),
        ],
        axis=1,
    )
    qkv_back = jnp.einsum("jsre,sjde->srd", d_proj, qkv_sel, preferred_element_type=jnp.float32)
    input_grad = scatter_sum(qkv_back) + d_one
    small = jnp.stack([rbias_grads, gain_grads, shift_grads])
    return (
        layer_out,
        input_grad,
        (grad_qkv, grad_qv, grad_out_w, grad_up, grad_ubias, grad_down),
        small,
    )


def local(
    inputs,
    cotangent,
    lengths,
    block_kind,
    w_qkv,
    qv_bias,
    w_out,
    resid_bias,
    norm_gain,
    norm_shift,
    w_up,
    up_bias,
    w_down,
):
    tok_dev = inputs.shape[0]
    n_tensor = lax.axis_size("tensor")
    rank = lax.axis_index("tensor")
    block_rows = BLOCK_SEQS * CHAIN
    assert block_rows % tok_dev == 0
    dev_chains = tok_dev // CHAIN
    chains = dev_chains // STREAMS
    seg_rows = chains * CHAIN
    weights = (w_qkv, qv_bias, w_out, resid_bias, norm_gain, norm_shift, w_up, up_bias, w_down)
    outs, ins, grads, smalls = [], [], [], []
    for part in range(STREAMS):
        first_row = jnp.arange(n_tensor) * tok_dev + part * seg_rows
        seg_kind = block_kind[first_row // block_rows]
        chain_ids = (
            jnp.arange(n_tensor)[:, None] * dev_chains + part * chains + jnp.arange(chains)[None, :]
        )
        seg_lens = lengths[chain_ids]
        own_rows = rank * tok_dev + part * seg_rows + jnp.arange(seg_rows)
        row_kind = block_kind[own_rows // block_rows]
        rows = slice(part * seg_rows, (part + 1) * seg_rows)
        out_part, in_part, grad_part, small_part = stream(
            inputs[rows], cotangent[rows], seg_kind, seg_lens, row_kind, *weights
        )
        outs.append(out_part)
        ins.append(in_part)
        grads.append(grad_part)
        smalls.append(small_part)
    layer_out = jnp.concatenate(outs, axis=0)
    input_grad = jnp.concatenate(ins, axis=0)
    grad_qkv, grad_qv, grad_out_w, grad_up, grad_ubias, grad_down = (
        sum(parts[1:], parts[0]) for parts in zip(*grads)
    )
    small = sum(smalls[1:], smalls[0])
    qkv_low, out_low, up_low, down_low = lax.psum(
        tuple(v.astype(jnp.bfloat16) for v in (grad_qkv, grad_out_w, grad_up, grad_down)), "dp"
    )
    qkv_total, out_total, up_total, down_total = (
        v.astype(jnp.float32) for v in (qkv_low, out_low, up_low, down_low)
    )
    small_grads = jnp.sum(lax.all_gather(small, "tensor"), axis=0)
    qv_total, ubias_total, small_total = lax.psum((grad_qv, grad_ubias, small_grads), "dp")
    return (
        layer_out,
        input_grad,
        qkv_total,
        qv_total,
        out_total,
        small_total[0],
        small_total[1],
        small_total[2],
        up_total,
        ubias_total,
        down_total,
    )


def solution(mesh):
    return jax.shard_map(
        local,
        mesh=mesh,
        in_specs=(
            P(("dp", "tensor"), None),
            P(("dp", "tensor"), None),
            P("dp"),
            P("dp"),
            P(None, None, None, "tensor"),
            P(None, None, "tensor"),
            P(None, "tensor", None),
            P(),
            P(),
            P(),
            P(None, None, "tensor"),
            P(None, "tensor"),
            P(None, "tensor", None),
        ),
        out_specs=(
            P(("dp", "tensor"), None),
            P(("dp", "tensor"), None),
            P(None, None, None, "tensor"),
            P(None, None, "tensor"),
            P(None, "tensor", None),
            P(),
            P(),
            P(),
            P(None, None, "tensor"),
            P(None, "tensor"),
            P(None, "tensor", None),
        ),
        check_vma=False,
    )
```

```python
import jax
import jax.numpy as jnp
from jax import lax
from jax.sharding import PartitionSpec as P

HEAD_DIM = 64
CHAIN = 128
BLOCK_SEQS = 4
STREAMS = 2


EPSILON = 1e-05
SQRT_HALF = 0.7071067811865476
INV_ROOT_TWO_PI = 0.3989422804014327


def norm_forward(row_data, gain_rows, shift_rows):
    mean_row = jnp.mean(row_data, axis=-1, keepdims=True)
    centred = row_data - mean_row
    var_row = jnp.mean(centred * centred, axis=-1, keepdims=True)
    inv_std = lax.rsqrt(var_row + EPSILON)
    unit_rows = centred * inv_std
    return (unit_rows * gain_rows + shift_rows, unit_rows, inv_std)


def norm_backward(grad_rows, gain_rows, unit_rows, inv_std):
    scaled = grad_rows * gain_rows
    mean_first = jnp.mean(scaled, axis=-1, keepdims=True)
    mean_second = jnp.mean(scaled * unit_rows, axis=-1, keepdims=True)
    return inv_std * (scaled - mean_first - unit_rows * mean_second)


def type_sum(kind_hot, values):
    return jnp.einsum("rt,rd->td", kind_hot, values, precision=lax.Precision.HIGHEST)


def gelu_slope(values):
    return 0.5 * (1.0 + lax.erf(values * SQRT_HALF)) + values * INV_ROOT_TWO_PI * jnp.exp(
        -0.5 * values * values
    )


def gather_rows(local_rows):
    return lax.all_gather(local_rows, "tensor", axis=0, tiled=False)


def scatter_sum(seg_parts):
    n_seg, seg_rows, width = seg_parts.shape
    summed = lax.psum_scatter(
        seg_parts.reshape(n_seg * seg_rows, width).astype(jnp.bfloat16),
        "tensor",
        scatter_dimension=0,
        tiled=True,
    )
    return summed.astype(jnp.float32)


def masked(seg_rows, seg_hot):
    return seg_rows[:, None] * seg_hot[:, :, None, None].astype(seg_rows.dtype)


def kind_sums(seg_hot, seg_totals):
    return jnp.einsum(
        "st,se->te", seg_hot, seg_totals, precision=lax.Precision.HIGHEST
    )


def dp_perm(n, bit):
    return [(j, j ^ bit) for j in range(n)]


def dp_sum_low(parts):
    shapes = [p.shape for p in parts]
    flat = jnp.concatenate([p.reshape(-1) for p in parts])
    n_dp = lax.axis_size("dp")
    idx = lax.axis_index("dp")
    steps = n_dp.bit_length() - 1
    assert 1 << steps == n_dp and flat.shape[0] % n_dp == 0
    cur = flat
    for b in range(steps):
        half = cur.shape[0] // 2
        low_half, high_half = cur[:half], cur[half:]
        upper = ((idx >> b) & 1) == 1
        keep = jnp.where(upper, high_half, low_half)
        send = jnp.where(upper, low_half, high_half)
        got = lax.ppermute(send.astype(jnp.bfloat16), "dp", dp_perm(n_dp, 1 << b))
        cur = keep + got.astype(jnp.float32)
    cur = cur.astype(jnp.bfloat16)
    for b in reversed(range(steps)):
        got = lax.ppermute(cur, "dp", dp_perm(n_dp, 1 << b))
        upper = ((idx >> b) & 1) == 1
        cur = jnp.where(upper, jnp.concatenate([got, cur]), jnp.concatenate([cur, got]))
    cur = cur.astype(jnp.float32)
    outs, start = [], 0
    for shape in shapes:
        size = 1
        for extent in shape:
            size *= extent
        outs.append(cur[start : start + size].reshape(shape))
        start += size
    return outs


def exact_sum(values, axis):
    n_ax = lax.axis_size(axis)
    steps = n_ax.bit_length() - 1
    assert 1 << steps == n_ax
    for b in range(steps):
        values = tuple(
            v + g for v, g in zip(values, lax.ppermute(values, axis, dp_perm(n_ax, 1 << b)))
        )
    return values


def stream(
    inputs,
    cotangent,
    seg_kind,
    seg_lens,
    row_kind,
    w_qkv,
    qv_bias,
    w_out,
    resid_bias,
    norm_gain,
    norm_shift,
    w_up,
    up_bias,
    w_down,
):
    n_seg, chains = seg_lens.shape
    seg_rows = chains * CHAIN
    heads_here = w_qkv.shape[3] // HEAD_DIM
    score_scale = HEAD_DIM ** (-0.5)
    highest = lax.Precision.HIGHEST
    seg_hot = (seg_kind[:, None] == jnp.arange(2)[None, :]).astype(jnp.float32)
    kind_hot = (row_kind[:, None] == jnp.arange(2)[None, :]).astype(jnp.float32)

    def pick(kind_table):
        return jnp.dot(kind_hot, kind_table.astype(jnp.float32), precision=highest)

    def heads(rows):
        return rows.reshape(n_seg, chains, CHAIN, heads_here, HEAD_DIM)

    key_valid = jnp.arange(CHAIN)[None, None, :] < seg_lens[:, :, None]

    qkv_sel = w_qkv[seg_kind]
    qvb_sel = qv_bias[seg_kind].astype(jnp.float32)
    out_sel = w_out[seg_kind]
    up_sel = w_up[seg_kind]
    ubias_sel = up_bias[seg_kind].astype(jnp.float32)
    down_sel = w_down[seg_kind]

    input_segs = gather_rows(inputs)
    projected = jnp.einsum(
        "srd,sjde->jsre", input_segs, qkv_sel, preferred_element_type=jnp.float32
    )
    query_rows = (projected[0] + qvb_sel[:, None, 0]).astype(jnp.bfloat16)
    key_rows = projected[1].astype(jnp.bfloat16)
    value_rows = (projected[2] + qvb_sel[:, None, 1]).astype(jnp.bfloat16)

    def probs_of():
        raw_scores = (
            jnp.einsum(
                "scqhd,sckhd->schqk",
                heads(query_rows),
                heads(key_rows),
                preferred_element_type=jnp.float32,
            )
            * score_scale
        )
        return jnp.where(key_valid[:, :, None, None, :], raw_scores, -1e30)

    scores = probs_of()
    row_max = jnp.max(scores, axis=-1, keepdims=True)
    log_total = row_max[..., 0] + jnp.log(jnp.sum(jnp.exp(scores - row_max), axis=-1))
    attn_probs = jnp.exp(scores - log_total[..., None])
    probs_low = attn_probs.astype(jnp.bfloat16)
    mixed = jnp.einsum(
        "schqk,sckhd->scqhd", probs_low, heads(value_rows), preferred_element_type=jnp.float32
    )
    mixed = mixed.reshape(n_seg, seg_rows, -1).astype(jnp.bfloat16)
    attn_parts = jnp.einsum("sre,sed->srd", mixed, out_sel, preferred_element_type=jnp.float32)
    attn_rows = scatter_sum(attn_parts)

    hidden_one = inputs.astype(jnp.float32) + attn_rows + pick(resid_bias[:, 0])
    gain_one = pick(norm_gain[:, 0])
    normed, unit_one, inv_one = norm_forward(hidden_one, gain_one, pick(norm_shift[:, 0]))
    normed_low = normed.astype(jnp.bfloat16)
    norm_segs = gather_rows(normed_low)
    pre_act = (
        jnp.einsum("srd,sdf->srf", norm_segs, up_sel, preferred_element_type=jnp.float32)
        + ubias_sel[:, None]
    )
    activ = jax.nn.gelu(pre_act, approximate=False).astype(jnp.bfloat16)
    ffn_parts = jnp.einsum("srf,sfd->srd", activ, down_sel, preferred_element_type=jnp.float32)
    ffn_rows = scatter_sum(ffn_parts)

    hidden_two = normed + ffn_rows + pick(resid_bias[:, 1])
    gain_two = pick(norm_gain[:, 1])
    output_rows, unit_two, inv_two = norm_forward(hidden_two, gain_two, pick(norm_shift[:, 1]))
    layer_out = output_rows.astype(jnp.bfloat16)
    grad_out = cotangent.astype(jnp.float32)
    d_two = norm_backward(grad_out, gain_two, unit_two, inv_two)
    two_segs = gather_rows(d_two.astype(jnp.bfloat16))

    grad_down = jnp.einsum(
        "strf,srd->tfd", masked(activ, seg_hot), two_segs, preferred_element_type=jnp.float32
    )
    d_activ = jnp.einsum(
        "srd,sfd->srf", two_segs, down_sel, preferred_element_type=jnp.float32
    ).astype(jnp.bfloat16)
    d_pre = (d_activ.astype(jnp.float32) * gelu_slope(pre_act)).astype(jnp.bfloat16)
    grad_up = jnp.einsum(
        "strd,srf->tdf", masked(norm_segs, seg_hot), d_pre, preferred_element_type=jnp.float32
    )
    grad_ubias = kind_sums(seg_hot, jnp.sum(d_pre.astype(jnp.float32), axis=1))
    ffn_back = jnp.einsum("srf,sdf->srd", d_pre, up_sel, preferred_element_type=jnp.float32)
    d_normed = scatter_sum(ffn_back) + d_two

    d_one = norm_backward(d_normed, gain_one, unit_one, inv_one)
    gain_grads = jnp.stack(
        [type_sum(kind_hot, d_normed * unit_one), type_sum(kind_hot, grad_out * unit_two)], axis=1
    )
    shift_grads = jnp.stack([type_sum(kind_hot, d_normed), type_sum(kind_hot, grad_out)], axis=1)
    rbias_grads = jnp.stack([type_sum(kind_hot, d_one), type_sum(kind_hot, d_two)], axis=1)
    one_segs = gather_rows(d_one.astype(jnp.bfloat16))

    grad_out_w = jnp.einsum(
        "stre,srd->ted", masked(mixed, seg_hot), one_segs, preferred_element_type=jnp.float32
    )
    d_mixed = jnp.einsum(
        "srd,sed->sre", one_segs, out_sel, preferred_element_type=jnp.float32
    ).astype(jnp.bfloat16)
    d_mixed_heads = heads(d_mixed)
    d_value = jnp.einsum(
        "schqk,scqhd->sckhd", probs_low, d_mixed_heads, preferred_element_type=jnp.float32
    )
    d_value = d_value.reshape(n_seg, seg_rows, -1).astype(jnp.bfloat16)
    d_probs = jnp.einsum(
        "scqhd,sckhd->schqk", d_mixed_heads, heads(value_rows), preferred_element_type=jnp.float32
    )
    prob_dot = jnp.sum(attn_probs * d_probs, axis=-1, keepdims=True)
    d_scores = (attn_probs * (d_probs - prob_dot)).astype(jnp.bfloat16)
    d_query = (
        jnp.einsum(
            "schqk,sckhd->scqhd", d_scores, heads(key_rows), preferred_element_type=jnp.float32
        )
        * score_scale
    )
    d_key = (
        jnp.einsum(
            "schqk,scqhd->sckhd", d_scores, heads(query_rows), preferred_element_type=jnp.float32
        )
        * score_scale
    )
    d_query = d_query.reshape(n_seg, seg_rows, -1).astype(jnp.bfloat16)
    d_key = d_key.reshape(n_seg, seg_rows, -1).astype(jnp.bfloat16)
    d_proj = jnp.stack([d_query, d_key, d_value])
    grad_qkv = jnp.einsum(
        "strd,jsre->tjde", masked(input_segs, seg_hot), d_proj, preferred_element_type=jnp.float32
    )
    grad_qv = jnp.stack(
        [
            kind_sums(seg_hot, jnp.sum(d_query.astype(jnp.float32), axis=1)),
            kind_sums(seg_hot, jnp.sum(d_value.astype(jnp.float32), axis=1)),
        ],
        axis=1,
    )
    qkv_back = jnp.einsum("jsre,sjde->srd", d_proj, qkv_sel, preferred_element_type=jnp.float32)
    input_grad = scatter_sum(qkv_back) + d_one
    small = jnp.stack([rbias_grads, gain_grads, shift_grads])
    return (
        layer_out,
        input_grad,
        (grad_qkv, grad_qv, grad_out_w, grad_up, grad_ubias, grad_down),
        small,
    )


def local(
    inputs,
    cotangent,
    lengths,
    block_kind,
    w_qkv,
    qv_bias,
    w_out,
    resid_bias,
    norm_gain,
    norm_shift,
    w_up,
    up_bias,
    w_down,
):
    tok_dev = inputs.shape[0]
    n_tensor = lax.axis_size("tensor")
    rank = lax.axis_index("tensor")
    block_rows = BLOCK_SEQS * CHAIN
    assert block_rows % tok_dev == 0
    dev_chains = tok_dev // CHAIN
    chains = dev_chains // STREAMS
    seg_rows = chains * CHAIN
    weights = (w_qkv, qv_bias, w_out, resid_bias, norm_gain, norm_shift, w_up, up_bias, w_down)
    outs, ins, grads, smalls = [], [], [], []
    for part in range(STREAMS):
        first_row = jnp.arange(n_tensor) * tok_dev + part * seg_rows
        seg_kind = block_kind[first_row // block_rows]
        chain_ids = (
            jnp.arange(n_tensor)[:, None] * dev_chains + part * chains + jnp.arange(chains)[None, :]
        )
        seg_lens = lengths[chain_ids]
        own_rows = rank * tok_dev + part * seg_rows + jnp.arange(seg_rows)
        row_kind = block_kind[own_rows // block_rows]
        rows = slice(part * seg_rows, (part + 1) * seg_rows)
        out_part, in_part, grad_part, small_part = stream(
            inputs[rows], cotangent[rows], seg_kind, seg_lens, row_kind, *weights
        )
        outs.append(out_part)
        ins.append(in_part)
        grads.append(grad_part)
        smalls.append(small_part)
    layer_out = jnp.concatenate(outs, axis=0)
    input_grad = jnp.concatenate(ins, axis=0)
    grad_qkv, grad_qv, grad_out_w, grad_up, grad_ubias, grad_down = (
        sum(parts[1:], parts[0]) for parts in zip(*grads)
    )
    small = sum(smalls[1:], smalls[0])
    up_total, down_total = dp_sum_low((grad_up, grad_down))
    qkv_total, out_total = dp_sum_low((grad_qkv, grad_out_w))
    (small_grads,) = exact_sum((small,), "tensor")
    qv_total, ubias_total, small_total = exact_sum((grad_qv, grad_ubias, small_grads), "dp")
    return (
        layer_out,
        input_grad,
        qkv_total,
        qv_total,
        out_total,
        small_total[0],
        small_total[1],
        small_total[2],
        up_total,
        ubias_total,
        down_total,
    )


def solution(mesh):
    return jax.shard_map(
        local,
        mesh=mesh,
        in_specs=(
            P(("dp", "tensor"), None),
            P(("dp", "tensor"), None),
            P("dp"),
            P("dp"),
            P(None, None, None, "tensor"),
            P(None, None, "tensor"),
            P(None, "tensor", None),
            P(),
            P(),
            P(),
            P(None, None, "tensor"),
            P(None, "tensor"),
            P(None, "tensor", None),
        ),
        out_specs=(
            P(("dp", "tensor"), None),
            P(("dp", "tensor"), None),
            P(None, None, None, "tensor"),
            P(None, None, "tensor"),
            P(None, "tensor", None),
            P(),
            P(),
            P(),
            P(None, None, "tensor"),
            P(None, "tensor"),
            P(None, "tensor", None),
        ),
        check_vma=False,
    )
```

```python
import jax
import jax.numpy as jnp
from jax import lax
from jax.sharding import PartitionSpec as P

HEAD_DIM = 64
CHAIN = 128
BLOCK_SEQS = 4
STREAMS = 2


EPSILON = 1e-05
SQRT_HALF = 0.7071067811865476
INV_ROOT_TWO_PI = 0.3989422804014327


def norm_forward(row_data, gain_rows, shift_rows):
    mean_row = jnp.mean(row_data, axis=-1, keepdims=True)
    centred = row_data - mean_row
    var_row = jnp.mean(centred * centred, axis=-1, keepdims=True)
    inv_std = lax.rsqrt(var_row + EPSILON)
    unit_rows = centred * inv_std
    return (unit_rows * gain_rows + shift_rows, unit_rows, inv_std)


def norm_backward(grad_rows, gain_rows, unit_rows, inv_std):
    scaled = grad_rows * gain_rows
    mean_first = jnp.mean(scaled, axis=-1, keepdims=True)
    mean_second = jnp.mean(scaled * unit_rows, axis=-1, keepdims=True)
    return inv_std * (scaled - mean_first - unit_rows * mean_second)


def type_sum(kind_hot, values):
    return jnp.einsum("rt,rd->td", kind_hot, values, precision=lax.Precision.HIGHEST)


def gelu_slope(values):
    return 0.5 * (1.0 + lax.erf(values * SQRT_HALF)) + values * INV_ROOT_TWO_PI * jnp.exp(
        -0.5 * values * values
    )


def gather_rows(local_rows):
    return lax.all_gather(local_rows, "tensor", axis=0, tiled=False)


def scatter_sum(seg_parts):
    n_seg, seg_rows, width = seg_parts.shape
    summed = lax.psum_scatter(
        seg_parts.reshape(n_seg * seg_rows, width).astype(jnp.bfloat16),
        "tensor",
        scatter_dimension=0,
        tiled=True,
    )
    return summed.astype(jnp.float32)


def masked(seg_rows, seg_hot):
    return seg_rows[:, None] * seg_hot[:, :, None, None].astype(seg_rows.dtype)


def kind_sums(seg_hot, seg_totals):
    return jnp.einsum(
        "st,se->te", seg_hot, seg_totals, precision=lax.Precision.HIGHEST
    )


def dp_perm(n, bit):
    return [(j, j ^ bit) for j in range(n)]


def dp_sum_low(parts):
    shapes = [p.shape for p in parts]
    flat = jnp.concatenate([p.reshape(-1) for p in parts])
    total = flat.shape[0]
    n_dp = lax.axis_size("dp")
    idx = lax.axis_index("dp")
    steps = n_dp.bit_length() - 1
    assert 1 << steps == n_dp and total % n_dp == 0
    cur = flat
    offset = jnp.int32(0)
    for b in range(steps):
        half = cur.shape[0] // 2
        upper = (idx >> b) & 1
        keep = lax.dynamic_slice_in_dim(cur, upper * half, half)
        send = lax.dynamic_slice_in_dim(cur, (1 - upper) * half, half)
        got = lax.ppermute(send.astype(jnp.bfloat16), "dp", dp_perm(n_dp, 1 << b))
        cur = keep + got.astype(jnp.float32)
        offset = offset + upper * half
    size = cur.shape[0]
    full = lax.dynamic_update_slice_in_dim(
        jnp.zeros((total,), jnp.bfloat16), cur.astype(jnp.bfloat16), offset, 0
    )
    for b in reversed(range(steps)):
        upper = (idx >> b) & 1
        block = lax.dynamic_slice_in_dim(full, offset, size)
        got = lax.ppermute(block, "dp", dp_perm(n_dp, 1 << b))
        full = lax.dynamic_update_slice_in_dim(full, got, offset + (1 - 2 * upper) * size, 0)
        offset = offset - upper * size
        size *= 2
    outs, start = [], 0
    for shape in shapes:
        count = 1
        for extent in shape:
            count *= extent
        outs.append(full[start : start + count].astype(jnp.float32).reshape(shape))
        start += count
    return outs


def exact_sum(values, axis):
    n_ax = lax.axis_size(axis)
    steps = n_ax.bit_length() - 1
    assert 1 << steps == n_ax
    for b in range(steps):
        values = tuple(
            v + g for v, g in zip(values, lax.ppermute(values, axis, dp_perm(n_ax, 1 << b)))
        )
    return values


def stream(
    inputs,
    cotangent,
    seg_kind,
    seg_lens,
    row_kind,
    w_qkv,
    qv_bias,
    w_out,
    resid_bias,
    norm_gain,
    norm_shift,
    w_up,
    up_bias,
    w_down,
):
    n_seg, chains = seg_lens.shape
    seg_rows = chains * CHAIN
    heads_here = w_qkv.shape[3] // HEAD_DIM
    score_scale = HEAD_DIM ** (-0.5)
    highest = lax.Precision.HIGHEST
    seg_hot = (seg_kind[:, None] == jnp.arange(2)[None, :]).astype(jnp.float32)
    kind_hot = (row_kind[:, None] == jnp.arange(2)[None, :]).astype(jnp.float32)

    def pick(kind_table):
        return jnp.dot(kind_hot, kind_table.astype(jnp.float32), precision=highest)

    def heads(rows):
        return rows.reshape(n_seg, chains, CHAIN, heads_here, HEAD_DIM)

    key_valid = jnp.arange(CHAIN)[None, None, :] < seg_lens[:, :, None]

    qkv_sel = w_qkv[seg_kind]
    qvb_sel = qv_bias[seg_kind].astype(jnp.float32)
    out_sel = w_out[seg_kind]
    up_sel = w_up[seg_kind]
    ubias_sel = up_bias[seg_kind].astype(jnp.float32)
    down_sel = w_down[seg_kind]

    input_segs = gather_rows(inputs)
    projected = jnp.einsum(
        "srd,sjde->jsre", input_segs, qkv_sel, preferred_element_type=jnp.float32
    )
    query_rows = (projected[0] + qvb_sel[:, None, 0]).astype(jnp.bfloat16)
    key_rows = projected[1].astype(jnp.bfloat16)
    value_rows = (projected[2] + qvb_sel[:, None, 1]).astype(jnp.bfloat16)

    def probs_of():
        raw_scores = (
            jnp.einsum(
                "scqhd,sckhd->schqk",
                heads(query_rows),
                heads(key_rows),
                preferred_element_type=jnp.float32,
            )
            * score_scale
        )
        return jnp.where(key_valid[:, :, None, None, :], raw_scores, -1e30)

    scores = probs_of()
    row_max = jnp.max(scores, axis=-1, keepdims=True)
    log_total = row_max[..., 0] + jnp.log(jnp.sum(jnp.exp(scores - row_max), axis=-1))
    attn_probs = jnp.exp(scores - log_total[..., None])
    probs_low = attn_probs.astype(jnp.bfloat16)
    mixed = jnp.einsum(
        "schqk,sckhd->scqhd", probs_low, heads(value_rows), preferred_element_type=jnp.float32
    )
    mixed = mixed.reshape(n_seg, seg_rows, -1).astype(jnp.bfloat16)
    attn_parts = jnp.einsum("sre,sed->srd", mixed, out_sel, preferred_element_type=jnp.float32)
    attn_rows = scatter_sum(attn_parts)

    hidden_one = inputs.astype(jnp.float32) + attn_rows + pick(resid_bias[:, 0])
    gain_one = pick(norm_gain[:, 0])
    normed, unit_one, inv_one = norm_forward(hidden_one, gain_one, pick(norm_shift[:, 0]))
    normed_low = normed.astype(jnp.bfloat16)
    norm_segs = gather_rows(normed_low)
    pre_act = (
        jnp.einsum("srd,sdf->srf", norm_segs, up_sel, preferred_element_type=jnp.float32)
        + ubias_sel[:, None]
    )
    activ = jax.nn.gelu(pre_act, approximate=False).astype(jnp.bfloat16)
    ffn_parts = jnp.einsum("srf,sfd->srd", activ, down_sel, preferred_element_type=jnp.float32)
    ffn_rows = scatter_sum(ffn_parts)

    hidden_two = normed + ffn_rows + pick(resid_bias[:, 1])
    gain_two = pick(norm_gain[:, 1])
    output_rows, unit_two, inv_two = norm_forward(hidden_two, gain_two, pick(norm_shift[:, 1]))
    layer_out = output_rows.astype(jnp.bfloat16)
    grad_out = cotangent.astype(jnp.float32)
    d_two = norm_backward(grad_out, gain_two, unit_two, inv_two)
    two_segs = gather_rows(d_two.astype(jnp.bfloat16))

    grad_down = jnp.einsum(
        "strf,srd->tfd", masked(activ, seg_hot), two_segs, preferred_element_type=jnp.float32
    )
    d_activ = jnp.einsum(
        "srd,sfd->srf", two_segs, down_sel, preferred_element_type=jnp.float32
    ).astype(jnp.bfloat16)
    d_pre = (d_activ.astype(jnp.float32) * gelu_slope(pre_act)).astype(jnp.bfloat16)
    grad_up = jnp.einsum(
        "strd,srf->tdf", masked(norm_segs, seg_hot), d_pre, preferred_element_type=jnp.float32
    )
    grad_ubias = kind_sums(seg_hot, jnp.sum(d_pre.astype(jnp.float32), axis=1))
    ffn_back = jnp.einsum("srf,sdf->srd", d_pre, up_sel, preferred_element_type=jnp.float32)
    d_normed = scatter_sum(ffn_back) + d_two

    d_one = norm_backward(d_normed, gain_one, unit_one, inv_one)
    gain_grads = jnp.stack(
        [type_sum(kind_hot, d_normed * unit_one), type_sum(kind_hot, grad_out * unit_two)], axis=1
    )
    shift_grads = jnp.stack([type_sum(kind_hot, d_normed), type_sum(kind_hot, grad_out)], axis=1)
    rbias_grads = jnp.stack([type_sum(kind_hot, d_one), type_sum(kind_hot, d_two)], axis=1)
    one_segs = gather_rows(d_one.astype(jnp.bfloat16))

    grad_out_w = jnp.einsum(
        "stre,srd->ted", masked(mixed, seg_hot), one_segs, preferred_element_type=jnp.float32
    )
    d_mixed = jnp.einsum(
        "srd,sed->sre", one_segs, out_sel, preferred_element_type=jnp.float32
    ).astype(jnp.bfloat16)
    d_mixed_heads = heads(d_mixed)
    d_value = jnp.einsum(
        "schqk,scqhd->sckhd", probs_low, d_mixed_heads, preferred_element_type=jnp.float32
    )
    d_value = d_value.reshape(n_seg, seg_rows, -1).astype(jnp.bfloat16)
    d_probs = jnp.einsum(
        "scqhd,sckhd->schqk", d_mixed_heads, heads(value_rows), preferred_element_type=jnp.float32
    )
    prob_dot = jnp.sum(attn_probs * d_probs, axis=-1, keepdims=True)
    d_scores = (attn_probs * (d_probs - prob_dot)).astype(jnp.bfloat16)
    d_query = (
        jnp.einsum(
            "schqk,sckhd->scqhd", d_scores, heads(key_rows), preferred_element_type=jnp.float32
        )
        * score_scale
    )
    d_key = (
        jnp.einsum(
            "schqk,scqhd->sckhd", d_scores, heads(query_rows), preferred_element_type=jnp.float32
        )
        * score_scale
    )
    d_query = d_query.reshape(n_seg, seg_rows, -1).astype(jnp.bfloat16)
    d_key = d_key.reshape(n_seg, seg_rows, -1).astype(jnp.bfloat16)
    d_proj = jnp.stack([d_query, d_key, d_value])
    grad_qkv = jnp.einsum(
        "strd,jsre->tjde", masked(input_segs, seg_hot), d_proj, preferred_element_type=jnp.float32
    )
    grad_qv = jnp.stack(
        [
            kind_sums(seg_hot, jnp.sum(d_query.astype(jnp.float32), axis=1)),
            kind_sums(seg_hot, jnp.sum(d_value.astype(jnp.float32), axis=1)),
        ],
        axis=1,
    )
    qkv_back = jnp.einsum("jsre,sjde->srd", d_proj, qkv_sel, preferred_element_type=jnp.float32)
    input_grad = scatter_sum(qkv_back) + d_one
    small = jnp.stack([rbias_grads, gain_grads, shift_grads])
    return (
        layer_out,
        input_grad,
        (grad_qkv, grad_qv, grad_out_w, grad_up, grad_ubias, grad_down),
        small,
    )


def local(
    inputs,
    cotangent,
    lengths,
    block_kind,
    w_qkv,
    qv_bias,
    w_out,
    resid_bias,
    norm_gain,
    norm_shift,
    w_up,
    up_bias,
    w_down,
):
    tok_dev = inputs.shape[0]
    n_tensor = lax.axis_size("tensor")
    rank = lax.axis_index("tensor")
    block_rows = BLOCK_SEQS * CHAIN
    assert block_rows % tok_dev == 0
    dev_chains = tok_dev // CHAIN
    chains = dev_chains // STREAMS
    seg_rows = chains * CHAIN
    weights = (w_qkv, qv_bias, w_out, resid_bias, norm_gain, norm_shift, w_up, up_bias, w_down)
    outs, ins, grads, smalls = [], [], [], []
    for part in range(STREAMS):
        first_row = jnp.arange(n_tensor) * tok_dev + part * seg_rows
        seg_kind = block_kind[first_row // block_rows]
        chain_ids = (
            jnp.arange(n_tensor)[:, None] * dev_chains + part * chains + jnp.arange(chains)[None, :]
        )
        seg_lens = lengths[chain_ids]
        own_rows = rank * tok_dev + part * seg_rows + jnp.arange(seg_rows)
        row_kind = block_kind[own_rows // block_rows]
        rows = slice(part * seg_rows, (part + 1) * seg_rows)
        out_part, in_part, grad_part, small_part = stream(
            inputs[rows], cotangent[rows], seg_kind, seg_lens, row_kind, *weights
        )
        outs.append(out_part)
        ins.append(in_part)
        grads.append(grad_part)
        smalls.append(small_part)
    layer_out = jnp.concatenate(outs, axis=0)
    input_grad = jnp.concatenate(ins, axis=0)
    grad_qkv, grad_qv, grad_out_w, grad_up, grad_ubias, grad_down = (
        sum(parts[1:], parts[0]) for parts in zip(*grads)
    )
    small = sum(smalls[1:], smalls[0])
    up_total, down_total = dp_sum_low((grad_up, grad_down))
    qkv_low, out_low = lax.psum((grad_qkv.astype(jnp.bfloat16), grad_out_w.astype(jnp.bfloat16)), "dp")
    qkv_total, out_total = qkv_low.astype(jnp.float32), out_low.astype(jnp.float32)
    (small_grads,) = exact_sum((small,), "tensor")
    qv_total, ubias_total, small_total = exact_sum((grad_qv, grad_ubias, small_grads), "dp")
    return (
        layer_out,
        input_grad,
        qkv_total,
        qv_total,
        out_total,
        small_total[0],
        small_total[1],
        small_total[2],
        up_total,
        ubias_total,
        down_total,
    )


def solution(mesh):
    return jax.shard_map(
        local,
        mesh=mesh,
        in_specs=(
            P(("dp", "tensor"), None),
            P(("dp", "tensor"), None),
            P("dp"),
            P("dp"),
            P(None, None, None, "tensor"),
            P(None, None, "tensor"),
            P(None, "tensor", None),
            P(),
            P(),
            P(),
            P(None, None, "tensor"),
            P(None, "tensor"),
            P(None, "tensor", None),
        ),
        out_specs=(
            P(("dp", "tensor"), None),
            P(("dp", "tensor"), None),
            P(None, None, None, "tensor"),
            P(None, None, "tensor"),
            P(None, "tensor", None),
            P(),
            P(),
            P(),
            P(None, None, "tensor"),
            P(None, "tensor"),
            P(None, "tensor", None),
        ),
        check_vma=False,
    )
```

```python
import jax
import jax.numpy as jnp
from jax import lax
from jax.sharding import PartitionSpec as P

HEAD_DIM = 64
CHAIN = 128
BLOCK_SEQS = 4
STREAMS = 2


EPSILON = 1e-05
SQRT_HALF = 0.7071067811865476
INV_ROOT_TWO_PI = 0.3989422804014327


def norm_forward(row_data, gain_rows, shift_rows):
    mean_row = jnp.mean(row_data, axis=-1, keepdims=True)
    centred = row_data - mean_row
    var_row = jnp.mean(centred * centred, axis=-1, keepdims=True)
    inv_std = lax.rsqrt(var_row + EPSILON)
    unit_rows = centred * inv_std
    return (unit_rows * gain_rows + shift_rows, unit_rows, inv_std)


def norm_backward(grad_rows, gain_rows, unit_rows, inv_std):
    scaled = grad_rows * gain_rows
    mean_first = jnp.mean(scaled, axis=-1, keepdims=True)
    mean_second = jnp.mean(scaled * unit_rows, axis=-1, keepdims=True)
    return inv_std * (scaled - mean_first - unit_rows * mean_second)


def type_sum(kind_hot, values):
    return jnp.einsum("rt,rd->td", kind_hot, values, precision=lax.Precision.HIGHEST)


def gelu_slope(values):
    return 0.5 * (1.0 + lax.erf(values * SQRT_HALF)) + values * INV_ROOT_TWO_PI * jnp.exp(
        -0.5 * values * values
    )


def gather_rows(local_rows):
    return lax.all_gather(local_rows, "tensor", axis=0, tiled=False)


def scatter_sum(seg_parts):
    n_seg, seg_rows, width = seg_parts.shape
    summed = lax.psum_scatter(
        seg_parts.reshape(n_seg * seg_rows, width).astype(jnp.bfloat16),
        "tensor",
        scatter_dimension=0,
        tiled=True,
    )
    return summed.astype(jnp.float32)


def masked(seg_rows, seg_hot):
    return seg_rows[:, None] * seg_hot[:, :, None, None].astype(seg_rows.dtype)


def kind_sums(seg_hot, seg_totals):
    return jnp.einsum(
        "st,se->te", seg_hot, seg_totals, precision=lax.Precision.HIGHEST
    )


def dp_perm(n, bit):
    return [(j, j ^ bit) for j in range(n)]


def dp_sum_low(parts):
    shapes = [p.shape for p in parts]
    n_dp = lax.axis_size("dp")
    idx = lax.axis_index("dp")
    steps = n_dp.bit_length() - 1
    cur = [p.reshape(-1, p.shape[-1]) for p in parts]
    assert 1 << steps == n_dp and all(c.shape[0] % n_dp == 0 for c in cur)
    for b in range(steps):
        upper = ((idx >> b) & 1) == 1
        halves = [(c[: c.shape[0] // 2], c[c.shape[0] // 2 :]) for c in cur]
        sends = tuple(jnp.where(upper, lo, hi).astype(jnp.bfloat16) for lo, hi in halves)
        gots = lax.ppermute(sends, "dp", dp_perm(n_dp, 1 << b))
        cur = [jnp.where(upper, hi, lo) + g.astype(jnp.float32) for (lo, hi), g in zip(halves, gots)]
    cur = [c.astype(jnp.bfloat16) for c in cur]
    for b in reversed(range(steps)):
        upper = ((idx >> b) & 1) == 1
        gots = lax.ppermute(tuple(cur), "dp", dp_perm(n_dp, 1 << b))
        cur = [
            jnp.where(upper, jnp.concatenate([g, c]), jnp.concatenate([c, g]))
            for c, g in zip(cur, gots)
        ]
    return [c.astype(jnp.float32).reshape(shape) for c, shape in zip(cur, shapes)]


def exact_sum(values, axis):
    n_ax = lax.axis_size(axis)
    steps = n_ax.bit_length() - 1
    assert 1 << steps == n_ax
    for b in range(steps):
        values = tuple(
            v + g for v, g in zip(values, lax.ppermute(values, axis, dp_perm(n_ax, 1 << b)))
        )
    return values


def stream(
    inputs,
    cotangent,
    seg_kind,
    seg_lens,
    row_kind,
    w_qkv,
    qv_bias,
    w_out,
    resid_bias,
    norm_gain,
    norm_shift,
    w_up,
    up_bias,
    w_down,
):
    n_seg, chains = seg_lens.shape
    seg_rows = chains * CHAIN
    heads_here = w_qkv.shape[3] // HEAD_DIM
    score_scale = HEAD_DIM ** (-0.5)
    highest = lax.Precision.HIGHEST
    seg_hot = (seg_kind[:, None] == jnp.arange(2)[None, :]).astype(jnp.float32)
    kind_hot = (row_kind[:, None] == jnp.arange(2)[None, :]).astype(jnp.float32)

    def pick(kind_table):
        return jnp.dot(kind_hot, kind_table.astype(jnp.float32), precision=highest)

    def heads(rows):
        return rows.reshape(n_seg, chains, CHAIN, heads_here, HEAD_DIM)

    key_valid = jnp.arange(CHAIN)[None, None, :] < seg_lens[:, :, None]

    qkv_sel = w_qkv[seg_kind]
    qvb_sel = qv_bias[seg_kind].astype(jnp.float32)
    out_sel = w_out[seg_kind]
    up_sel = w_up[seg_kind]
    ubias_sel = up_bias[seg_kind].astype(jnp.float32)
    down_sel = w_down[seg_kind]

    input_segs = gather_rows(inputs)
    projected = jnp.einsum(
        "srd,sjde->jsre", input_segs, qkv_sel, preferred_element_type=jnp.float32
    )
    query_rows = (projected[0] + qvb_sel[:, None, 0]).astype(jnp.bfloat16)
    key_rows = projected[1].astype(jnp.bfloat16)
    value_rows = (projected[2] + qvb_sel[:, None, 1]).astype(jnp.bfloat16)

    def probs_of():
        raw_scores = (
            jnp.einsum(
                "scqhd,sckhd->schqk",
                heads(query_rows),
                heads(key_rows),
                preferred_element_type=jnp.float32,
            )
            * score_scale
        )
        return jnp.where(key_valid[:, :, None, None, :], raw_scores, -1e30)

    scores = probs_of()
    row_max = jnp.max(scores, axis=-1, keepdims=True)
    log_total = row_max[..., 0] + jnp.log(jnp.sum(jnp.exp(scores - row_max), axis=-1))
    attn_probs = jnp.exp(scores - log_total[..., None])
    probs_low = attn_probs.astype(jnp.bfloat16)
    mixed = jnp.einsum(
        "schqk,sckhd->scqhd", probs_low, heads(value_rows), preferred_element_type=jnp.float32
    )
    mixed = mixed.reshape(n_seg, seg_rows, -1).astype(jnp.bfloat16)
    attn_parts = jnp.einsum("sre,sed->srd", mixed, out_sel, preferred_element_type=jnp.float32)
    attn_rows = scatter_sum(attn_parts)

    hidden_one = inputs.astype(jnp.float32) + attn_rows + pick(resid_bias[:, 0])
    gain_one = pick(norm_gain[:, 0])
    normed, unit_one, inv_one = norm_forward(hidden_one, gain_one, pick(norm_shift[:, 0]))
    normed_low = normed.astype(jnp.bfloat16)
    norm_segs = gather_rows(normed_low)
    pre_act = (
        jnp.einsum("srd,sdf->srf", norm_segs, up_sel, preferred_element_type=jnp.float32)
        + ubias_sel[:, None]
    )
    activ = jax.nn.gelu(pre_act, approximate=False).astype(jnp.bfloat16)
    ffn_parts = jnp.einsum("srf,sfd->srd", activ, down_sel, preferred_element_type=jnp.float32)
    ffn_rows = scatter_sum(ffn_parts)

    hidden_two = normed + ffn_rows + pick(resid_bias[:, 1])
    gain_two = pick(norm_gain[:, 1])
    output_rows, unit_two, inv_two = norm_forward(hidden_two, gain_two, pick(norm_shift[:, 1]))
    layer_out = output_rows.astype(jnp.bfloat16)
    grad_out = cotangent.astype(jnp.float32)
    d_two = norm_backward(grad_out, gain_two, unit_two, inv_two)
    two_segs = gather_rows(d_two.astype(jnp.bfloat16))

    grad_down = jnp.einsum(
        "strf,srd->tfd", masked(activ, seg_hot), two_segs, preferred_element_type=jnp.float32
    )
    d_activ = jnp.einsum(
        "srd,sfd->srf", two_segs, down_sel, preferred_element_type=jnp.float32
    ).astype(jnp.bfloat16)
    d_pre = (d_activ.astype(jnp.float32) * gelu_slope(pre_act)).astype(jnp.bfloat16)
    grad_up = jnp.einsum(
        "strd,srf->tdf", masked(norm_segs, seg_hot), d_pre, preferred_element_type=jnp.float32
    )
    grad_ubias = kind_sums(seg_hot, jnp.sum(d_pre.astype(jnp.float32), axis=1))
    ffn_back = jnp.einsum("srf,sdf->srd", d_pre, up_sel, preferred_element_type=jnp.float32)
    d_normed = scatter_sum(ffn_back) + d_two

    d_one = norm_backward(d_normed, gain_one, unit_one, inv_one)
    gain_grads = jnp.stack(
        [type_sum(kind_hot, d_normed * unit_one), type_sum(kind_hot, grad_out * unit_two)], axis=1
    )
    shift_grads = jnp.stack([type_sum(kind_hot, d_normed), type_sum(kind_hot, grad_out)], axis=1)
    rbias_grads = jnp.stack([type_sum(kind_hot, d_one), type_sum(kind_hot, d_two)], axis=1)
    one_segs = gather_rows(d_one.astype(jnp.bfloat16))

    grad_out_w = jnp.einsum(
        "stre,srd->ted", masked(mixed, seg_hot), one_segs, preferred_element_type=jnp.float32
    )
    d_mixed = jnp.einsum(
        "srd,sed->sre", one_segs, out_sel, preferred_element_type=jnp.float32
    ).astype(jnp.bfloat16)
    d_mixed_heads = heads(d_mixed)
    d_value = jnp.einsum(
        "schqk,scqhd->sckhd", probs_low, d_mixed_heads, preferred_element_type=jnp.float32
    )
    d_value = d_value.reshape(n_seg, seg_rows, -1).astype(jnp.bfloat16)
    d_probs = jnp.einsum(
        "scqhd,sckhd->schqk", d_mixed_heads, heads(value_rows), preferred_element_type=jnp.float32
    )
    prob_dot = jnp.sum(attn_probs * d_probs, axis=-1, keepdims=True)
    d_scores = (attn_probs * (d_probs - prob_dot)).astype(jnp.bfloat16)
    d_query = (
        jnp.einsum(
            "schqk,sckhd->scqhd", d_scores, heads(key_rows), preferred_element_type=jnp.float32
        )
        * score_scale
    )
    d_key = (
        jnp.einsum(
            "schqk,scqhd->sckhd", d_scores, heads(query_rows), preferred_element_type=jnp.float32
        )
        * score_scale
    )
    d_query = d_query.reshape(n_seg, seg_rows, -1).astype(jnp.bfloat16)
    d_key = d_key.reshape(n_seg, seg_rows, -1).astype(jnp.bfloat16)
    d_proj = jnp.stack([d_query, d_key, d_value])
    grad_qkv = jnp.einsum(
        "strd,jsre->tjde", masked(input_segs, seg_hot), d_proj, preferred_element_type=jnp.float32
    )
    grad_qv = jnp.stack(
        [
            kind_sums(seg_hot, jnp.sum(d_query.astype(jnp.float32), axis=1)),
            kind_sums(seg_hot, jnp.sum(d_value.astype(jnp.float32), axis=1)),
        ],
        axis=1,
    )
    qkv_back = jnp.einsum("jsre,sjde->srd", d_proj, qkv_sel, preferred_element_type=jnp.float32)
    input_grad = scatter_sum(qkv_back) + d_one
    small = jnp.stack([rbias_grads, gain_grads, shift_grads])
    return (
        layer_out,
        input_grad,
        (grad_qkv, grad_qv, grad_out_w, grad_up, grad_ubias, grad_down),
        small,
    )


def local(
    inputs,
    cotangent,
    lengths,
    block_kind,
    w_qkv,
    qv_bias,
    w_out,
    resid_bias,
    norm_gain,
    norm_shift,
    w_up,
    up_bias,
    w_down,
):
    tok_dev = inputs.shape[0]
    n_tensor = lax.axis_size("tensor")
    rank = lax.axis_index("tensor")
    block_rows = BLOCK_SEQS * CHAIN
    assert block_rows % tok_dev == 0
    dev_chains = tok_dev // CHAIN
    chains = dev_chains // STREAMS
    seg_rows = chains * CHAIN
    weights = (w_qkv, qv_bias, w_out, resid_bias, norm_gain, norm_shift, w_up, up_bias, w_down)
    outs, ins, grads, smalls = [], [], [], []
    for part in range(STREAMS):
        first_row = jnp.arange(n_tensor) * tok_dev + part * seg_rows
        seg_kind = block_kind[first_row // block_rows]
        chain_ids = (
            jnp.arange(n_tensor)[:, None] * dev_chains + part * chains + jnp.arange(chains)[None, :]
        )
        seg_lens = lengths[chain_ids]
        own_rows = rank * tok_dev + part * seg_rows + jnp.arange(seg_rows)
        row_kind = block_kind[own_rows // block_rows]
        rows = slice(part * seg_rows, (part + 1) * seg_rows)
        out_part, in_part, grad_part, small_part = stream(
            inputs[rows], cotangent[rows], seg_kind, seg_lens, row_kind, *weights
        )
        outs.append(out_part)
        ins.append(in_part)
        grads.append(grad_part)
        smalls.append(small_part)
    layer_out = jnp.concatenate(outs, axis=0)
    input_grad = jnp.concatenate(ins, axis=0)
    grad_qkv, grad_qv, grad_out_w, grad_up, grad_ubias, grad_down = (
        sum(parts[1:], parts[0]) for parts in zip(*grads)
    )
    small = sum(smalls[1:], smalls[0])
    up_total, down_total = dp_sum_low((grad_up, grad_down))
    qkv_total, out_total = dp_sum_low((grad_qkv, grad_out_w))
    (small_grads,) = exact_sum((small,), "tensor")
    qv_total, ubias_total, small_total = exact_sum((grad_qv, grad_ubias, small_grads), "dp")
    return (
        layer_out,
        input_grad,
        qkv_total,
        qv_total,
        out_total,
        small_total[0],
        small_total[1],
        small_total[2],
        up_total,
        ubias_total,
        down_total,
    )


def solution(mesh):
    return jax.shard_map(
        local,
        mesh=mesh,
        in_specs=(
            P(("dp", "tensor"), None),
            P(("dp", "tensor"), None),
            P("dp"),
            P("dp"),
            P(None, None, None, "tensor"),
            P(None, None, "tensor"),
            P(None, "tensor", None),
            P(),
            P(),
            P(),
            P(None, None, "tensor"),
            P(None, "tensor"),
            P(None, "tensor", None),
        ),
        out_specs=(
            P(("dp", "tensor"), None),
            P(("dp", "tensor"), None),
            P(None, None, None, "tensor"),
            P(None, None, "tensor"),
            P(None, "tensor", None),
            P(),
            P(),
            P(),
            P(None, None, "tensor"),
            P(None, "tensor"),
            P(None, "tensor", None),
        ),
        check_vma=False,
    )
```

```python
import jax
import jax.numpy as jnp
from jax import lax
from jax.sharding import PartitionSpec as P

HEAD_DIM = 64
CHAIN = 128
BLOCK_SEQS = 4
STREAMS = 2


EPSILON = 1e-05
SQRT_HALF = 0.7071067811865476
INV_ROOT_TWO_PI = 0.3989422804014327


def norm_forward(row_data, gain_rows, shift_rows):
    mean_row = jnp.mean(row_data, axis=-1, keepdims=True)
    centred = row_data - mean_row
    var_row = jnp.mean(centred * centred, axis=-1, keepdims=True)
    inv_std = lax.rsqrt(var_row + EPSILON)
    unit_rows = centred * inv_std
    return (unit_rows * gain_rows + shift_rows, unit_rows, inv_std)


def norm_backward(grad_rows, gain_rows, unit_rows, inv_std):
    scaled = grad_rows * gain_rows
    mean_first = jnp.mean(scaled, axis=-1, keepdims=True)
    mean_second = jnp.mean(scaled * unit_rows, axis=-1, keepdims=True)
    return inv_std * (scaled - mean_first - unit_rows * mean_second)


def type_sum(kind_hot, values):
    return jnp.einsum("rt,rd->td", kind_hot, values, precision=lax.Precision.HIGHEST)


def gelu_slope(values):
    return 0.5 * (1.0 + lax.erf(values * SQRT_HALF)) + values * INV_ROOT_TWO_PI * jnp.exp(
        -0.5 * values * values
    )


def gather_rows(local_rows):
    return lax.all_gather(local_rows, "tensor", axis=0, tiled=False)


def scatter_sum(seg_parts):
    n_seg, seg_rows, width = seg_parts.shape
    summed = lax.psum_scatter(
        seg_parts.reshape(n_seg * seg_rows, width).astype(jnp.bfloat16),
        "tensor",
        scatter_dimension=0,
        tiled=True,
    )
    return summed.astype(jnp.float32)


def masked(seg_rows, seg_hot):
    return seg_rows[:, None] * seg_hot[:, :, None, None].astype(seg_rows.dtype)


def kind_sums(seg_hot, seg_totals):
    return jnp.einsum(
        "st,se->te", seg_hot, seg_totals, precision=lax.Precision.HIGHEST
    )


def dp_perm(n, bit):
    return [(j, j ^ bit) for j in range(n)]


def dp_sum_low(parts):
    shapes = [p.shape for p in parts]
    n_dp = lax.axis_size("dp")
    idx = lax.axis_index("dp")
    steps = n_dp.bit_length() - 1
    cur = [p.reshape(-1, p.shape[-1]) for p in parts]
    assert 1 << steps == n_dp and all(c.shape[0] % n_dp == 0 for c in cur)
    for b in range(steps):
        upper = ((idx >> b) & 1) == 1
        halves = [(c[: c.shape[0] // 2], c[c.shape[0] // 2 :]) for c in cur]
        sends = tuple(jnp.where(upper, lo, hi).astype(jnp.bfloat16) for lo, hi in halves)
        gots = lax.ppermute(sends, "dp", dp_perm(n_dp, 1 << b))
        cur = [jnp.where(upper, hi, lo) + g.astype(jnp.float32) for (lo, hi), g in zip(halves, gots)]
    cur = [c.astype(jnp.bfloat16) for c in cur]
    for b in reversed(range(steps)):
        upper = ((idx >> b) & 1) == 1
        gots = lax.ppermute(tuple(cur), "dp", dp_perm(n_dp, 1 << b))
        cur = [
            jnp.where(upper, jnp.concatenate([g, c]), jnp.concatenate([c, g]))
            for c, g in zip(cur, gots)
        ]
    return [c.astype(jnp.float32).reshape(shape) for c, shape in zip(cur, shapes)]


def exact_sum(values, axis):
    n_ax = lax.axis_size(axis)
    steps = n_ax.bit_length() - 1
    assert 1 << steps == n_ax
    for b in range(steps):
        values = tuple(
            v + g for v, g in zip(values, lax.ppermute(values, axis, dp_perm(n_ax, 1 << b)))
        )
    return values


def stream(
    inputs,
    cotangent,
    seg_kind,
    seg_lens,
    row_kind,
    out_rows_w,
    w_qkv,
    qv_bias,
    w_out,
    resid_bias,
    norm_gain,
    norm_shift,
    w_up,
    up_bias,
    w_down,
):
    n_seg, chains = seg_lens.shape
    seg_rows = chains * CHAIN
    heads_here = w_qkv.shape[3] // HEAD_DIM
    score_scale = HEAD_DIM ** (-0.5)
    highest = lax.Precision.HIGHEST
    seg_hot = (seg_kind[:, None] == jnp.arange(2)[None, :]).astype(jnp.float32)
    kind_hot = (row_kind[:, None] == jnp.arange(2)[None, :]).astype(jnp.float32)

    def pick(kind_table):
        return jnp.dot(kind_hot, kind_table.astype(jnp.float32), precision=highest)

    def heads(rows):
        return rows.reshape(n_seg, chains, CHAIN, heads_here, HEAD_DIM)

    key_valid = jnp.arange(CHAIN)[None, None, :] < seg_lens[:, :, None]

    qkv_sel = w_qkv[seg_kind]
    qvb_sel = qv_bias[seg_kind].astype(jnp.float32)
    out_sel = w_out[seg_kind]
    up_sel = w_up[seg_kind]
    ubias_sel = up_bias[seg_kind].astype(jnp.float32)
    down_sel = w_down[seg_kind]

    input_segs = gather_rows(inputs)
    projected = jnp.einsum(
        "srd,sjde->jsre", input_segs, qkv_sel, preferred_element_type=jnp.float32
    )
    query_rows = (projected[0] + qvb_sel[:, None, 0]).astype(jnp.bfloat16)
    key_rows = projected[1].astype(jnp.bfloat16)
    value_rows = (projected[2] + qvb_sel[:, None, 1]).astype(jnp.bfloat16)

    def probs_of():
        raw_scores = (
            jnp.einsum(
                "scqhd,sckhd->schqk",
                heads(query_rows),
                heads(key_rows),
                preferred_element_type=jnp.float32,
            )
            * score_scale
        )
        return jnp.where(key_valid[:, :, None, None, :], raw_scores, -1e30)

    scores = probs_of()
    row_max = jnp.max(scores, axis=-1, keepdims=True)
    log_total = row_max[..., 0] + jnp.log(jnp.sum(jnp.exp(scores - row_max), axis=-1))
    attn_probs = jnp.exp(scores - log_total[..., None])
    probs_low = attn_probs.astype(jnp.bfloat16)
    mixed = jnp.einsum(
        "schqk,sckhd->scqhd", probs_low, heads(value_rows), preferred_element_type=jnp.float32
    )
    mixed = mixed.reshape(n_seg, seg_rows, -1).astype(jnp.bfloat16)
    mixed_rows = lax.all_to_all(mixed, "tensor", 0, 0, tiled=True)
    attn_rows = jnp.einsum(
        "erc,ecd->rd", mixed_rows, out_rows_w, preferred_element_type=jnp.float32
    )

    hidden_one = inputs.astype(jnp.float32) + attn_rows + pick(resid_bias[:, 0])
    gain_one = pick(norm_gain[:, 0])
    normed, unit_one, inv_one = norm_forward(hidden_one, gain_one, pick(norm_shift[:, 0]))
    normed_low = normed.astype(jnp.bfloat16)
    norm_segs = gather_rows(normed_low)
    pre_act = (
        jnp.einsum("srd,sdf->srf", norm_segs, up_sel, preferred_element_type=jnp.float32)
        + ubias_sel[:, None]
    )
    activ = jax.nn.gelu(pre_act, approximate=False).astype(jnp.bfloat16)
    ffn_parts = jnp.einsum("srf,sfd->srd", activ, down_sel, preferred_element_type=jnp.float32)
    ffn_rows = scatter_sum(ffn_parts)

    hidden_two = normed + ffn_rows + pick(resid_bias[:, 1])
    gain_two = pick(norm_gain[:, 1])
    output_rows, unit_two, inv_two = norm_forward(hidden_two, gain_two, pick(norm_shift[:, 1]))
    layer_out = output_rows.astype(jnp.bfloat16)
    grad_out = cotangent.astype(jnp.float32)
    d_two = norm_backward(grad_out, gain_two, unit_two, inv_two)
    two_segs = gather_rows(d_two.astype(jnp.bfloat16))

    grad_down = jnp.einsum(
        "strf,srd->tfd", masked(activ, seg_hot), two_segs, preferred_element_type=jnp.float32
    )
    d_activ = jnp.einsum(
        "srd,sfd->srf", two_segs, down_sel, preferred_element_type=jnp.float32
    ).astype(jnp.bfloat16)
    d_pre = (d_activ.astype(jnp.float32) * gelu_slope(pre_act)).astype(jnp.bfloat16)
    grad_up = jnp.einsum(
        "strd,srf->tdf", masked(norm_segs, seg_hot), d_pre, preferred_element_type=jnp.float32
    )
    grad_ubias = kind_sums(seg_hot, jnp.sum(d_pre.astype(jnp.float32), axis=1))
    ffn_back = jnp.einsum("srf,sdf->srd", d_pre, up_sel, preferred_element_type=jnp.float32)
    d_normed = scatter_sum(ffn_back) + d_two

    d_one = norm_backward(d_normed, gain_one, unit_one, inv_one)
    gain_grads = jnp.stack(
        [type_sum(kind_hot, d_normed * unit_one), type_sum(kind_hot, grad_out * unit_two)], axis=1
    )
    shift_grads = jnp.stack([type_sum(kind_hot, d_normed), type_sum(kind_hot, grad_out)], axis=1)
    rbias_grads = jnp.stack([type_sum(kind_hot, d_one), type_sum(kind_hot, d_two)], axis=1)
    one_segs = gather_rows(d_one.astype(jnp.bfloat16))

    grad_out_w = jnp.einsum(
        "stre,srd->ted", masked(mixed, seg_hot), one_segs, preferred_element_type=jnp.float32
    )
    d_mixed = jnp.einsum(
        "srd,sed->sre", one_segs, out_sel, preferred_element_type=jnp.float32
    ).astype(jnp.bfloat16)
    d_mixed_heads = heads(d_mixed)
    d_value = jnp.einsum(
        "schqk,scqhd->sckhd", probs_low, d_mixed_heads, preferred_element_type=jnp.float32
    )
    d_value = d_value.reshape(n_seg, seg_rows, -1).astype(jnp.bfloat16)
    d_probs = jnp.einsum(
        "scqhd,sckhd->schqk", d_mixed_heads, heads(value_rows), preferred_element_type=jnp.float32
    )
    prob_dot = jnp.sum(attn_probs * d_probs, axis=-1, keepdims=True)
    d_scores = (attn_probs * (d_probs - prob_dot)).astype(jnp.bfloat16)
    d_query = (
        jnp.einsum(
            "schqk,sckhd->scqhd", d_scores, heads(key_rows), preferred_element_type=jnp.float32
        )
        * score_scale
    )
    d_key = (
        jnp.einsum(
            "schqk,scqhd->sckhd", d_scores, heads(query_rows), preferred_element_type=jnp.float32
        )
        * score_scale
    )
    d_query = d_query.reshape(n_seg, seg_rows, -1).astype(jnp.bfloat16)
    d_key = d_key.reshape(n_seg, seg_rows, -1).astype(jnp.bfloat16)
    d_proj = jnp.stack([d_query, d_key, d_value])
    grad_qkv = jnp.einsum(
        "strd,jsre->tjde", masked(input_segs, seg_hot), d_proj, preferred_element_type=jnp.float32
    )
    grad_qv = jnp.stack(
        [
            kind_sums(seg_hot, jnp.sum(d_query.astype(jnp.float32), axis=1)),
            kind_sums(seg_hot, jnp.sum(d_value.astype(jnp.float32), axis=1)),
        ],
        axis=1,
    )
    qkv_back = jnp.einsum("jsre,sjde->srd", d_proj, qkv_sel, preferred_element_type=jnp.float32)
    input_grad = scatter_sum(qkv_back) + d_one
    small = jnp.stack([rbias_grads, gain_grads, shift_grads])
    return (
        layer_out,
        input_grad,
        (grad_qkv, grad_qv, grad_out_w, grad_up, grad_ubias, grad_down),
        small,
    )


def local(
    inputs,
    cotangent,
    lengths,
    block_kind,
    w_qkv,
    qv_bias,
    w_out,
    resid_bias,
    norm_gain,
    norm_shift,
    w_up,
    up_bias,
    w_down,
):
    tok_dev = inputs.shape[0]
    n_tensor = lax.axis_size("tensor")
    rank = lax.axis_index("tensor")
    block_rows = BLOCK_SEQS * CHAIN
    assert block_rows % tok_dev == 0
    dev_chains = tok_dev // CHAIN
    chains = dev_chains // STREAMS
    seg_rows = chains * CHAIN
    weights = (w_qkv, qv_bias, w_out, resid_bias, norm_gain, norm_shift, w_up, up_bias, w_down)
    peer_kind = block_kind[(jnp.arange(n_tensor) * tok_dev) // block_rows]
    out_rows_w = lax.all_to_all(w_out[peer_kind], "tensor", 0, 0, tiled=True)
    outs, ins, grads, smalls = [], [], [], []
    for part in range(STREAMS):
        first_row = jnp.arange(n_tensor) * tok_dev + part * seg_rows
        seg_kind = block_kind[first_row // block_rows]
        chain_ids = (
            jnp.arange(n_tensor)[:, None] * dev_chains + part * chains + jnp.arange(chains)[None, :]
        )
        seg_lens = lengths[chain_ids]
        own_rows = rank * tok_dev + part * seg_rows + jnp.arange(seg_rows)
        row_kind = block_kind[own_rows // block_rows]
        rows = slice(part * seg_rows, (part + 1) * seg_rows)
        out_part, in_part, grad_part, small_part = stream(
            inputs[rows], cotangent[rows], seg_kind, seg_lens, row_kind, out_rows_w, *weights
        )
        outs.append(out_part)
        ins.append(in_part)
        grads.append(grad_part)
        smalls.append(small_part)
    layer_out = jnp.concatenate(outs, axis=0)
    input_grad = jnp.concatenate(ins, axis=0)
    grad_qkv, grad_qv, grad_out_w, grad_up, grad_ubias, grad_down = (
        sum(parts[1:], parts[0]) for parts in zip(*grads)
    )
    small = sum(smalls[1:], smalls[0])
    up_total, down_total = dp_sum_low((grad_up, grad_down))
    qkv_total, out_total = dp_sum_low((grad_qkv, grad_out_w))
    (small_grads,) = exact_sum((small,), "tensor")
    qv_total, ubias_total, small_total = exact_sum((grad_qv, grad_ubias, small_grads), "dp")
    return (
        layer_out,
        input_grad,
        qkv_total,
        qv_total,
        out_total,
        small_total[0],
        small_total[1],
        small_total[2],
        up_total,
        ubias_total,
        down_total,
    )


def solution(mesh):
    return jax.shard_map(
        local,
        mesh=mesh,
        in_specs=(
            P(("dp", "tensor"), None),
            P(("dp", "tensor"), None),
            P("dp"),
            P("dp"),
            P(None, None, None, "tensor"),
            P(None, None, "tensor"),
            P(None, "tensor", None),
            P(),
            P(),
            P(),
            P(None, None, "tensor"),
            P(None, "tensor"),
            P(None, "tensor", None),
        ),
        out_specs=(
            P(("dp", "tensor"), None),
            P(("dp", "tensor"), None),
            P(None, None, None, "tensor"),
            P(None, None, "tensor"),
            P(None, "tensor", None),
            P(),
            P(),
            P(),
            P(None, None, "tensor"),
            P(None, "tensor"),
            P(None, "tensor", None),
        ),
        check_vma=False,
    )
```

```python
import jax
import jax.numpy as jnp
from jax import lax
from jax.sharding import PartitionSpec as P

HEAD_DIM = 64
CHAIN = 128
BLOCK_SEQS = 4
STREAMS = 2


EPSILON = 1e-05
SQRT_HALF = 0.7071067811865476
INV_ROOT_TWO_PI = 0.3989422804014327


def norm_forward(row_data, gain_rows, shift_rows):
    mean_row = jnp.mean(row_data, axis=-1, keepdims=True)
    centred = row_data - mean_row
    var_row = jnp.mean(centred * centred, axis=-1, keepdims=True)
    inv_std = lax.rsqrt(var_row + EPSILON)
    unit_rows = centred * inv_std
    return (unit_rows * gain_rows + shift_rows, unit_rows, inv_std)


def norm_backward(grad_rows, gain_rows, unit_rows, inv_std):
    scaled = grad_rows * gain_rows
    mean_first = jnp.mean(scaled, axis=-1, keepdims=True)
    mean_second = jnp.mean(scaled * unit_rows, axis=-1, keepdims=True)
    return inv_std * (scaled - mean_first - unit_rows * mean_second)


def type_sum(kind_hot, values):
    return jnp.einsum("rt,rd->td", kind_hot, values, precision=lax.Precision.HIGHEST)


def gelu_slope(values):
    return 0.5 * (1.0 + lax.erf(values * SQRT_HALF)) + values * INV_ROOT_TWO_PI * jnp.exp(
        -0.5 * values * values
    )


def gather_rows(local_rows):
    return lax.all_gather(local_rows, "tensor", axis=0, tiled=False)


def scatter_sum(seg_parts):
    n_seg, seg_rows, width = seg_parts.shape
    summed = lax.psum_scatter(
        seg_parts.reshape(n_seg * seg_rows, width).astype(jnp.bfloat16),
        "tensor",
        scatter_dimension=0,
        tiled=True,
    )
    return summed.astype(jnp.float32)


def masked(seg_rows, seg_hot):
    return seg_rows[:, None] * seg_hot[:, :, None, None].astype(seg_rows.dtype)


def kind_sums(seg_hot, seg_totals):
    return jnp.einsum(
        "st,se->te", seg_hot, seg_totals, precision=lax.Precision.HIGHEST
    )


def dp_perm(n, bit):
    return [(j, j ^ bit) for j in range(n)]


def dp_sum_low(parts):
    shapes = [p.shape for p in parts]
    n_dp = lax.axis_size("dp")
    idx = lax.axis_index("dp")
    steps = n_dp.bit_length() - 1
    cur = [p.reshape(-1, p.shape[-1]) for p in parts]
    assert 1 << steps == n_dp and all(c.shape[0] % n_dp == 0 for c in cur)
    for b in range(steps):
        upper = ((idx >> b) & 1) == 1
        halves = [(c[: c.shape[0] // 2], c[c.shape[0] // 2 :]) for c in cur]
        sends = tuple(jnp.where(upper, lo, hi).astype(jnp.bfloat16) for lo, hi in halves)
        gots = lax.ppermute(sends, "dp", dp_perm(n_dp, 1 << b))
        cur = [jnp.where(upper, hi, lo) + g.astype(jnp.float32) for (lo, hi), g in zip(halves, gots)]
    cur = [c.astype(jnp.bfloat16) for c in cur]
    for b in reversed(range(steps)):
        upper = ((idx >> b) & 1) == 1
        gots = lax.ppermute(tuple(cur), "dp", dp_perm(n_dp, 1 << b))
        cur = [
            jnp.where(upper, jnp.concatenate([g, c]), jnp.concatenate([c, g]))
            for c, g in zip(cur, gots)
        ]
    return [c.astype(jnp.float32).reshape(shape) for c, shape in zip(cur, shapes)]


def exact_sum(values, axis):
    n_ax = lax.axis_size(axis)
    steps = n_ax.bit_length() - 1
    assert 1 << steps == n_ax
    for b in range(steps):
        values = tuple(
            v + g for v, g in zip(values, lax.ppermute(values, axis, dp_perm(n_ax, 1 << b)))
        )
    return values


def stream(
    inputs,
    cotangent,
    seg_kind,
    seg_lens,
    row_kind,
    out_rows_w,
    selected,
    resid_bias,
    norm_gain,
    norm_shift,
):
    qkv_sel, qvb_sel, out_sel, up_sel, ubias_sel, down_sel = selected
    n_seg, chains = seg_lens.shape
    seg_rows = chains * CHAIN
    heads_here = qkv_sel.shape[3] // HEAD_DIM
    score_scale = HEAD_DIM ** (-0.5)
    highest = lax.Precision.HIGHEST
    seg_hot = (seg_kind[:, None] == jnp.arange(2)[None, :]).astype(jnp.float32)
    kind_hot = (row_kind[:, None] == jnp.arange(2)[None, :]).astype(jnp.float32)

    def pick(kind_table):
        return jnp.dot(kind_hot, kind_table.astype(jnp.float32), precision=highest)

    def heads(rows):
        return rows.reshape(n_seg, chains, CHAIN, heads_here, HEAD_DIM)

    key_valid = jnp.arange(CHAIN)[None, None, :] < seg_lens[:, :, None]


    input_segs = gather_rows(inputs)
    projected = jnp.einsum(
        "srd,sjde->jsre", input_segs, qkv_sel, preferred_element_type=jnp.float32
    )
    query_rows = (projected[0] + qvb_sel[:, None, 0]).astype(jnp.bfloat16)
    key_rows = projected[1].astype(jnp.bfloat16)
    value_rows = (projected[2] + qvb_sel[:, None, 1]).astype(jnp.bfloat16)

    def probs_of():
        raw_scores = (
            jnp.einsum(
                "scqhd,sckhd->schqk",
                heads(query_rows),
                heads(key_rows),
                preferred_element_type=jnp.float32,
            )
            * score_scale
        )
        return jnp.where(key_valid[:, :, None, None, :], raw_scores, -1e30)

    scores = probs_of()
    row_max = jnp.max(scores, axis=-1, keepdims=True)
    log_total = row_max[..., 0] + jnp.log(jnp.sum(jnp.exp(scores - row_max), axis=-1))
    attn_probs = jnp.exp(scores - log_total[..., None])
    probs_low = attn_probs.astype(jnp.bfloat16)
    mixed = jnp.einsum(
        "schqk,sckhd->scqhd", probs_low, heads(value_rows), preferred_element_type=jnp.float32
    )
    mixed = mixed.reshape(n_seg, seg_rows, -1).astype(jnp.bfloat16)
    mixed_rows = lax.all_to_all(mixed, "tensor", 0, 0, tiled=True)
    attn_rows = jnp.einsum(
        "erc,ecd->rd", mixed_rows, out_rows_w, preferred_element_type=jnp.float32
    )

    hidden_one = inputs.astype(jnp.float32) + attn_rows + pick(resid_bias[:, 0])
    gain_one = pick(norm_gain[:, 0])
    normed, unit_one, inv_one = norm_forward(hidden_one, gain_one, pick(norm_shift[:, 0]))
    normed_low = normed.astype(jnp.bfloat16)
    norm_segs = gather_rows(normed_low)
    pre_act = (
        jnp.einsum("srd,sdf->srf", norm_segs, up_sel, preferred_element_type=jnp.float32)
        + ubias_sel[:, None]
    )
    activ = jax.nn.gelu(pre_act, approximate=False).astype(jnp.bfloat16)
    ffn_parts = jnp.einsum("srf,sfd->srd", activ, down_sel, preferred_element_type=jnp.float32)
    ffn_rows = scatter_sum(ffn_parts)

    hidden_two = normed + ffn_rows + pick(resid_bias[:, 1])
    gain_two = pick(norm_gain[:, 1])
    output_rows, unit_two, inv_two = norm_forward(hidden_two, gain_two, pick(norm_shift[:, 1]))
    layer_out = output_rows.astype(jnp.bfloat16)
    grad_out = cotangent.astype(jnp.float32)
    d_two = norm_backward(grad_out, gain_two, unit_two, inv_two)
    two_segs = gather_rows(d_two.astype(jnp.bfloat16))

    grad_down = jnp.einsum(
        "strf,srd->tfd", masked(activ, seg_hot), two_segs, preferred_element_type=jnp.float32
    )
    d_activ = jnp.einsum(
        "srd,sfd->srf", two_segs, down_sel, preferred_element_type=jnp.float32
    ).astype(jnp.bfloat16)
    d_pre = (d_activ.astype(jnp.float32) * gelu_slope(pre_act)).astype(jnp.bfloat16)
    grad_up = jnp.einsum(
        "strd,srf->tdf", masked(norm_segs, seg_hot), d_pre, preferred_element_type=jnp.float32
    )
    grad_ubias = kind_sums(seg_hot, jnp.sum(d_pre.astype(jnp.float32), axis=1))
    ffn_back = jnp.einsum("srf,sdf->srd", d_pre, up_sel, preferred_element_type=jnp.float32)
    d_normed = scatter_sum(ffn_back) + d_two

    d_one = norm_backward(d_normed, gain_one, unit_one, inv_one)
    gain_grads = jnp.stack(
        [type_sum(kind_hot, d_normed * unit_one), type_sum(kind_hot, grad_out * unit_two)], axis=1
    )
    shift_grads = jnp.stack([type_sum(kind_hot, d_normed), type_sum(kind_hot, grad_out)], axis=1)
    rbias_grads = jnp.stack([type_sum(kind_hot, d_one), type_sum(kind_hot, d_two)], axis=1)
    one_segs = gather_rows(d_one.astype(jnp.bfloat16))

    grad_out_w = jnp.einsum(
        "stre,srd->ted", masked(mixed, seg_hot), one_segs, preferred_element_type=jnp.float32
    )
    d_mixed = jnp.einsum(
        "srd,sed->sre", one_segs, out_sel, preferred_element_type=jnp.float32
    ).astype(jnp.bfloat16)
    d_mixed_heads = heads(d_mixed)
    d_value = jnp.einsum(
        "schqk,scqhd->sckhd", probs_low, d_mixed_heads, preferred_element_type=jnp.float32
    )
    d_value = d_value.reshape(n_seg, seg_rows, -1).astype(jnp.bfloat16)
    d_probs = jnp.einsum(
        "scqhd,sckhd->schqk", d_mixed_heads, heads(value_rows), preferred_element_type=jnp.float32
    )
    prob_dot = jnp.sum(attn_probs * d_probs, axis=-1, keepdims=True)
    d_scores = (attn_probs * (d_probs - prob_dot)).astype(jnp.bfloat16)
    d_query = (
        jnp.einsum(
            "schqk,sckhd->scqhd", d_scores, heads(key_rows), preferred_element_type=jnp.float32
        )
        * score_scale
    )
    d_key = (
        jnp.einsum(
            "schqk,scqhd->sckhd", d_scores, heads(query_rows), preferred_element_type=jnp.float32
        )
        * score_scale
    )
    d_query = d_query.reshape(n_seg, seg_rows, -1).astype(jnp.bfloat16)
    d_key = d_key.reshape(n_seg, seg_rows, -1).astype(jnp.bfloat16)
    d_proj = jnp.stack([d_query, d_key, d_value])
    grad_qkv = jnp.einsum(
        "strd,jsre->tjed", masked(input_segs, seg_hot), d_proj, preferred_element_type=jnp.float32
    )
    grad_qv = jnp.stack(
        [
            kind_sums(seg_hot, jnp.sum(d_query.astype(jnp.float32), axis=1)),
            kind_sums(seg_hot, jnp.sum(d_value.astype(jnp.float32), axis=1)),
        ],
        axis=1,
    )
    qkv_back = jnp.einsum("jsre,sjde->srd", d_proj, qkv_sel, preferred_element_type=jnp.float32)
    input_grad = scatter_sum(qkv_back) + d_one
    small = jnp.stack([rbias_grads, gain_grads, shift_grads])
    return (
        layer_out,
        input_grad,
        (grad_qkv, grad_qv, grad_out_w, grad_up, grad_ubias, grad_down),
        small,
    )


def local(
    inputs,
    cotangent,
    lengths,
    block_kind,
    w_qkv,
    qv_bias,
    w_out,
    resid_bias,
    norm_gain,
    norm_shift,
    w_up,
    up_bias,
    w_down,
):
    tok_dev = inputs.shape[0]
    n_tensor = lax.axis_size("tensor")
    rank = lax.axis_index("tensor")
    block_rows = BLOCK_SEQS * CHAIN
    assert block_rows % tok_dev == 0
    dev_chains = tok_dev // CHAIN
    chains = dev_chains // STREAMS
    seg_rows = chains * CHAIN
    peer_kind = block_kind[(jnp.arange(n_tensor) * tok_dev) // block_rows]
    out_sel = w_out[peer_kind]
    selected = (
        w_qkv[peer_kind],
        qv_bias[peer_kind].astype(jnp.float32),
        out_sel,
        w_up[peer_kind],
        up_bias[peer_kind].astype(jnp.float32),
        w_down[peer_kind],
    )
    out_rows_w = lax.all_to_all(out_sel, "tensor", 0, 0, tiled=True)
    outs, ins, grads, smalls = [], [], [], []
    for part in range(STREAMS):
        chain_ids = (
            jnp.arange(n_tensor)[:, None] * dev_chains + part * chains + jnp.arange(chains)[None, :]
        )
        seg_lens = lengths[chain_ids]
        own_rows = rank * tok_dev + part * seg_rows + jnp.arange(seg_rows)
        row_kind = block_kind[own_rows // block_rows]
        rows = slice(part * seg_rows, (part + 1) * seg_rows)
        out_part, in_part, grad_part, small_part = stream(
            inputs[rows],
            cotangent[rows],
            peer_kind,
            seg_lens,
            row_kind,
            out_rows_w,
            selected,
            resid_bias,
            norm_gain,
            norm_shift,
        )
        outs.append(out_part)
        ins.append(in_part)
        grads.append(grad_part)
        smalls.append(small_part)
    layer_out = jnp.concatenate(outs, axis=0)
    input_grad = jnp.concatenate(ins, axis=0)
    grad_qkv, grad_qv, grad_out_w, grad_up, grad_ubias, grad_down = (
        sum(parts[1:], parts[0]) for parts in zip(*grads)
    )
    small = sum(smalls[1:], smalls[0])
    up_total, down_total = dp_sum_low((grad_up, grad_down))
    qkv_t_total, out_total = dp_sum_low((grad_qkv, grad_out_w))
    qkv_total = jnp.swapaxes(qkv_t_total, 2, 3)
    (small_grads,) = exact_sum((small,), "tensor")
    width = small.shape[-1]
    packed = jnp.concatenate(
        [small_grads.reshape(-1, width), grad_ubias.reshape(-1, width), grad_qv.reshape(-1, width)]
    )
    (packed,) = exact_sum((packed,), "dp")
    n_small, n_ubias = small_grads.size // width, grad_ubias.size // width
    small_total = packed[:n_small].reshape(small_grads.shape)
    ubias_total = packed[n_small : n_small + n_ubias].reshape(grad_ubias.shape)
    qv_total = packed[n_small + n_ubias :].reshape(grad_qv.shape)
    return (
        layer_out,
        input_grad,
        qkv_total,
        qv_total,
        out_total,
        small_total[0],
        small_total[1],
        small_total[2],
        up_total,
        ubias_total,
        down_total,
    )


def solution(mesh):
    return jax.shard_map(
        local,
        mesh=mesh,
        in_specs=(
            P(("dp", "tensor"), None),
            P(("dp", "tensor"), None),
            P("dp"),
            P("dp"),
            P(None, None, None, "tensor"),
            P(None, None, "tensor"),
            P(None, "tensor", None),
            P(),
            P(),
            P(),
            P(None, None, "tensor"),
            P(None, "tensor"),
            P(None, "tensor", None),
        ),
        out_specs=(
            P(("dp", "tensor"), None),
            P(("dp", "tensor"), None),
            P(None, None, None, "tensor"),
            P(None, None, "tensor"),
            P(None, "tensor", None),
            P(),
            P(),
            P(),
            P(None, None, "tensor"),
            P(None, "tensor"),
            P(None, "tensor", None),
        ),
        check_vma=False,
    )
```

```python
import jax
import jax.numpy as jnp
from jax import lax
from jax.sharding import PartitionSpec as P

HEAD_DIM = 64
CHAIN = 128
BLOCK_SEQS = 4
STREAMS = 2


EPSILON = 1e-05
SQRT_HALF = 0.7071067811865476
INV_ROOT_TWO_PI = 0.3989422804014327


def norm_forward(row_data, gain_rows, shift_rows):
    mean_row = jnp.mean(row_data, axis=-1, keepdims=True)
    centred = row_data - mean_row
    var_row = jnp.mean(centred * centred, axis=-1, keepdims=True)
    inv_std = lax.rsqrt(var_row + EPSILON)
    unit_rows = centred * inv_std
    return (unit_rows * gain_rows + shift_rows, unit_rows, inv_std)


def norm_backward(grad_rows, gain_rows, unit_rows, inv_std):
    scaled = grad_rows * gain_rows
    mean_first = jnp.mean(scaled, axis=-1, keepdims=True)
    mean_second = jnp.mean(scaled * unit_rows, axis=-1, keepdims=True)
    return inv_std * (scaled - mean_first - unit_rows * mean_second)


def type_sum(kind_hot, values):
    return jnp.einsum("rt,rd->td", kind_hot, values, precision=lax.Precision.HIGHEST)


def gelu_slope(values):
    return 0.5 * (1.0 + lax.erf(values * SQRT_HALF)) + values * INV_ROOT_TWO_PI * jnp.exp(
        -0.5 * values * values
    )


def gather_rows(local_rows):
    return lax.all_gather(local_rows, "tensor", axis=0, tiled=False)


def scatter_sum(seg_parts):
    n_seg, seg_rows, width = seg_parts.shape
    summed = lax.psum_scatter(
        seg_parts.reshape(n_seg * seg_rows, width).astype(jnp.bfloat16),
        "tensor",
        scatter_dimension=0,
        tiled=True,
    )
    return summed.astype(jnp.float32)


def masked(seg_rows, seg_hot):
    return seg_rows[:, None] * seg_hot[:, :, None, None].astype(seg_rows.dtype)


def kind_sums(seg_hot, seg_totals):
    return jnp.einsum(
        "st,se->te", seg_hot, seg_totals, precision=lax.Precision.HIGHEST
    )


def dp_perm(n, bit):
    return [(j, j ^ bit) for j in range(n)]


def dp_sum_low(parts):
    shapes = [p.shape for p in parts]
    n_dp = lax.axis_size("dp")
    idx = lax.axis_index("dp")
    steps = n_dp.bit_length() - 1
    cur = [p.reshape(-1, p.shape[-1]) for p in parts]
    assert 1 << steps == n_dp and all(c.shape[0] % n_dp == 0 for c in cur)
    for b in range(steps):
        upper = ((idx >> b) & 1) == 1
        halves = [(c[: c.shape[0] // 2], c[c.shape[0] // 2 :]) for c in cur]
        sends = tuple(jnp.where(upper, lo, hi).astype(jnp.bfloat16) for lo, hi in halves)
        gots = lax.ppermute(sends, "dp", dp_perm(n_dp, 1 << b))
        cur = [jnp.where(upper, hi, lo) + g.astype(jnp.float32) for (lo, hi), g in zip(halves, gots)]
    cur = [c.astype(jnp.bfloat16) for c in cur]
    for b in reversed(range(steps)):
        upper = ((idx >> b) & 1) == 1
        gots = lax.ppermute(tuple(cur), "dp", dp_perm(n_dp, 1 << b))
        cur = [
            jnp.where(upper, jnp.concatenate([g, c]), jnp.concatenate([c, g]))
            for c, g in zip(cur, gots)
        ]
    return [c.astype(jnp.float32).reshape(shape) for c, shape in zip(cur, shapes)]


def exact_sum(values, axis):
    n_ax = lax.axis_size(axis)
    steps = n_ax.bit_length() - 1
    assert 1 << steps == n_ax
    for b in range(steps):
        values = tuple(
            v + g for v, g in zip(values, lax.ppermute(values, axis, dp_perm(n_ax, 1 << b)))
        )
    return values


def stream(
    inputs,
    input_segs,
    cotangent,
    seg_kind,
    seg_lens,
    row_kind,
    out_rows_w,
    selected,
    resid_bias,
    norm_gain,
    norm_shift,
):
    qkv_sel, qvb_sel, out_sel, up_sel, ubias_sel, down_sel = selected
    n_seg, chains = seg_lens.shape
    seg_rows = chains * CHAIN
    heads_here = qkv_sel.shape[3] // HEAD_DIM
    score_scale = HEAD_DIM ** (-0.5)
    highest = lax.Precision.HIGHEST
    seg_hot = (seg_kind[:, None] == jnp.arange(2)[None, :]).astype(jnp.float32)
    kind_hot = (row_kind[:, None] == jnp.arange(2)[None, :]).astype(jnp.float32)

    def pick(kind_table):
        return jnp.dot(kind_hot, kind_table.astype(jnp.float32), precision=highest)

    def heads(rows):
        return rows.reshape(n_seg, chains, CHAIN, heads_here, HEAD_DIM)

    key_valid = jnp.arange(CHAIN)[None, None, :] < seg_lens[:, :, None]


    projected = jnp.einsum(
        "srd,sjde->jsre", input_segs, qkv_sel, preferred_element_type=jnp.float32
    )
    query_rows = (projected[0] + qvb_sel[:, None, 0]).astype(jnp.bfloat16)
    key_rows = projected[1].astype(jnp.bfloat16)
    value_rows = (projected[2] + qvb_sel[:, None, 1]).astype(jnp.bfloat16)

    def probs_of():
        raw_scores = (
            jnp.einsum(
                "scqhd,sckhd->schqk",
                heads(query_rows),
                heads(key_rows),
                preferred_element_type=jnp.float32,
            )
            * score_scale
        )
        return jnp.where(key_valid[:, :, None, None, :], raw_scores, -1e30)

    scores = probs_of()
    row_max = jnp.max(scores, axis=-1, keepdims=True)
    log_total = row_max[..., 0] + jnp.log(jnp.sum(jnp.exp(scores - row_max), axis=-1))
    attn_probs = jnp.exp(scores - log_total[..., None])
    probs_low = attn_probs.astype(jnp.bfloat16)
    mixed = jnp.einsum(
        "schqk,sckhd->scqhd", probs_low, heads(value_rows), preferred_element_type=jnp.float32
    )
    mixed = mixed.reshape(n_seg, seg_rows, -1).astype(jnp.bfloat16)
    mixed_rows = lax.all_to_all(mixed, "tensor", 0, 0, tiled=True)
    attn_rows = jnp.einsum(
        "erc,ecd->rd", mixed_rows, out_rows_w, preferred_element_type=jnp.float32
    )

    hidden_one = inputs.astype(jnp.float32) + attn_rows + pick(resid_bias[:, 0])
    gain_one = pick(norm_gain[:, 0])
    normed, unit_one, inv_one = norm_forward(hidden_one, gain_one, pick(norm_shift[:, 0]))
    normed_low = normed.astype(jnp.bfloat16)
    norm_segs = gather_rows(normed_low)
    pre_act = (
        jnp.einsum("srd,sdf->srf", norm_segs, up_sel, preferred_element_type=jnp.float32)
        + ubias_sel[:, None]
    )
    activ = jax.nn.gelu(pre_act, approximate=False).astype(jnp.bfloat16)
    ffn_parts = jnp.einsum("srf,sfd->srd", activ, down_sel, preferred_element_type=jnp.float32)
    ffn_rows = scatter_sum(ffn_parts)

    hidden_two = normed + ffn_rows + pick(resid_bias[:, 1])
    gain_two = pick(norm_gain[:, 1])
    output_rows, unit_two, inv_two = norm_forward(hidden_two, gain_two, pick(norm_shift[:, 1]))
    layer_out = output_rows.astype(jnp.bfloat16)
    grad_out = cotangent.astype(jnp.float32)
    d_two = norm_backward(grad_out, gain_two, unit_two, inv_two)
    two_segs = gather_rows(d_two.astype(jnp.bfloat16))

    grad_down = jnp.einsum(
        "strf,srd->tfd", masked(activ, seg_hot), two_segs, preferred_element_type=jnp.float32
    )
    d_activ = jnp.einsum(
        "srd,sfd->srf", two_segs, down_sel, preferred_element_type=jnp.float32
    ).astype(jnp.bfloat16)
    d_pre = (d_activ.astype(jnp.float32) * gelu_slope(pre_act)).astype(jnp.bfloat16)
    grad_up = jnp.einsum(
        "strd,srf->tdf", masked(norm_segs, seg_hot), d_pre, preferred_element_type=jnp.float32
    )
    grad_ubias = kind_sums(seg_hot, jnp.sum(d_pre.astype(jnp.float32), axis=1))
    ffn_back = jnp.einsum("srf,sdf->srd", d_pre, up_sel, preferred_element_type=jnp.float32)
    d_normed = scatter_sum(ffn_back) + d_two

    d_one = norm_backward(d_normed, gain_one, unit_one, inv_one)
    gain_grads = jnp.stack(
        [type_sum(kind_hot, d_normed * unit_one), type_sum(kind_hot, grad_out * unit_two)], axis=1
    )
    shift_grads = jnp.stack([type_sum(kind_hot, d_normed), type_sum(kind_hot, grad_out)], axis=1)
    rbias_grads = jnp.stack([type_sum(kind_hot, d_one), type_sum(kind_hot, d_two)], axis=1)
    one_segs = gather_rows(d_one.astype(jnp.bfloat16))

    grad_out_w = jnp.einsum(
        "stre,srd->ted", masked(mixed, seg_hot), one_segs, preferred_element_type=jnp.float32
    )
    d_mixed = jnp.einsum(
        "srd,sed->sre", one_segs, out_sel, preferred_element_type=jnp.float32
    ).astype(jnp.bfloat16)
    d_mixed_heads = heads(d_mixed)
    d_value = jnp.einsum(
        "schqk,scqhd->sckhd", probs_low, d_mixed_heads, preferred_element_type=jnp.float32
    )
    d_value = d_value.reshape(n_seg, seg_rows, -1).astype(jnp.bfloat16)
    d_probs = jnp.einsum(
        "scqhd,sckhd->schqk", d_mixed_heads, heads(value_rows), preferred_element_type=jnp.float32
    )
    prob_dot = jnp.sum(attn_probs * d_probs, axis=-1, keepdims=True)
    d_scores = (attn_probs * (d_probs - prob_dot)).astype(jnp.bfloat16)
    d_query = (
        jnp.einsum(
            "schqk,sckhd->scqhd", d_scores, heads(key_rows), preferred_element_type=jnp.float32
        )
        * score_scale
    )
    d_key = (
        jnp.einsum(
            "schqk,scqhd->sckhd", d_scores, heads(query_rows), preferred_element_type=jnp.float32
        )
        * score_scale
    )
    d_query = d_query.reshape(n_seg, seg_rows, -1).astype(jnp.bfloat16)
    d_key = d_key.reshape(n_seg, seg_rows, -1).astype(jnp.bfloat16)
    d_proj = jnp.stack([d_query, d_key, d_value])
    grad_qkv = jnp.einsum(
        "strd,jsre->tjed", masked(input_segs, seg_hot), d_proj, preferred_element_type=jnp.float32
    )
    grad_qv = jnp.stack(
        [
            kind_sums(seg_hot, jnp.sum(d_query.astype(jnp.float32), axis=1)),
            kind_sums(seg_hot, jnp.sum(d_value.astype(jnp.float32), axis=1)),
        ],
        axis=1,
    )
    qkv_back = jnp.einsum("jsre,sjde->srd", d_proj, qkv_sel, preferred_element_type=jnp.float32)
    input_grad = scatter_sum(qkv_back) + d_one
    small = jnp.stack([rbias_grads, gain_grads, shift_grads])
    return (
        layer_out,
        input_grad,
        (grad_qkv, grad_qv, grad_out_w, grad_up, grad_ubias, grad_down),
        small,
    )


def local(
    inputs,
    cotangent,
    lengths,
    block_kind,
    w_qkv,
    qv_bias,
    w_out,
    resid_bias,
    norm_gain,
    norm_shift,
    w_up,
    up_bias,
    w_down,
):
    tok_dev = inputs.shape[0]
    n_tensor = lax.axis_size("tensor")
    rank = lax.axis_index("tensor")
    block_rows = BLOCK_SEQS * CHAIN
    assert block_rows % tok_dev == 0
    dev_chains = tok_dev // CHAIN
    chains = dev_chains // STREAMS
    seg_rows = chains * CHAIN
    peer_kind = block_kind[(jnp.arange(n_tensor) * tok_dev) // block_rows]
    out_sel = w_out[peer_kind]
    selected = (
        w_qkv[peer_kind],
        qv_bias[peer_kind].astype(jnp.float32),
        out_sel,
        w_up[peer_kind],
        up_bias[peer_kind].astype(jnp.float32),
        w_down[peer_kind],
    )
    row_parts = [slice(part * seg_rows, (part + 1) * seg_rows) for part in range(STREAMS)]
    gathered = [gather_rows(inputs[rows]) for rows in row_parts]
    out_sel, gathered[0] = lax.optimization_barrier((out_sel, gathered[0]))
    out_rows_w = lax.all_to_all(out_sel, "tensor", 0, 0, tiled=True)
    outs, ins, grads, smalls = [], [], [], []
    for part in range(STREAMS):
        chain_ids = (
            jnp.arange(n_tensor)[:, None] * dev_chains + part * chains + jnp.arange(chains)[None, :]
        )
        seg_lens = lengths[chain_ids]
        own_rows = rank * tok_dev + part * seg_rows + jnp.arange(seg_rows)
        row_kind = block_kind[own_rows // block_rows]
        rows = row_parts[part]
        out_part, in_part, grad_part, small_part = stream(
            inputs[rows],
            gathered[part],
            cotangent[rows],
            peer_kind,
            seg_lens,
            row_kind,
            out_rows_w,
            selected,
            resid_bias,
            norm_gain,
            norm_shift,
        )
        outs.append(out_part)
        ins.append(in_part)
        grads.append(grad_part)
        smalls.append(small_part)
    layer_out = jnp.concatenate(outs, axis=0)
    input_grad = jnp.concatenate(ins, axis=0)
    grad_qkv, grad_qv, grad_out_w, grad_up, grad_ubias, grad_down = (
        sum(parts[1:], parts[0]) for parts in zip(*grads)
    )
    small = sum(smalls[1:], smalls[0])
    up_total, down_total = dp_sum_low((grad_up, grad_down))
    qkv_t_total, out_total = dp_sum_low((grad_qkv, grad_out_w))
    qkv_total = jnp.swapaxes(qkv_t_total, 2, 3)
    (small_grads,) = exact_sum((small,), "tensor")
    width = small.shape[-1]
    packed = jnp.concatenate(
        [small_grads.reshape(-1, width), grad_ubias.reshape(-1, width), grad_qv.reshape(-1, width)]
    )
    (packed,) = exact_sum((packed,), "dp")
    n_small, n_ubias = small_grads.size // width, grad_ubias.size // width
    small_total = packed[:n_small].reshape(small_grads.shape)
    ubias_total = packed[n_small : n_small + n_ubias].reshape(grad_ubias.shape)
    qv_total = packed[n_small + n_ubias :].reshape(grad_qv.shape)
    return (
        layer_out,
        input_grad,
        qkv_total,
        qv_total,
        out_total,
        small_total[0],
        small_total[1],
        small_total[2],
        up_total,
        ubias_total,
        down_total,
    )


def solution(mesh):
    return jax.shard_map(
        local,
        mesh=mesh,
        in_specs=(
            P(("dp", "tensor"), None),
            P(("dp", "tensor"), None),
            P("dp"),
            P("dp"),
            P(None, None, None, "tensor"),
            P(None, None, "tensor"),
            P(None, "tensor", None),
            P(),
            P(),
            P(),
            P(None, None, "tensor"),
            P(None, "tensor"),
            P(None, "tensor", None),
        ),
        out_specs=(
            P(("dp", "tensor"), None),
            P(("dp", "tensor"), None),
            P(None, None, None, "tensor"),
            P(None, None, "tensor"),
            P(None, "tensor", None),
            P(),
            P(),
            P(),
            P(None, None, "tensor"),
            P(None, "tensor"),
            P(None, "tensor", None),
        ),
        check_vma=False,
    )
```

```python
import jax
import jax.numpy as jnp
from jax import lax
from jax.sharding import PartitionSpec as P

HEAD_DIM = 64
CHAIN = 128
BLOCK_SEQS = 4
STREAMS = 2


EPSILON = 1e-05
SQRT_HALF = 0.7071067811865476
INV_ROOT_TWO_PI = 0.3989422804014327


def norm_forward(row_data, gain_rows, shift_rows):
    mean_row = jnp.mean(row_data, axis=-1, keepdims=True)
    centred = row_data - mean_row
    var_row = jnp.mean(centred * centred, axis=-1, keepdims=True)
    inv_std = lax.rsqrt(var_row + EPSILON)
    unit_rows = centred * inv_std
    return (unit_rows * gain_rows + shift_rows, unit_rows, inv_std)


def norm_backward(grad_rows, gain_rows, unit_rows, inv_std):
    scaled = grad_rows * gain_rows
    mean_first = jnp.mean(scaled, axis=-1, keepdims=True)
    mean_second = jnp.mean(scaled * unit_rows, axis=-1, keepdims=True)
    return inv_std * (scaled - mean_first - unit_rows * mean_second)


def type_sum(kind_hot, values):
    return jnp.einsum("rt,rd->td", kind_hot, values, precision=lax.Precision.HIGHEST)


def gelu_slope(values):
    return 0.5 * (1.0 + lax.erf(values * SQRT_HALF)) + values * INV_ROOT_TWO_PI * jnp.exp(
        -0.5 * values * values
    )


def gather_rows(local_rows):
    return lax.all_gather(local_rows, "tensor", axis=0, tiled=False)


def scatter_sum(seg_parts):
    n_seg, seg_rows, width = seg_parts.shape
    summed = lax.psum_scatter(
        seg_parts.reshape(n_seg * seg_rows, width).astype(jnp.bfloat16),
        "tensor",
        scatter_dimension=0,
        tiled=True,
    )
    return summed.astype(jnp.float32)


def masked(seg_rows, seg_hot):
    return seg_rows[:, None] * seg_hot[:, :, None, None].astype(seg_rows.dtype)


def kind_sums(seg_hot, seg_totals):
    return jnp.einsum(
        "st,se->te", seg_hot, seg_totals, precision=lax.Precision.HIGHEST
    )


def dp_perm(n, bit):
    return [(j, j ^ bit) for j in range(n)]


def dp_sum_low(parts):
    shapes = [p.shape for p in parts]
    n_dp = lax.axis_size("dp")
    idx = lax.axis_index("dp")
    steps = n_dp.bit_length() - 1
    cur = [p.reshape(-1, p.shape[-1]) for p in parts]
    assert 1 << steps == n_dp and all(c.shape[0] % n_dp == 0 for c in cur)
    for b in range(steps):
        upper = ((idx >> b) & 1) == 1
        halves = [(c[: c.shape[0] // 2], c[c.shape[0] // 2 :]) for c in cur]
        sends = tuple(jnp.where(upper, lo, hi).astype(jnp.bfloat16) for lo, hi in halves)
        gots = lax.ppermute(sends, "dp", dp_perm(n_dp, 1 << b))
        cur = [jnp.where(upper, hi, lo) + g.astype(jnp.float32) for (lo, hi), g in zip(halves, gots)]
    cur = [c.astype(jnp.bfloat16) for c in cur]
    for b in reversed(range(steps)):
        upper = ((idx >> b) & 1) == 1
        gots = lax.ppermute(tuple(cur), "dp", dp_perm(n_dp, 1 << b))
        cur = [
            jnp.where(upper, jnp.concatenate([g, c]), jnp.concatenate([c, g]))
            for c, g in zip(cur, gots)
        ]
    return [c.astype(jnp.float32).reshape(shape) for c, shape in zip(cur, shapes)]


def exact_sum(values, axis):
    n_ax = lax.axis_size(axis)
    steps = n_ax.bit_length() - 1
    assert 1 << steps == n_ax
    for b in range(steps):
        values = tuple(
            v + g for v, g in zip(values, lax.ppermute(values, axis, dp_perm(n_ax, 1 << b)))
        )
    return values


def stream(
    inputs,
    input_segs,
    cotangent,
    seg_kind,
    seg_lens,
    row_kind,
    out_rows_w,
    selected,
    resid_bias,
    norm_gain,
    norm_shift,
):
    qkv_sel, qvb_sel, out_sel, up_sel, ubias_sel, down_sel = selected
    n_seg, chains = seg_lens.shape
    seg_rows = chains * CHAIN
    heads_here = qkv_sel.shape[3] // HEAD_DIM
    score_scale = HEAD_DIM ** (-0.5)
    highest = lax.Precision.HIGHEST
    seg_hot = (seg_kind[:, None] == jnp.arange(2)[None, :]).astype(jnp.float32)
    kind_hot = (row_kind[:, None] == jnp.arange(2)[None, :]).astype(jnp.float32)

    def pick(kind_table):
        return jnp.dot(kind_hot, kind_table.astype(jnp.float32), precision=highest)

    def heads(rows):
        return rows.reshape(n_seg, chains, CHAIN, heads_here, HEAD_DIM)

    key_valid = jnp.arange(CHAIN)[None, None, :] < seg_lens[:, :, None]


    projected = jnp.einsum(
        "srd,sjde->jsre", input_segs, qkv_sel, preferred_element_type=jnp.float32
    )
    query_rows = (projected[0] + qvb_sel[:, None, 0]).astype(jnp.bfloat16)
    key_rows = projected[1].astype(jnp.bfloat16)
    value_rows = (projected[2] + qvb_sel[:, None, 1]).astype(jnp.bfloat16)

    def probs_of():
        raw_scores = (
            jnp.einsum(
                "scqhd,sckhd->schqk",
                heads(query_rows),
                heads(key_rows),
                preferred_element_type=jnp.float32,
            )
            * score_scale
        )
        return jnp.where(key_valid[:, :, None, None, :], raw_scores, -1e30)

    scores = probs_of()
    row_max = jnp.max(scores, axis=-1, keepdims=True)
    log_total = row_max[..., 0] + jnp.log(jnp.sum(jnp.exp(scores - row_max), axis=-1))
    attn_probs = jnp.exp(scores - log_total[..., None])
    probs_low = attn_probs.astype(jnp.bfloat16)
    mixed = jnp.einsum(
        "schqk,sckhd->scqhd", probs_low, heads(value_rows), preferred_element_type=jnp.float32
    )
    mixed = mixed.reshape(n_seg, seg_rows, -1).astype(jnp.bfloat16)
    if out_rows_w is None:
        attn_rows = scatter_sum(
            jnp.einsum("sre,sed->srd", mixed, out_sel, preferred_element_type=jnp.float32)
        )
    else:
        mixed_rows = lax.all_to_all(mixed, "tensor", 0, 0, tiled=True)
        attn_rows = jnp.einsum(
            "erc,ecd->rd", mixed_rows, out_rows_w, preferred_element_type=jnp.float32
        )

    hidden_one = inputs.astype(jnp.float32) + attn_rows + pick(resid_bias[:, 0])
    gain_one = pick(norm_gain[:, 0])
    normed, unit_one, inv_one = norm_forward(hidden_one, gain_one, pick(norm_shift[:, 0]))
    normed_low = normed.astype(jnp.bfloat16)
    norm_segs = gather_rows(normed_low)
    pre_act = (
        jnp.einsum("srd,sdf->srf", norm_segs, up_sel, preferred_element_type=jnp.float32)
        + ubias_sel[:, None]
    )
    activ = jax.nn.gelu(pre_act, approximate=False).astype(jnp.bfloat16)
    ffn_parts = jnp.einsum("srf,sfd->srd", activ, down_sel, preferred_element_type=jnp.float32)
    ffn_rows = scatter_sum(ffn_parts)

    hidden_two = normed + ffn_rows + pick(resid_bias[:, 1])
    gain_two = pick(norm_gain[:, 1])
    output_rows, unit_two, inv_two = norm_forward(hidden_two, gain_two, pick(norm_shift[:, 1]))
    layer_out = output_rows.astype(jnp.bfloat16)
    grad_out = cotangent.astype(jnp.float32)
    d_two = norm_backward(grad_out, gain_two, unit_two, inv_two)
    two_segs = gather_rows(d_two.astype(jnp.bfloat16))

    grad_down = jnp.einsum(
        "strf,srd->tfd", masked(activ, seg_hot), two_segs, preferred_element_type=jnp.float32
    )
    d_activ = jnp.einsum(
        "srd,sfd->srf", two_segs, down_sel, preferred_element_type=jnp.float32
    ).astype(jnp.bfloat16)
    d_pre = (d_activ.astype(jnp.float32) * gelu_slope(pre_act)).astype(jnp.bfloat16)
    grad_up = jnp.einsum(
        "strd,srf->tdf", masked(norm_segs, seg_hot), d_pre, preferred_element_type=jnp.float32
    )
    grad_ubias = kind_sums(seg_hot, jnp.sum(d_pre.astype(jnp.float32), axis=1))
    ffn_back = jnp.einsum("srf,sdf->srd", d_pre, up_sel, preferred_element_type=jnp.float32)
    d_normed = scatter_sum(ffn_back) + d_two

    d_one = norm_backward(d_normed, gain_one, unit_one, inv_one)
    gain_grads = jnp.stack(
        [type_sum(kind_hot, d_normed * unit_one), type_sum(kind_hot, grad_out * unit_two)], axis=1
    )
    shift_grads = jnp.stack([type_sum(kind_hot, d_normed), type_sum(kind_hot, grad_out)], axis=1)
    rbias_grads = jnp.stack([type_sum(kind_hot, d_one), type_sum(kind_hot, d_two)], axis=1)
    one_segs = gather_rows(d_one.astype(jnp.bfloat16))

    grad_out_w = jnp.einsum(
        "stre,srd->ted", masked(mixed, seg_hot), one_segs, preferred_element_type=jnp.float32
    )
    d_mixed = jnp.einsum(
        "srd,sed->sre", one_segs, out_sel, preferred_element_type=jnp.float32
    ).astype(jnp.bfloat16)
    d_mixed_heads = heads(d_mixed)
    d_value = jnp.einsum(
        "schqk,scqhd->sckhd", probs_low, d_mixed_heads, preferred_element_type=jnp.float32
    )
    d_value = d_value.reshape(n_seg, seg_rows, -1).astype(jnp.bfloat16)
    d_probs = jnp.einsum(
        "scqhd,sckhd->schqk", d_mixed_heads, heads(value_rows), preferred_element_type=jnp.float32
    )
    prob_dot = jnp.sum(attn_probs * d_probs, axis=-1, keepdims=True)
    d_scores = (attn_probs * (d_probs - prob_dot)).astype(jnp.bfloat16)
    d_query = (
        jnp.einsum(
            "schqk,sckhd->scqhd", d_scores, heads(key_rows), preferred_element_type=jnp.float32
        )
        * score_scale
    )
    d_key = (
        jnp.einsum(
            "schqk,scqhd->sckhd", d_scores, heads(query_rows), preferred_element_type=jnp.float32
        )
        * score_scale
    )
    d_query = d_query.reshape(n_seg, seg_rows, -1).astype(jnp.bfloat16)
    d_key = d_key.reshape(n_seg, seg_rows, -1).astype(jnp.bfloat16)
    d_proj = jnp.stack([d_query, d_key, d_value])
    grad_qkv = jnp.einsum(
        "strd,jsre->tjed", masked(input_segs, seg_hot), d_proj, preferred_element_type=jnp.float32
    )
    grad_qv = jnp.stack(
        [
            kind_sums(seg_hot, jnp.sum(d_query.astype(jnp.float32), axis=1)),
            kind_sums(seg_hot, jnp.sum(d_value.astype(jnp.float32), axis=1)),
        ],
        axis=1,
    )
    qkv_back = jnp.einsum("jsre,sjde->srd", d_proj, qkv_sel, preferred_element_type=jnp.float32)
    input_grad = scatter_sum(qkv_back) + d_one
    small = jnp.stack([rbias_grads, gain_grads, shift_grads])
    return (
        layer_out,
        input_grad,
        (grad_qkv, grad_qv, grad_out_w, grad_up, grad_ubias, grad_down),
        small,
    )


def local(
    inputs,
    cotangent,
    lengths,
    block_kind,
    w_qkv,
    qv_bias,
    w_out,
    resid_bias,
    norm_gain,
    norm_shift,
    w_up,
    up_bias,
    w_down,
):
    tok_dev = inputs.shape[0]
    n_tensor = lax.axis_size("tensor")
    rank = lax.axis_index("tensor")
    block_rows = BLOCK_SEQS * CHAIN
    assert block_rows % tok_dev == 0
    dev_chains = tok_dev // CHAIN
    chains = dev_chains // STREAMS
    seg_rows = chains * CHAIN
    peer_kind = block_kind[(jnp.arange(n_tensor) * tok_dev) // block_rows]
    out_sel = w_out[peer_kind]
    selected = (
        w_qkv[peer_kind],
        qv_bias[peer_kind].astype(jnp.float32),
        out_sel,
        w_up[peer_kind],
        up_bias[peer_kind].astype(jnp.float32),
        w_down[peer_kind],
    )
    row_parts = [slice(part * seg_rows, (part + 1) * seg_rows) for part in range(STREAMS)]
    gathered = [gather_rows(inputs[rows]) for rows in row_parts]
    out_sel, gathered[0] = lax.optimization_barrier((out_sel, gathered[0]))
    out_rows_w = lax.all_to_all(out_sel, "tensor", 0, 0, tiled=True)
    outs, ins, grads, smalls = [], [], [], []
    for part in range(STREAMS):
        chain_ids = (
            jnp.arange(n_tensor)[:, None] * dev_chains + part * chains + jnp.arange(chains)[None, :]
        )
        seg_lens = lengths[chain_ids]
        own_rows = rank * tok_dev + part * seg_rows + jnp.arange(seg_rows)
        row_kind = block_kind[own_rows // block_rows]
        rows = row_parts[part]
        out_part, in_part, grad_part, small_part = stream(
            inputs[rows],
            gathered[part],
            cotangent[rows],
            peer_kind,
            seg_lens,
            row_kind,
            out_rows_w if part > 0 else None,
            selected,
            resid_bias,
            norm_gain,
            norm_shift,
        )
        outs.append(out_part)
        ins.append(in_part)
        grads.append(grad_part)
        smalls.append(small_part)
    layer_out = jnp.concatenate(outs, axis=0)
    input_grad = jnp.concatenate(ins, axis=0)
    grad_qkv, grad_qv, grad_out_w, grad_up, grad_ubias, grad_down = (
        sum(parts[1:], parts[0]) for parts in zip(*grads)
    )
    small = sum(smalls[1:], smalls[0])
    up_total, down_total = dp_sum_low((grad_up, grad_down))
    qkv_t_total, out_total = dp_sum_low((grad_qkv, grad_out_w))
    qkv_total = jnp.swapaxes(qkv_t_total, 2, 3)
    (small_grads,) = exact_sum((small,), "tensor")
    width = small.shape[-1]
    packed = jnp.concatenate(
        [small_grads.reshape(-1, width), grad_ubias.reshape(-1, width), grad_qv.reshape(-1, width)]
    )
    (packed,) = exact_sum((packed,), "dp")
    n_small, n_ubias = small_grads.size // width, grad_ubias.size // width
    small_total = packed[:n_small].reshape(small_grads.shape)
    ubias_total = packed[n_small : n_small + n_ubias].reshape(grad_ubias.shape)
    qv_total = packed[n_small + n_ubias :].reshape(grad_qv.shape)
    return (
        layer_out,
        input_grad,
        qkv_total,
        qv_total,
        out_total,
        small_total[0],
        small_total[1],
        small_total[2],
        up_total,
        ubias_total,
        down_total,
    )


def solution(mesh):
    return jax.shard_map(
        local,
        mesh=mesh,
        in_specs=(
            P(("dp", "tensor"), None),
            P(("dp", "tensor"), None),
            P("dp"),
            P("dp"),
            P(None, None, None, "tensor"),
            P(None, None, "tensor"),
            P(None, "tensor", None),
            P(),
            P(),
            P(),
            P(None, None, "tensor"),
            P(None, "tensor"),
            P(None, "tensor", None),
        ),
        out_specs=(
            P(("dp", "tensor"), None),
            P(("dp", "tensor"), None),
            P(None, None, None, "tensor"),
            P(None, None, "tensor"),
            P(None, "tensor", None),
            P(),
            P(),
            P(),
            P(None, None, "tensor"),
            P(None, "tensor"),
            P(None, "tensor", None),
        ),
        check_vma=False,
    )
```

```python
import jax
import jax.numpy as jnp
from jax import lax
from jax.sharding import PartitionSpec as P

HEAD_DIM = 64
CHAIN = 128
BLOCK_SEQS = 4
STREAMS = 2


EPSILON = 1e-05
SQRT_HALF = 0.7071067811865476
INV_ROOT_TWO_PI = 0.3989422804014327


def norm_forward(row_data, gain_rows, shift_rows):
    mean_row = jnp.mean(row_data, axis=-1, keepdims=True)
    centred = row_data - mean_row
    var_row = jnp.mean(centred * centred, axis=-1, keepdims=True)
    inv_std = lax.rsqrt(var_row + EPSILON)
    unit_rows = centred * inv_std
    return (unit_rows * gain_rows + shift_rows, unit_rows, inv_std)


def norm_backward(grad_rows, gain_rows, unit_rows, inv_std):
    scaled = grad_rows * gain_rows
    mean_first = jnp.mean(scaled, axis=-1, keepdims=True)
    mean_second = jnp.mean(scaled * unit_rows, axis=-1, keepdims=True)
    return inv_std * (scaled - mean_first - unit_rows * mean_second)


def type_sum(kind_hot, values):
    return jnp.einsum("rt,rd->td", kind_hot, values, precision=lax.Precision.HIGHEST)


def gelu_slope(values):
    return 0.5 * (1.0 + lax.erf(values * SQRT_HALF)) + values * INV_ROOT_TWO_PI * jnp.exp(
        -0.5 * values * values
    )


def gather_rows(local_rows):
    return lax.all_gather(local_rows, "tensor", axis=0, tiled=False)


def scatter_sum(seg_parts):
    n_seg, seg_rows, width = seg_parts.shape
    summed = lax.psum_scatter(
        seg_parts.reshape(n_seg * seg_rows, width).astype(jnp.bfloat16),
        "tensor",
        scatter_dimension=0,
        tiled=True,
    )
    return summed.astype(jnp.float32)


def masked(seg_rows, seg_hot):
    return seg_rows[:, None] * seg_hot[:, :, None, None].astype(seg_rows.dtype)


def kind_sums(seg_hot, seg_totals):
    return jnp.einsum(
        "st,se->te", seg_hot, seg_totals, precision=lax.Precision.HIGHEST
    )


def dp_perm(n, bit):
    return [(j, j ^ bit) for j in range(n)]


def dp_sum_low(parts):
    shapes = [p.shape for p in parts]
    n_dp = lax.axis_size("dp")
    idx = lax.axis_index("dp")
    steps = n_dp.bit_length() - 1
    cur = [p.reshape(-1, p.shape[-1]) for p in parts]
    assert 1 << steps == n_dp and all(c.shape[0] % n_dp == 0 for c in cur)
    for b in range(steps):
        upper = ((idx >> b) & 1) == 1
        halves = [(c[: c.shape[0] // 2], c[c.shape[0] // 2 :]) for c in cur]
        sends = tuple(jnp.where(upper, lo, hi).astype(jnp.bfloat16) for lo, hi in halves)
        gots = lax.ppermute(sends, "dp", dp_perm(n_dp, 1 << b))
        cur = [jnp.where(upper, hi, lo) + g.astype(jnp.float32) for (lo, hi), g in zip(halves, gots)]
    cur = [c.astype(jnp.bfloat16) for c in cur]
    for b in reversed(range(steps)):
        upper = ((idx >> b) & 1) == 1
        gots = lax.ppermute(tuple(cur), "dp", dp_perm(n_dp, 1 << b))
        cur = [
            jnp.where(upper, jnp.concatenate([g, c]), jnp.concatenate([c, g]))
            for c, g in zip(cur, gots)
        ]
    return [c.astype(jnp.float32).reshape(shape) for c, shape in zip(cur, shapes)]


def exact_sum(values, axis):
    n_ax = lax.axis_size(axis)
    steps = n_ax.bit_length() - 1
    assert 1 << steps == n_ax
    for b in range(steps):
        values = tuple(
            v + g for v, g in zip(values, lax.ppermute(values, axis, dp_perm(n_ax, 1 << b)))
        )
    return values


def stream(
    inputs,
    cotangent,
    seg_kind,
    seg_lens,
    row_kind,
    out_rows_w,
    w_qkv,
    qv_bias,
    w_out,
    resid_bias,
    norm_gain,
    norm_shift,
    w_up,
    up_bias,
    w_down,
):
    n_seg, chains = seg_lens.shape
    seg_rows = chains * CHAIN
    heads_here = w_qkv.shape[3] // HEAD_DIM
    score_scale = HEAD_DIM ** (-0.5)
    highest = lax.Precision.HIGHEST
    seg_hot = (seg_kind[:, None] == jnp.arange(2)[None, :]).astype(jnp.float32)
    kind_hot = (row_kind[:, None] == jnp.arange(2)[None, :]).astype(jnp.float32)

    def pick(kind_table):
        return jnp.dot(kind_hot, kind_table.astype(jnp.float32), precision=highest)

    def heads(rows):
        return rows.reshape(n_seg, chains, CHAIN, heads_here, HEAD_DIM)

    key_valid = jnp.arange(CHAIN)[None, None, :] < seg_lens[:, :, None]

    qkv_sel = w_qkv[seg_kind]
    qvb_sel = qv_bias[seg_kind].astype(jnp.float32)
    out_sel = w_out[seg_kind]
    up_sel = w_up[seg_kind]
    ubias_sel = up_bias[seg_kind].astype(jnp.float32)
    down_sel = w_down[seg_kind]

    input_segs = gather_rows(inputs)
    projected = jnp.einsum(
        "srd,sjde->jsre", input_segs, qkv_sel, preferred_element_type=jnp.float32
    )
    query_rows = (projected[0] + qvb_sel[:, None, 0]).astype(jnp.bfloat16)
    key_rows = projected[1].astype(jnp.bfloat16)
    value_rows = (projected[2] + qvb_sel[:, None, 1]).astype(jnp.bfloat16)

    def probs_of():
        raw_scores = (
            jnp.einsum(
                "scqhd,sckhd->schqk",
                heads(query_rows),
                heads(key_rows),
                preferred_element_type=jnp.float32,
            )
            * score_scale
        )
        return jnp.where(key_valid[:, :, None, None, :], raw_scores, -1e30)

    scores = probs_of()
    row_max = jnp.max(scores, axis=-1, keepdims=True)
    log_total = row_max[..., 0] + jnp.log(jnp.sum(jnp.exp(scores - row_max), axis=-1))
    attn_probs = jnp.exp(scores - log_total[..., None])
    probs_low = attn_probs.astype(jnp.bfloat16)
    mixed = jnp.einsum(
        "schqk,sckhd->scqhd", probs_low, heads(value_rows), preferred_element_type=jnp.float32
    )
    mixed = mixed.reshape(n_seg, seg_rows, -1).astype(jnp.bfloat16)
    mixed_rows = lax.all_to_all(mixed, "tensor", 0, 0, tiled=True)
    attn_rows = jnp.einsum(
        "erc,ecd->rd", mixed_rows, out_rows_w, preferred_element_type=jnp.float32
    )

    hidden_one = inputs.astype(jnp.float32) + attn_rows + pick(resid_bias[:, 0])
    gain_one = pick(norm_gain[:, 0])
    normed, unit_one, inv_one = norm_forward(hidden_one, gain_one, pick(norm_shift[:, 0]))
    normed_low = normed.astype(jnp.bfloat16)
    norm_segs = gather_rows(normed_low)
    pre_act = (
        jnp.einsum("srd,sdf->srf", norm_segs, up_sel, preferred_element_type=jnp.float32)
        + ubias_sel[:, None]
    )
    activ = jax.nn.gelu(pre_act, approximate=False).astype(jnp.bfloat16)
    ffn_parts = jnp.einsum("srf,sfd->srd", activ, down_sel, preferred_element_type=jnp.float32)
    ffn_rows = scatter_sum(ffn_parts)

    hidden_two = normed + ffn_rows + pick(resid_bias[:, 1])
    gain_two = pick(norm_gain[:, 1])
    output_rows, unit_two, inv_two = norm_forward(hidden_two, gain_two, pick(norm_shift[:, 1]))
    layer_out = output_rows.astype(jnp.bfloat16)
    grad_out = cotangent.astype(jnp.float32)
    d_two = norm_backward(grad_out, gain_two, unit_two, inv_two)
    two_segs = gather_rows(d_two.astype(jnp.bfloat16))

    grad_down = jnp.einsum(
        "strf,srd->tfd", masked(activ, seg_hot), two_segs, preferred_element_type=jnp.float32
    )
    d_activ = jnp.einsum(
        "srd,sfd->srf", two_segs, down_sel, preferred_element_type=jnp.float32
    ).astype(jnp.bfloat16)
    d_pre = (d_activ.astype(jnp.float32) * gelu_slope(pre_act)).astype(jnp.bfloat16)
    grad_up = jnp.einsum(
        "strd,srf->tdf", masked(norm_segs, seg_hot), d_pre, preferred_element_type=jnp.float32
    )
    grad_ubias = kind_sums(seg_hot, jnp.sum(d_pre.astype(jnp.float32), axis=1))
    ffn_back = jnp.einsum("srf,sdf->srd", d_pre, up_sel, preferred_element_type=jnp.float32)
    d_normed = scatter_sum(ffn_back) + d_two

    d_one = norm_backward(d_normed, gain_one, unit_one, inv_one)
    gain_grads = jnp.stack(
        [type_sum(kind_hot, d_normed * unit_one), type_sum(kind_hot, grad_out * unit_two)], axis=1
    )
    shift_grads = jnp.stack([type_sum(kind_hot, d_normed), type_sum(kind_hot, grad_out)], axis=1)
    rbias_grads = jnp.stack([type_sum(kind_hot, d_one), type_sum(kind_hot, d_two)], axis=1)
    one_segs = gather_rows(d_one.astype(jnp.bfloat16))

    grad_out_w = jnp.einsum(
        "stre,srd->ted", masked(mixed, seg_hot), one_segs, preferred_element_type=jnp.float32
    )
    d_mixed = jnp.einsum(
        "srd,sed->sre", one_segs, out_sel, preferred_element_type=jnp.float32
    ).astype(jnp.bfloat16)
    d_mixed_heads = heads(d_mixed)
    d_value = jnp.einsum(
        "schqk,scqhd->sckhd", probs_low, d_mixed_heads, preferred_element_type=jnp.float32
    )
    d_value = d_value.reshape(n_seg, seg_rows, -1).astype(jnp.bfloat16)
    d_probs = jnp.einsum(
        "scqhd,sckhd->schqk", d_mixed_heads, heads(value_rows), preferred_element_type=jnp.float32
    )
    prob_dot = jnp.sum(attn_probs * d_probs, axis=-1, keepdims=True)
    d_scores = (attn_probs * (d_probs - prob_dot)).astype(jnp.bfloat16)
    d_query = (
        jnp.einsum(
            "schqk,sckhd->scqhd", d_scores, heads(key_rows), preferred_element_type=jnp.float32
        )
        * score_scale
    )
    d_key = (
        jnp.einsum(
            "schqk,scqhd->sckhd", d_scores, heads(query_rows), preferred_element_type=jnp.float32
        )
        * score_scale
    )
    d_query = d_query.reshape(n_seg, seg_rows, -1).astype(jnp.bfloat16)
    d_key = d_key.reshape(n_seg, seg_rows, -1).astype(jnp.bfloat16)
    d_proj = jnp.stack([d_query, d_key, d_value])
    grad_qkv = jnp.einsum(
        "strd,jsre->tjed", masked(input_segs, seg_hot), d_proj, preferred_element_type=jnp.float32
    )
    grad_qv = jnp.stack(
        [
            kind_sums(seg_hot, jnp.sum(d_query.astype(jnp.float32), axis=1)),
            kind_sums(seg_hot, jnp.sum(d_value.astype(jnp.float32), axis=1)),
        ],
        axis=1,
    )
    qkv_back = jnp.einsum("jsre,sjde->srd", d_proj, qkv_sel, preferred_element_type=jnp.float32)
    input_grad = scatter_sum(qkv_back) + d_one
    small = jnp.stack([rbias_grads, gain_grads, shift_grads])
    return (
        layer_out,
        input_grad,
        (grad_qkv, grad_qv, grad_out_w, grad_up, grad_ubias, grad_down),
        small,
    )


def local(
    inputs,
    cotangent,
    lengths,
    block_kind,
    w_qkv,
    qv_bias,
    w_out,
    resid_bias,
    norm_gain,
    norm_shift,
    w_up,
    up_bias,
    w_down,
):
    tok_dev = inputs.shape[0]
    n_tensor = lax.axis_size("tensor")
    rank = lax.axis_index("tensor")
    block_rows = BLOCK_SEQS * CHAIN
    assert block_rows % tok_dev == 0
    dev_chains = tok_dev // CHAIN
    chains = dev_chains // STREAMS
    seg_rows = chains * CHAIN
    weights = (w_qkv, qv_bias, w_out, resid_bias, norm_gain, norm_shift, w_up, up_bias, w_down)
    peer_kind = block_kind[(jnp.arange(n_tensor) * tok_dev) // block_rows]
    out_rows_w = lax.all_to_all(w_out[peer_kind], "tensor", 0, 0, tiled=True)
    outs, ins, grads, smalls = [], [], [], []
    for part in range(STREAMS):
        first_row = jnp.arange(n_tensor) * tok_dev + part * seg_rows
        seg_kind = block_kind[first_row // block_rows]
        chain_ids = (
            jnp.arange(n_tensor)[:, None] * dev_chains + part * chains + jnp.arange(chains)[None, :]
        )
        seg_lens = lengths[chain_ids]
        own_rows = rank * tok_dev + part * seg_rows + jnp.arange(seg_rows)
        row_kind = block_kind[own_rows // block_rows]
        rows = slice(part * seg_rows, (part + 1) * seg_rows)
        out_part, in_part, grad_part, small_part = stream(
            inputs[rows], cotangent[rows], seg_kind, seg_lens, row_kind, out_rows_w, *weights
        )
        outs.append(out_part)
        ins.append(in_part)
        grads.append(grad_part)
        smalls.append(small_part)
    layer_out = jnp.concatenate(outs, axis=0)
    input_grad = jnp.concatenate(ins, axis=0)
    grad_qkv, grad_qv, grad_out_w, grad_up, grad_ubias, grad_down = (
        sum(parts[1:], parts[0]) for parts in zip(*grads)
    )
    small = sum(smalls[1:], smalls[0])
    up_total, down_total = dp_sum_low((grad_up, grad_down))
    qkv_t_total, out_total = dp_sum_low((grad_qkv, grad_out_w))
    qkv_total = jnp.swapaxes(qkv_t_total, 2, 3)
    (small_grads,) = exact_sum((small,), "tensor")
    width = small.shape[-1]
    packed = jnp.concatenate(
        [small_grads.reshape(-1, width), grad_ubias.reshape(-1, width), grad_qv.reshape(-1, width)]
    )
    (packed,) = exact_sum((packed,), "dp")
    n_small, n_ubias = small_grads.size // width, grad_ubias.size // width
    small_total = packed[:n_small].reshape(small_grads.shape)
    ubias_total = packed[n_small : n_small + n_ubias].reshape(grad_ubias.shape)
    qv_total = packed[n_small + n_ubias :].reshape(grad_qv.shape)
    return (
        layer_out,
        input_grad,
        qkv_total,
        qv_total,
        out_total,
        small_total[0],
        small_total[1],
        small_total[2],
        up_total,
        ubias_total,
        down_total,
    )


def solution(mesh):
    return jax.shard_map(
        local,
        mesh=mesh,
        in_specs=(
            P(("dp", "tensor"), None),
            P(("dp", "tensor"), None),
            P("dp"),
            P("dp"),
            P(None, None, None, "tensor"),
            P(None, None, "tensor"),
            P(None, "tensor", None),
            P(),
            P(),
            P(),
            P(None, None, "tensor"),
            P(None, "tensor"),
            P(None, "tensor", None),
        ),
        out_specs=(
            P(("dp", "tensor"), None),
            P(("dp", "tensor"), None),
            P(None, None, None, "tensor"),
            P(None, None, "tensor"),
            P(None, "tensor", None),
            P(),
            P(),
            P(),
            P(None, None, "tensor"),
            P(None, "tensor"),
            P(None, "tensor", None),
        ),
        check_vma=False,
    )
```

```python
import jax
import jax.numpy as jnp
from jax import lax
from jax.sharding import PartitionSpec as P

HEAD_DIM = 64
CHAIN = 128
BLOCK_SEQS = 4
STREAMS = 2


EPSILON = 1e-05
SQRT_HALF = 0.7071067811865476
INV_ROOT_TWO_PI = 0.3989422804014327


def norm_forward(row_data, gain_rows, shift_rows):
    mean_row = jnp.mean(row_data, axis=-1, keepdims=True)
    centred = row_data - mean_row
    var_row = jnp.mean(centred * centred, axis=-1, keepdims=True)
    inv_std = lax.rsqrt(var_row + EPSILON)
    unit_rows = centred * inv_std
    return (unit_rows * gain_rows + shift_rows, unit_rows, inv_std)


def norm_backward(grad_rows, gain_rows, unit_rows, inv_std):
    scaled = grad_rows * gain_rows
    mean_first = jnp.mean(scaled, axis=-1, keepdims=True)
    mean_second = jnp.mean(scaled * unit_rows, axis=-1, keepdims=True)
    return inv_std * (scaled - mean_first - unit_rows * mean_second)


def type_sum(kind_hot, values):
    return jnp.einsum("rt,rd->td", kind_hot, values, precision=lax.Precision.HIGHEST)


def gelu_slope(values):
    return 0.5 * (1.0 + lax.erf(values * SQRT_HALF)) + values * INV_ROOT_TWO_PI * jnp.exp(
        -0.5 * values * values
    )


def gather_rows(local_rows):
    return lax.all_gather(local_rows, "tensor", axis=0, tiled=False)


def scatter_sum(seg_parts):
    n_seg, seg_rows, width = seg_parts.shape
    summed = lax.psum_scatter(
        seg_parts.reshape(n_seg * seg_rows, width).astype(jnp.bfloat16),
        "tensor",
        scatter_dimension=0,
        tiled=True,
    )
    return summed.astype(jnp.float32)


def masked(seg_rows, seg_hot):
    return seg_rows[:, None] * seg_hot[:, :, None, None].astype(seg_rows.dtype)


def kind_sums(seg_hot, seg_totals):
    return jnp.einsum(
        "st,se->te", seg_hot, seg_totals, precision=lax.Precision.HIGHEST
    )


def dp_perm(n, bit):
    return [(j, j ^ bit) for j in range(n)]


def dp_sum_low(parts):
    shapes = [p.shape for p in parts]
    n_dp = lax.axis_size("dp")
    idx = lax.axis_index("dp")
    steps = n_dp.bit_length() - 1
    cur = [p.reshape(-1, p.shape[-1]) for p in parts]
    assert 1 << steps == n_dp and all(c.shape[0] % n_dp == 0 for c in cur)
    for b in range(steps):
        upper = ((idx >> b) & 1) == 1
        halves = [(c[: c.shape[0] // 2], c[c.shape[0] // 2 :]) for c in cur]
        sends = tuple(jnp.where(upper, lo, hi).astype(jnp.bfloat16) for lo, hi in halves)
        gots = lax.ppermute(sends, "dp", dp_perm(n_dp, 1 << b))
        cur = [jnp.where(upper, hi, lo) + g.astype(jnp.float32) for (lo, hi), g in zip(halves, gots)]
    cur = [c.astype(jnp.bfloat16) for c in cur]
    for b in reversed(range(steps)):
        upper = ((idx >> b) & 1) == 1
        gots = lax.ppermute(tuple(cur), "dp", dp_perm(n_dp, 1 << b))
        cur = [
            jnp.where(upper, jnp.concatenate([g, c]), jnp.concatenate([c, g]))
            for c, g in zip(cur, gots)
        ]
    return [c.astype(jnp.float32).reshape(shape) for c, shape in zip(cur, shapes)]


def exact_sum(values, axis):
    n_ax = lax.axis_size(axis)
    steps = n_ax.bit_length() - 1
    assert 1 << steps == n_ax
    for b in range(steps):
        values = tuple(
            v + g for v, g in zip(values, lax.ppermute(values, axis, dp_perm(n_ax, 1 << b)))
        )
    return values


def stream(
    inputs,
    input_segs,
    after,
    cotangent,
    seg_kind,
    seg_lens,
    row_kind,
    out_rows_w,
    w_qkv,
    qv_bias,
    w_out,
    resid_bias,
    norm_gain,
    norm_shift,
    w_up,
    up_bias,
    w_down,
):
    n_seg, chains = seg_lens.shape
    seg_rows = chains * CHAIN
    heads_here = w_qkv.shape[3] // HEAD_DIM
    score_scale = HEAD_DIM ** (-0.5)
    highest = lax.Precision.HIGHEST
    seg_hot = (seg_kind[:, None] == jnp.arange(2)[None, :]).astype(jnp.float32)
    kind_hot = (row_kind[:, None] == jnp.arange(2)[None, :]).astype(jnp.float32)

    def pick(kind_table):
        return jnp.dot(kind_hot, kind_table.astype(jnp.float32), precision=highest)

    def heads(rows):
        return rows.reshape(n_seg, chains, CHAIN, heads_here, HEAD_DIM)

    key_valid = jnp.arange(CHAIN)[None, None, :] < seg_lens[:, :, None]

    qkv_sel = w_qkv[seg_kind]
    qvb_sel = qv_bias[seg_kind].astype(jnp.float32)
    out_sel = w_out[seg_kind]
    up_sel = w_up[seg_kind]
    ubias_sel = up_bias[seg_kind].astype(jnp.float32)
    down_sel = w_down[seg_kind]

    if after is not None:
        input_segs, _ = lax.optimization_barrier((input_segs, after["normed"]))
    projected = jnp.einsum(
        "srd,sjde->jsre", input_segs, qkv_sel, preferred_element_type=jnp.float32
    )
    query_rows = (projected[0] + qvb_sel[:, None, 0]).astype(jnp.bfloat16)
    key_rows = projected[1].astype(jnp.bfloat16)
    value_rows = (projected[2] + qvb_sel[:, None, 1]).astype(jnp.bfloat16)

    def probs_of():
        raw_scores = (
            jnp.einsum(
                "scqhd,sckhd->schqk",
                heads(query_rows),
                heads(key_rows),
                preferred_element_type=jnp.float32,
            )
            * score_scale
        )
        return jnp.where(key_valid[:, :, None, None, :], raw_scores, -1e30)

    scores = probs_of()
    row_max = jnp.max(scores, axis=-1, keepdims=True)
    log_total = row_max[..., 0] + jnp.log(jnp.sum(jnp.exp(scores - row_max), axis=-1))
    attn_probs = jnp.exp(scores - log_total[..., None])
    probs_low = attn_probs.astype(jnp.bfloat16)
    mixed = jnp.einsum(
        "schqk,sckhd->scqhd", probs_low, heads(value_rows), preferred_element_type=jnp.float32
    )
    mixed = mixed.reshape(n_seg, seg_rows, -1).astype(jnp.bfloat16)
    mixed_rows = lax.all_to_all(mixed, "tensor", 0, 0, tiled=True)
    attn_rows = jnp.einsum(
        "erc,ecd->rd", mixed_rows, out_rows_w, preferred_element_type=jnp.float32
    )

    hidden_one = inputs.astype(jnp.float32) + attn_rows + pick(resid_bias[:, 0])
    gain_one = pick(norm_gain[:, 0])
    normed, unit_one, inv_one = norm_forward(hidden_one, gain_one, pick(norm_shift[:, 0]))
    normed_low = normed.astype(jnp.bfloat16)
    norm_segs = gather_rows(normed_low)
    pre_act = (
        jnp.einsum("srd,sdf->srf", norm_segs, up_sel, preferred_element_type=jnp.float32)
        + ubias_sel[:, None]
    )
    activ = jax.nn.gelu(pre_act, approximate=False).astype(jnp.bfloat16)
    ffn_parts = jnp.einsum("srf,sfd->srd", activ, down_sel, preferred_element_type=jnp.float32)
    ffn_rows = scatter_sum(ffn_parts)

    hidden_two = normed + ffn_rows + pick(resid_bias[:, 1])
    gain_two = pick(norm_gain[:, 1])
    output_rows, unit_two, inv_two = norm_forward(hidden_two, gain_two, pick(norm_shift[:, 1]))
    layer_out = output_rows.astype(jnp.bfloat16)
    grad_out = cotangent.astype(jnp.float32)
    d_two = norm_backward(grad_out, gain_two, unit_two, inv_two)
    two_segs = gather_rows(d_two.astype(jnp.bfloat16))

    grad_down = jnp.einsum(
        "strf,srd->tfd", masked(activ, seg_hot), two_segs, preferred_element_type=jnp.float32
    )
    d_activ = jnp.einsum(
        "srd,sfd->srf", two_segs, down_sel, preferred_element_type=jnp.float32
    ).astype(jnp.bfloat16)
    d_pre = (d_activ.astype(jnp.float32) * gelu_slope(pre_act)).astype(jnp.bfloat16)
    grad_up = jnp.einsum(
        "strd,srf->tdf", masked(norm_segs, seg_hot), d_pre, preferred_element_type=jnp.float32
    )
    grad_ubias = kind_sums(seg_hot, jnp.sum(d_pre.astype(jnp.float32), axis=1))
    ffn_back = jnp.einsum("srf,sdf->srd", d_pre, up_sel, preferred_element_type=jnp.float32)
    d_normed = scatter_sum(ffn_back) + d_two

    d_one = norm_backward(d_normed, gain_one, unit_one, inv_one)
    gain_grads = jnp.stack(
        [type_sum(kind_hot, d_normed * unit_one), type_sum(kind_hot, grad_out * unit_two)], axis=1
    )
    shift_grads = jnp.stack([type_sum(kind_hot, d_normed), type_sum(kind_hot, grad_out)], axis=1)
    rbias_grads = jnp.stack([type_sum(kind_hot, d_one), type_sum(kind_hot, d_two)], axis=1)
    one_segs = gather_rows(d_one.astype(jnp.bfloat16))
    if after is not None:
        one_segs, _ = lax.optimization_barrier((one_segs, after["qkv_back"]))

    grad_out_w = jnp.einsum(
        "stre,srd->ted", masked(mixed, seg_hot), one_segs, preferred_element_type=jnp.float32
    )
    d_mixed = jnp.einsum(
        "srd,sed->sre", one_segs, out_sel, preferred_element_type=jnp.float32
    ).astype(jnp.bfloat16)
    d_mixed_heads = heads(d_mixed)
    d_value = jnp.einsum(
        "schqk,scqhd->sckhd", probs_low, d_mixed_heads, preferred_element_type=jnp.float32
    )
    d_value = d_value.reshape(n_seg, seg_rows, -1).astype(jnp.bfloat16)
    d_probs = jnp.einsum(
        "scqhd,sckhd->schqk", d_mixed_heads, heads(value_rows), preferred_element_type=jnp.float32
    )
    prob_dot = jnp.sum(attn_probs * d_probs, axis=-1, keepdims=True)
    d_scores = (attn_probs * (d_probs - prob_dot)).astype(jnp.bfloat16)
    d_query = (
        jnp.einsum(
            "schqk,sckhd->scqhd", d_scores, heads(key_rows), preferred_element_type=jnp.float32
        )
        * score_scale
    )
    d_key = (
        jnp.einsum(
            "schqk,scqhd->sckhd", d_scores, heads(query_rows), preferred_element_type=jnp.float32
        )
        * score_scale
    )
    d_query = d_query.reshape(n_seg, seg_rows, -1).astype(jnp.bfloat16)
    d_key = d_key.reshape(n_seg, seg_rows, -1).astype(jnp.bfloat16)
    d_proj = jnp.stack([d_query, d_key, d_value])
    grad_qkv = jnp.einsum(
        "strd,jsre->tjed", masked(input_segs, seg_hot), d_proj, preferred_element_type=jnp.float32
    )
    grad_qv = jnp.stack(
        [
            kind_sums(seg_hot, jnp.sum(d_query.astype(jnp.float32), axis=1)),
            kind_sums(seg_hot, jnp.sum(d_value.astype(jnp.float32), axis=1)),
        ],
        axis=1,
    )
    qkv_back = jnp.einsum("jsre,sjde->srd", d_proj, qkv_sel, preferred_element_type=jnp.float32)
    input_grad = scatter_sum(qkv_back) + d_one
    marks = {"normed": normed_low, "qkv_back": qkv_back}
    small = jnp.stack([rbias_grads, gain_grads, shift_grads])
    return (
        layer_out,
        input_grad,
        (grad_qkv, grad_qv, grad_out_w, grad_up, grad_ubias, grad_down),
        small,
        marks,
    )


def local(
    inputs,
    cotangent,
    lengths,
    block_kind,
    w_qkv,
    qv_bias,
    w_out,
    resid_bias,
    norm_gain,
    norm_shift,
    w_up,
    up_bias,
    w_down,
):
    tok_dev = inputs.shape[0]
    n_tensor = lax.axis_size("tensor")
    rank = lax.axis_index("tensor")
    block_rows = BLOCK_SEQS * CHAIN
    assert block_rows % tok_dev == 0
    dev_chains = tok_dev // CHAIN
    chains = dev_chains // STREAMS
    seg_rows = chains * CHAIN
    weights = (w_qkv, qv_bias, w_out, resid_bias, norm_gain, norm_shift, w_up, up_bias, w_down)
    peer_kind = block_kind[(jnp.arange(n_tensor) * tok_dev) // block_rows]
    row_parts = [slice(part * seg_rows, (part + 1) * seg_rows) for part in range(STREAMS)]
    gathered = [gather_rows(inputs[rows]) for rows in row_parts]
    out_sel, gathered[0] = lax.optimization_barrier((w_out[peer_kind], gathered[0]))
    out_rows_w = lax.all_to_all(out_sel, "tensor", 0, 0, tiled=True)
    marks = None
    outs, ins, grads, smalls = [], [], [], []
    for part in range(STREAMS):
        first_row = jnp.arange(n_tensor) * tok_dev + part * seg_rows
        seg_kind = block_kind[first_row // block_rows]
        chain_ids = (
            jnp.arange(n_tensor)[:, None] * dev_chains + part * chains + jnp.arange(chains)[None, :]
        )
        seg_lens = lengths[chain_ids]
        own_rows = rank * tok_dev + part * seg_rows + jnp.arange(seg_rows)
        row_kind = block_kind[own_rows // block_rows]
        rows = row_parts[part]
        out_part, in_part, grad_part, small_part, marks = stream(
            inputs[rows],
            gathered[part],
            marks,
            cotangent[rows],
            seg_kind,
            seg_lens,
            row_kind,
            out_rows_w,
            *weights,
        )
        outs.append(out_part)
        ins.append(in_part)
        grads.append(grad_part)
        smalls.append(small_part)
    layer_out = jnp.concatenate(outs, axis=0)
    input_grad = jnp.concatenate(ins, axis=0)
    grad_qkv, grad_qv, grad_out_w, grad_up, grad_ubias, grad_down = (
        sum(parts[1:], parts[0]) for parts in zip(*grads)
    )
    small = sum(smalls[1:], smalls[0])
    up_total, down_total = dp_sum_low((grad_up, grad_down))
    qkv_t_total, out_total = dp_sum_low((grad_qkv, grad_out_w))
    qkv_total = jnp.swapaxes(qkv_t_total, 2, 3)
    (small_grads,) = exact_sum((small,), "tensor")
    width = small.shape[-1]
    packed = jnp.concatenate(
        [small_grads.reshape(-1, width), grad_ubias.reshape(-1, width), grad_qv.reshape(-1, width)]
    )
    (packed,) = exact_sum((packed,), "dp")
    n_small, n_ubias = small_grads.size // width, grad_ubias.size // width
    small_total = packed[:n_small].reshape(small_grads.shape)
    ubias_total = packed[n_small : n_small + n_ubias].reshape(grad_ubias.shape)
    qv_total = packed[n_small + n_ubias :].reshape(grad_qv.shape)
    return (
        layer_out,
        input_grad,
        qkv_total,
        qv_total,
        out_total,
        small_total[0],
        small_total[1],
        small_total[2],
        up_total,
        ubias_total,
        down_total,
    )


def solution(mesh):
    return jax.shard_map(
        local,
        mesh=mesh,
        in_specs=(
            P(("dp", "tensor"), None),
            P(("dp", "tensor"), None),
            P("dp"),
            P("dp"),
            P(None, None, None, "tensor"),
            P(None, None, "tensor"),
            P(None, "tensor", None),
            P(),
            P(),
            P(),
            P(None, None, "tensor"),
            P(None, "tensor"),
            P(None, "tensor", None),
        ),
        out_specs=(
            P(("dp", "tensor"), None),
            P(("dp", "tensor"), None),
            P(None, None, None, "tensor"),
            P(None, None, "tensor"),
            P(None, "tensor", None),
            P(),
            P(),
            P(),
            P(None, None, "tensor"),
            P(None, "tensor"),
            P(None, "tensor", None),
        ),
        check_vma=False,
    )
```

```python
import jax
import jax.numpy as jnp
from jax import lax
from jax.sharding import PartitionSpec as P

HEAD_DIM = 64
CHAIN = 128
BLOCK_SEQS = 4
STREAMS = 2


EPSILON = 1e-05
SQRT_HALF = 0.7071067811865476
INV_ROOT_TWO_PI = 0.3989422804014327


def norm_forward(row_data, gain_rows, shift_rows):
    mean_row = jnp.mean(row_data, axis=-1, keepdims=True)
    centred = row_data - mean_row
    var_row = jnp.mean(centred * centred, axis=-1, keepdims=True)
    inv_std = lax.rsqrt(var_row + EPSILON)
    unit_rows = centred * inv_std
    return (unit_rows * gain_rows + shift_rows, unit_rows, inv_std)


def norm_backward(grad_rows, gain_rows, unit_rows, inv_std):
    scaled = grad_rows * gain_rows
    mean_first = jnp.mean(scaled, axis=-1, keepdims=True)
    mean_second = jnp.mean(scaled * unit_rows, axis=-1, keepdims=True)
    return inv_std * (scaled - mean_first - unit_rows * mean_second)


def type_sum(kind_hot, values):
    return jnp.einsum("rt,rd->td", kind_hot, values, precision=lax.Precision.HIGHEST)


def gelu_slope(values):
    return 0.5 * (1.0 + lax.erf(values * SQRT_HALF)) + values * INV_ROOT_TWO_PI * jnp.exp(
        -0.5 * values * values
    )


def gather_rows(local_rows):
    return lax.all_gather(local_rows, "tensor", axis=0, tiled=False)


def scatter_sum(seg_parts):
    n_seg, seg_rows, width = seg_parts.shape
    summed = lax.psum_scatter(
        seg_parts.reshape(n_seg * seg_rows, width).astype(jnp.bfloat16),
        "tensor",
        scatter_dimension=0,
        tiled=True,
    )
    return summed.astype(jnp.float32)


def masked(seg_rows, seg_hot):
    return seg_rows[:, None] * seg_hot[:, :, None, None].astype(seg_rows.dtype)


def kind_sums(seg_hot, seg_totals):
    return jnp.einsum(
        "st,se->te", seg_hot, seg_totals, precision=lax.Precision.HIGHEST
    )


def dp_perm(n, bit):
    return [(j, j ^ bit) for j in range(n)]


def dp_sum_low(parts):
    shapes = [p.shape for p in parts]
    n_dp = lax.axis_size("dp")
    idx = lax.axis_index("dp")
    steps = n_dp.bit_length() - 1
    cur = [p.reshape(-1, p.shape[-1]) for p in parts]
    assert 1 << steps == n_dp and all(c.shape[0] % n_dp == 0 for c in cur)
    for b in range(steps):
        upper = ((idx >> b) & 1) == 1
        halves = [(c[: c.shape[0] // 2], c[c.shape[0] // 2 :]) for c in cur]
        sends = tuple(jnp.where(upper, lo, hi).astype(jnp.bfloat16) for lo, hi in halves)
        gots = lax.ppermute(sends, "dp", dp_perm(n_dp, 1 << b))
        cur = [jnp.where(upper, hi, lo) + g.astype(jnp.float32) for (lo, hi), g in zip(halves, gots)]
    cur = [c.astype(jnp.bfloat16) for c in cur]
    for b in reversed(range(steps)):
        upper = ((idx >> b) & 1) == 1
        gots = lax.ppermute(tuple(cur), "dp", dp_perm(n_dp, 1 << b))
        cur = [
            jnp.where(upper, jnp.concatenate([g, c]), jnp.concatenate([c, g]))
            for c, g in zip(cur, gots)
        ]
    return [c.astype(jnp.float32).reshape(shape) for c, shape in zip(cur, shapes)]


def exact_sum(values, axis):
    n_ax = lax.axis_size(axis)
    steps = n_ax.bit_length() - 1
    assert 1 << steps == n_ax
    for b in range(steps):
        values = tuple(
            v + g for v, g in zip(values, lax.ppermute(values, axis, dp_perm(n_ax, 1 << b)))
        )
    return values


def stream(
    inputs,
    input_segs,
    after,
    cotangent,
    seg_kind,
    seg_lens,
    row_kind,
    out_rows_w,
    w_qkv,
    qv_bias,
    w_out,
    resid_bias,
    norm_gain,
    norm_shift,
    w_up,
    up_bias,
    w_down,
):
    n_seg, chains = seg_lens.shape
    seg_rows = chains * CHAIN
    heads_here = w_qkv.shape[3] // HEAD_DIM
    score_scale = HEAD_DIM ** (-0.5)
    highest = lax.Precision.HIGHEST
    seg_hot = (seg_kind[:, None] == jnp.arange(2)[None, :]).astype(jnp.float32)
    kind_hot = (row_kind[:, None] == jnp.arange(2)[None, :]).astype(jnp.float32)

    def pick(kind_table):
        return jnp.dot(kind_hot, kind_table.astype(jnp.float32), precision=highest)

    def heads(rows):
        return rows.reshape(n_seg, chains, CHAIN, heads_here, HEAD_DIM)

    key_valid = jnp.arange(CHAIN)[None, None, :] < seg_lens[:, :, None]

    qkv_sel = w_qkv[seg_kind]
    qvb_sel = qv_bias[seg_kind].astype(jnp.float32)
    out_sel = w_out[seg_kind]
    up_sel = w_up[seg_kind]
    ubias_sel = up_bias[seg_kind].astype(jnp.float32)
    down_sel = w_down[seg_kind]

    if after is not None:
        input_segs, _ = lax.optimization_barrier((input_segs, after["normed"]))
    projected = jnp.einsum(
        "srd,sjde->jsre", input_segs, qkv_sel, preferred_element_type=jnp.float32
    )
    query_rows = (projected[0] + qvb_sel[:, None, 0]).astype(jnp.bfloat16)
    key_rows = projected[1].astype(jnp.bfloat16)
    value_rows = (projected[2] + qvb_sel[:, None, 1]).astype(jnp.bfloat16)

    def probs_of():
        raw_scores = (
            jnp.einsum(
                "scqhd,sckhd->schqk",
                heads(query_rows),
                heads(key_rows),
                preferred_element_type=jnp.float32,
            )
            * score_scale
        )
        return jnp.where(key_valid[:, :, None, None, :], raw_scores, -1e30)

    scores = probs_of()
    row_max = jnp.max(scores, axis=-1, keepdims=True)
    log_total = row_max[..., 0] + jnp.log(jnp.sum(jnp.exp(scores - row_max), axis=-1))
    attn_probs = jnp.exp(scores - log_total[..., None])
    probs_low = attn_probs.astype(jnp.bfloat16)
    mixed = jnp.einsum(
        "schqk,sckhd->scqhd", probs_low, heads(value_rows), preferred_element_type=jnp.float32
    )
    mixed = mixed.reshape(n_seg, seg_rows, -1).astype(jnp.bfloat16)
    mixed_rows = lax.all_to_all(mixed, "tensor", 0, 0, tiled=True)
    attn_rows = jnp.einsum(
        "erc,ecd->rd", mixed_rows, out_rows_w, preferred_element_type=jnp.float32
    )

    hidden_one = inputs.astype(jnp.float32) + attn_rows + pick(resid_bias[:, 0])
    gain_one = pick(norm_gain[:, 0])
    normed, unit_one, inv_one = norm_forward(hidden_one, gain_one, pick(norm_shift[:, 0]))
    normed_low = normed.astype(jnp.bfloat16)
    norm_segs = gather_rows(normed_low)
    pre_act = (
        jnp.einsum("srd,sdf->srf", norm_segs, up_sel, preferred_element_type=jnp.float32)
        + ubias_sel[:, None]
    )
    activ = jax.nn.gelu(pre_act, approximate=False).astype(jnp.bfloat16)
    ffn_parts = jnp.einsum("srf,sfd->srd", activ, down_sel, preferred_element_type=jnp.float32)
    ffn_rows = scatter_sum(ffn_parts)

    hidden_two = normed + ffn_rows + pick(resid_bias[:, 1])
    gain_two = pick(norm_gain[:, 1])
    output_rows, unit_two, inv_two = norm_forward(hidden_two, gain_two, pick(norm_shift[:, 1]))
    layer_out = output_rows.astype(jnp.bfloat16)
    grad_out = cotangent.astype(jnp.float32)
    d_two = norm_backward(grad_out, gain_two, unit_two, inv_two)
    two_segs = gather_rows(d_two.astype(jnp.bfloat16))

    grad_down = jnp.einsum(
        "strf,srd->tfd", masked(activ, seg_hot), two_segs, preferred_element_type=jnp.float32
    )
    d_activ = jnp.einsum(
        "srd,sfd->srf", two_segs, down_sel, preferred_element_type=jnp.float32
    ).astype(jnp.bfloat16)
    d_pre = (d_activ.astype(jnp.float32) * gelu_slope(pre_act)).astype(jnp.bfloat16)
    grad_up = jnp.einsum(
        "strd,srf->tdf", masked(norm_segs, seg_hot), d_pre, preferred_element_type=jnp.float32
    )
    grad_ubias = kind_sums(seg_hot, jnp.sum(d_pre.astype(jnp.float32), axis=1))
    ffn_back = jnp.einsum("srf,sdf->srd", d_pre, up_sel, preferred_element_type=jnp.float32)
    d_normed = scatter_sum(ffn_back) + d_two

    d_one = norm_backward(d_normed, gain_one, unit_one, inv_one)
    gain_grads = jnp.stack(
        [type_sum(kind_hot, d_normed * unit_one), type_sum(kind_hot, grad_out * unit_two)], axis=1
    )
    shift_grads = jnp.stack([type_sum(kind_hot, d_normed), type_sum(kind_hot, grad_out)], axis=1)
    rbias_grads = jnp.stack([type_sum(kind_hot, d_one), type_sum(kind_hot, d_two)], axis=1)
    one_segs = gather_rows(d_one.astype(jnp.bfloat16))
    if after is not None:
        one_segs, _ = lax.optimization_barrier((one_segs, after["qkv_back"]))

    grad_out_w = jnp.einsum(
        "stre,srd->ted", masked(mixed, seg_hot), one_segs, preferred_element_type=jnp.float32
    )
    d_mixed = jnp.einsum(
        "srd,sed->sre", one_segs, out_sel, preferred_element_type=jnp.float32
    ).astype(jnp.bfloat16)
    d_mixed_heads = heads(d_mixed)
    d_value = jnp.einsum(
        "schqk,scqhd->sckhd", probs_low, d_mixed_heads, preferred_element_type=jnp.float32
    )
    d_value = d_value.reshape(n_seg, seg_rows, -1).astype(jnp.bfloat16)
    d_probs = jnp.einsum(
        "scqhd,sckhd->schqk", d_mixed_heads, heads(value_rows), preferred_element_type=jnp.float32
    )
    prob_dot = jnp.sum(attn_probs * d_probs, axis=-1, keepdims=True)
    d_scores = (attn_probs * (d_probs - prob_dot)).astype(jnp.bfloat16)
    d_query = (
        jnp.einsum(
            "schqk,sckhd->scqhd", d_scores, heads(key_rows), preferred_element_type=jnp.float32
        )
        * score_scale
    )
    d_key = (
        jnp.einsum(
            "schqk,scqhd->sckhd", d_scores, heads(query_rows), preferred_element_type=jnp.float32
        )
        * score_scale
    )
    d_query = d_query.reshape(n_seg, seg_rows, -1).astype(jnp.bfloat16)
    d_key = d_key.reshape(n_seg, seg_rows, -1).astype(jnp.bfloat16)
    d_proj = jnp.stack([d_query, d_key, d_value])
    grad_qkv = jnp.einsum(
        "strd,jsre->tjed", masked(input_segs, seg_hot), d_proj, preferred_element_type=jnp.float32
    )
    grad_qv = jnp.stack(
        [
            kind_sums(seg_hot, jnp.sum(d_query.astype(jnp.float32), axis=1)),
            kind_sums(seg_hot, jnp.sum(d_value.astype(jnp.float32), axis=1)),
        ],
        axis=1,
    )
    qkv_back = jnp.einsum("jsre,sjde->srd", d_proj, qkv_sel, preferred_element_type=jnp.float32)
    input_grad = scatter_sum(qkv_back) + d_one
    marks = {"normed": normed_low, "qkv_back": qkv_back}
    small = jnp.stack([rbias_grads, gain_grads, shift_grads])
    return (
        layer_out,
        input_grad,
        (grad_qkv, grad_qv, grad_out_w, grad_up, grad_ubias, grad_down),
        small,
        marks,
    )


def local(
    inputs,
    cotangent,
    lengths,
    block_kind,
    w_qkv,
    qv_bias,
    w_out,
    resid_bias,
    norm_gain,
    norm_shift,
    w_up,
    up_bias,
    w_down,
):
    tok_dev = inputs.shape[0]
    n_tensor = lax.axis_size("tensor")
    rank = lax.axis_index("tensor")
    block_rows = BLOCK_SEQS * CHAIN
    assert block_rows % tok_dev == 0
    dev_chains = tok_dev // CHAIN
    chains = dev_chains // STREAMS
    seg_rows = chains * CHAIN
    weights = (w_qkv, qv_bias, w_out, resid_bias, norm_gain, norm_shift, w_up, up_bias, w_down)
    peer_kind = block_kind[(jnp.arange(n_tensor) * tok_dev) // block_rows]
    row_parts = [slice(part * seg_rows, (part + 1) * seg_rows) for part in range(STREAMS)]
    gathered = [gather_rows(inputs[rows]) for rows in row_parts]
    out_rows_w = lax.all_to_all(w_out[peer_kind], "tensor", 0, 0, tiled=True)
    marks = None
    outs, ins, grads, smalls = [], [], [], []
    for part in range(STREAMS):
        first_row = jnp.arange(n_tensor) * tok_dev + part * seg_rows
        seg_kind = block_kind[first_row // block_rows]
        chain_ids = (
            jnp.arange(n_tensor)[:, None] * dev_chains + part * chains + jnp.arange(chains)[None, :]
        )
        seg_lens = lengths[chain_ids]
        own_rows = rank * tok_dev + part * seg_rows + jnp.arange(seg_rows)
        row_kind = block_kind[own_rows // block_rows]
        rows = row_parts[part]
        out_part, in_part, grad_part, small_part, marks = stream(
            inputs[rows],
            gathered[part],
            marks,
            cotangent[rows],
            seg_kind,
            seg_lens,
            row_kind,
            out_rows_w,
            *weights,
        )
        outs.append(out_part)
        ins.append(in_part)
        grads.append(grad_part)
        smalls.append(small_part)
    layer_out = jnp.concatenate(outs, axis=0)
    input_grad = jnp.concatenate(ins, axis=0)
    grad_qkv, grad_qv, grad_out_w, grad_up, grad_ubias, grad_down = (
        sum(parts[1:], parts[0]) for parts in zip(*grads)
    )
    small = sum(smalls[1:], smalls[0])
    up_total, down_total = dp_sum_low((grad_up, grad_down))
    qkv_t_total, out_total = dp_sum_low((grad_qkv, grad_out_w))
    qkv_total = jnp.swapaxes(qkv_t_total, 2, 3)
    (small_grads,) = exact_sum((small,), "tensor")
    width = small.shape[-1]
    packed = jnp.concatenate(
        [small_grads.reshape(-1, width), grad_ubias.reshape(-1, width), grad_qv.reshape(-1, width)]
    )
    (packed,) = exact_sum((packed,), "dp")
    n_small, n_ubias = small_grads.size // width, grad_ubias.size // width
    small_total = packed[:n_small].reshape(small_grads.shape)
    ubias_total = packed[n_small : n_small + n_ubias].reshape(grad_ubias.shape)
    qv_total = packed[n_small + n_ubias :].reshape(grad_qv.shape)
    return (
        layer_out,
        input_grad,
        qkv_total,
        qv_total,
        out_total,
        small_total[0],
        small_total[1],
        small_total[2],
        up_total,
        ubias_total,
        down_total,
    )


def solution(mesh):
    return jax.shard_map(
        local,
        mesh=mesh,
        in_specs=(
            P(("dp", "tensor"), None),
            P(("dp", "tensor"), None),
            P("dp"),
            P("dp"),
            P(None, None, None, "tensor"),
            P(None, None, "tensor"),
            P(None, "tensor", None),
            P(),
            P(),
            P(),
            P(None, None, "tensor"),
            P(None, "tensor"),
            P(None, "tensor", None),
        ),
        out_specs=(
            P(("dp", "tensor"), None),
            P(("dp", "tensor"), None),
            P(None, None, None, "tensor"),
            P(None, None, "tensor"),
            P(None, "tensor", None),
            P(),
            P(),
            P(),
            P(None, None, "tensor"),
            P(None, "tensor"),
            P(None, "tensor", None),
        ),
        check_vma=False,
    )
```

```python
import jax
import jax.numpy as jnp
from jax import lax
from jax.sharding import PartitionSpec as P

HEAD_DIM = 64
CHAIN = 128
BLOCK_SEQS = 4
STREAMS = 2


EPSILON = 1e-05
SQRT_HALF = 0.7071067811865476
INV_ROOT_TWO_PI = 0.3989422804014327


def norm_forward(row_data, gain_rows, shift_rows):
    mean_row = jnp.mean(row_data, axis=-1, keepdims=True)
    centred = row_data - mean_row
    var_row = jnp.mean(centred * centred, axis=-1, keepdims=True)
    inv_std = lax.rsqrt(var_row + EPSILON)
    unit_rows = centred * inv_std
    return (unit_rows * gain_rows + shift_rows, unit_rows, inv_std)


def norm_backward(grad_rows, gain_rows, unit_rows, inv_std):
    scaled = grad_rows * gain_rows
    mean_first = jnp.mean(scaled, axis=-1, keepdims=True)
    mean_second = jnp.mean(scaled * unit_rows, axis=-1, keepdims=True)
    return inv_std * (scaled - mean_first - unit_rows * mean_second)


def type_sum(kind_hot, values):
    return jnp.einsum("rt,rd->td", kind_hot, values, precision=lax.Precision.HIGHEST)


def gelu_slope(values):
    return 0.5 * (1.0 + lax.erf(values * SQRT_HALF)) + values * INV_ROOT_TWO_PI * jnp.exp(
        -0.5 * values * values
    )


def gather_rows(local_rows):
    return lax.all_gather(local_rows, "tensor", axis=0, tiled=False)


def scatter_sum(seg_parts):
    n_seg, seg_rows, width = seg_parts.shape
    summed = lax.psum_scatter(
        seg_parts.reshape(n_seg * seg_rows, width).astype(jnp.bfloat16),
        "tensor",
        scatter_dimension=0,
        tiled=True,
    )
    return summed.astype(jnp.float32)


def masked(seg_rows, seg_hot):
    return seg_rows[:, None] * seg_hot[:, :, None, None].astype(seg_rows.dtype)


def kind_sums(seg_hot, seg_totals):
    return jnp.einsum(
        "st,se->te", seg_hot, seg_totals, precision=lax.Precision.HIGHEST
    )


def dp_perm(n, bit):
    return [(j, j ^ bit) for j in range(n)]


def dp_sum_low(parts):
    shapes = [p.shape for p in parts]
    n_dp = lax.axis_size("dp")
    idx = lax.axis_index("dp")
    steps = n_dp.bit_length() - 1
    cur = [p.reshape(-1, p.shape[-1]) for p in parts]
    assert 1 << steps == n_dp and all(c.shape[0] % n_dp == 0 for c in cur)
    for b in range(steps):
        upper = ((idx >> b) & 1) == 1
        halves = [(c[: c.shape[0] // 2], c[c.shape[0] // 2 :]) for c in cur]
        sends = tuple(jnp.where(upper, lo, hi).astype(jnp.bfloat16) for lo, hi in halves)
        gots = lax.ppermute(sends, "dp", dp_perm(n_dp, 1 << b))
        cur = [jnp.where(upper, hi, lo) + g.astype(jnp.float32) for (lo, hi), g in zip(halves, gots)]
    cur = [c.astype(jnp.bfloat16) for c in cur]
    for b in reversed(range(steps)):
        upper = ((idx >> b) & 1) == 1
        gots = lax.ppermute(tuple(cur), "dp", dp_perm(n_dp, 1 << b))
        cur = [
            jnp.where(upper, jnp.concatenate([g, c]), jnp.concatenate([c, g]))
            for c, g in zip(cur, gots)
        ]
    return [c.astype(jnp.float32).reshape(shape) for c, shape in zip(cur, shapes)]


def exact_sum(values, axis):
    n_ax = lax.axis_size(axis)
    steps = n_ax.bit_length() - 1
    assert 1 << steps == n_ax
    for b in range(steps):
        values = tuple(
            v + g for v, g in zip(values, lax.ppermute(values, axis, dp_perm(n_ax, 1 << b)))
        )
    return values


def stream(
    inputs,
    input_segs,
    after,
    cotangent,
    seg_kind,
    seg_lens,
    row_kind,
    out_rows_w,
    w_qkv,
    qv_bias,
    w_out,
    resid_bias,
    norm_gain,
    norm_shift,
    w_up,
    up_bias,
    w_down,
):
    n_seg, chains = seg_lens.shape
    seg_rows = chains * CHAIN
    heads_here = w_qkv.shape[3] // HEAD_DIM
    score_scale = HEAD_DIM ** (-0.5)
    highest = lax.Precision.HIGHEST
    seg_hot = (seg_kind[:, None] == jnp.arange(2)[None, :]).astype(jnp.float32)
    kind_hot = (row_kind[:, None] == jnp.arange(2)[None, :]).astype(jnp.float32)

    def pick(kind_table):
        return jnp.dot(kind_hot, kind_table.astype(jnp.float32), precision=highest)

    def heads(rows):
        return rows.reshape(n_seg, chains, CHAIN, heads_here, HEAD_DIM)

    key_valid = jnp.arange(CHAIN)[None, None, :] < seg_lens[:, :, None]

    qkv_sel = w_qkv[seg_kind]
    qvb_sel = qv_bias[seg_kind].astype(jnp.float32)
    out_sel = w_out[seg_kind]
    up_sel = w_up[seg_kind]
    ubias_sel = up_bias[seg_kind].astype(jnp.float32)
    down_sel = w_down[seg_kind]

    projected = jnp.einsum(
        "srd,sjde->jsre", input_segs, qkv_sel, preferred_element_type=jnp.float32
    )
    query_rows = (projected[0] + qvb_sel[:, None, 0]).astype(jnp.bfloat16)
    key_rows = projected[1].astype(jnp.bfloat16)
    value_rows = (projected[2] + qvb_sel[:, None, 1]).astype(jnp.bfloat16)

    def probs_of():
        raw_scores = (
            jnp.einsum(
                "scqhd,sckhd->schqk",
                heads(query_rows),
                heads(key_rows),
                preferred_element_type=jnp.float32,
            )
            * score_scale
        )
        return jnp.where(key_valid[:, :, None, None, :], raw_scores, -1e30)

    scores = probs_of()
    row_max = jnp.max(scores, axis=-1, keepdims=True)
    log_total = row_max[..., 0] + jnp.log(jnp.sum(jnp.exp(scores - row_max), axis=-1))
    attn_probs = jnp.exp(scores - log_total[..., None])
    probs_low = attn_probs.astype(jnp.bfloat16)
    mixed = jnp.einsum(
        "schqk,sckhd->scqhd", probs_low, heads(value_rows), preferred_element_type=jnp.float32
    )
    mixed = mixed.reshape(n_seg, seg_rows, -1).astype(jnp.bfloat16)
    mixed_rows = lax.all_to_all(mixed, "tensor", 0, 0, tiled=True)
    attn_rows = jnp.einsum(
        "erc,ecd->rd", mixed_rows, out_rows_w, preferred_element_type=jnp.float32
    )

    hidden_one = inputs.astype(jnp.float32) + attn_rows + pick(resid_bias[:, 0])
    gain_one = pick(norm_gain[:, 0])
    normed, unit_one, inv_one = norm_forward(hidden_one, gain_one, pick(norm_shift[:, 0]))
    normed_low = normed.astype(jnp.bfloat16)
    norm_segs = gather_rows(normed_low)
    pre_act = (
        jnp.einsum("srd,sdf->srf", norm_segs, up_sel, preferred_element_type=jnp.float32)
        + ubias_sel[:, None]
    )
    activ = jax.nn.gelu(pre_act, approximate=False).astype(jnp.bfloat16)
    ffn_parts = jnp.einsum("srf,sfd->srd", activ, down_sel, preferred_element_type=jnp.float32)
    ffn_rows = scatter_sum(ffn_parts)

    hidden_two = normed + ffn_rows + pick(resid_bias[:, 1])
    gain_two = pick(norm_gain[:, 1])
    output_rows, unit_two, inv_two = norm_forward(hidden_two, gain_two, pick(norm_shift[:, 1]))
    layer_out = output_rows.astype(jnp.bfloat16)
    grad_out = cotangent.astype(jnp.float32)
    d_two = norm_backward(grad_out, gain_two, unit_two, inv_two)
    two_segs = gather_rows(d_two.astype(jnp.bfloat16))

    grad_down = jnp.einsum(
        "strf,srd->tfd", masked(activ, seg_hot), two_segs, preferred_element_type=jnp.float32
    )
    d_activ = jnp.einsum(
        "srd,sfd->srf", two_segs, down_sel, preferred_element_type=jnp.float32
    ).astype(jnp.bfloat16)
    d_pre = (d_activ.astype(jnp.float32) * gelu_slope(pre_act)).astype(jnp.bfloat16)
    grad_up = jnp.einsum(
        "strd,srf->tdf", masked(norm_segs, seg_hot), d_pre, preferred_element_type=jnp.float32
    )
    grad_ubias = kind_sums(seg_hot, jnp.sum(d_pre.astype(jnp.float32), axis=1))
    ffn_back = jnp.einsum("srf,sdf->srd", d_pre, up_sel, preferred_element_type=jnp.float32)
    d_normed = scatter_sum(ffn_back) + d_two

    d_one = norm_backward(d_normed, gain_one, unit_one, inv_one)
    gain_grads = jnp.stack(
        [type_sum(kind_hot, d_normed * unit_one), type_sum(kind_hot, grad_out * unit_two)], axis=1
    )
    shift_grads = jnp.stack([type_sum(kind_hot, d_normed), type_sum(kind_hot, grad_out)], axis=1)
    rbias_grads = jnp.stack([type_sum(kind_hot, d_one), type_sum(kind_hot, d_two)], axis=1)
    one_segs = gather_rows(d_one.astype(jnp.bfloat16))
    if after is not None:
        one_segs, _ = lax.optimization_barrier((one_segs, after["qkv_back"]))

    grad_out_w = jnp.einsum(
        "stre,srd->ted", masked(mixed, seg_hot), one_segs, preferred_element_type=jnp.float32
    )
    d_mixed = jnp.einsum(
        "srd,sed->sre", one_segs, out_sel, preferred_element_type=jnp.float32
    ).astype(jnp.bfloat16)
    d_mixed_heads = heads(d_mixed)
    d_value = jnp.einsum(
        "schqk,scqhd->sckhd", probs_low, d_mixed_heads, preferred_element_type=jnp.float32
    )
    d_value = d_value.reshape(n_seg, seg_rows, -1).astype(jnp.bfloat16)
    d_probs = jnp.einsum(
        "scqhd,sckhd->schqk", d_mixed_heads, heads(value_rows), preferred_element_type=jnp.float32
    )
    prob_dot = jnp.sum(attn_probs * d_probs, axis=-1, keepdims=True)
    d_scores = (attn_probs * (d_probs - prob_dot)).astype(jnp.bfloat16)
    d_query = (
        jnp.einsum(
            "schqk,sckhd->scqhd", d_scores, heads(key_rows), preferred_element_type=jnp.float32
        )
        * score_scale
    )
    d_key = (
        jnp.einsum(
            "schqk,scqhd->sckhd", d_scores, heads(query_rows), preferred_element_type=jnp.float32
        )
        * score_scale
    )
    d_query = d_query.reshape(n_seg, seg_rows, -1).astype(jnp.bfloat16)
    d_key = d_key.reshape(n_seg, seg_rows, -1).astype(jnp.bfloat16)
    d_proj = jnp.stack([d_query, d_key, d_value])
    grad_qkv = jnp.einsum(
        "strd,jsre->tjed", masked(input_segs, seg_hot), d_proj, preferred_element_type=jnp.float32
    )
    grad_qv = jnp.stack(
        [
            kind_sums(seg_hot, jnp.sum(d_query.astype(jnp.float32), axis=1)),
            kind_sums(seg_hot, jnp.sum(d_value.astype(jnp.float32), axis=1)),
        ],
        axis=1,
    )
    qkv_back = jnp.einsum("jsre,sjde->srd", d_proj, qkv_sel, preferred_element_type=jnp.float32)
    input_grad = scatter_sum(qkv_back) + d_one
    marks = {"qkv_back": qkv_back}
    small = jnp.stack([rbias_grads, gain_grads, shift_grads])
    return (
        layer_out,
        input_grad,
        (grad_qkv, grad_qv, grad_out_w, grad_up, grad_ubias, grad_down),
        small,
        marks,
    )


def local(
    inputs,
    cotangent,
    lengths,
    block_kind,
    w_qkv,
    qv_bias,
    w_out,
    resid_bias,
    norm_gain,
    norm_shift,
    w_up,
    up_bias,
    w_down,
):
    tok_dev = inputs.shape[0]
    n_tensor = lax.axis_size("tensor")
    rank = lax.axis_index("tensor")
    block_rows = BLOCK_SEQS * CHAIN
    assert block_rows % tok_dev == 0
    dev_chains = tok_dev // CHAIN
    chains = dev_chains // STREAMS
    seg_rows = chains * CHAIN
    weights = (w_qkv, qv_bias, w_out, resid_bias, norm_gain, norm_shift, w_up, up_bias, w_down)
    peer_kind = block_kind[(jnp.arange(n_tensor) * tok_dev) // block_rows]
    row_parts = [slice(part * seg_rows, (part + 1) * seg_rows) for part in range(STREAMS)]
    gathered = [gather_rows(inputs[rows]) for rows in row_parts]
    out_rows_w = lax.all_to_all(w_out[peer_kind], "tensor", 0, 0, tiled=True)
    marks = None
    outs, ins, grads, smalls = [], [], [], []
    for part in range(STREAMS):
        first_row = jnp.arange(n_tensor) * tok_dev + part * seg_rows
        seg_kind = block_kind[first_row // block_rows]
        chain_ids = (
            jnp.arange(n_tensor)[:, None] * dev_chains + part * chains + jnp.arange(chains)[None, :]
        )
        seg_lens = lengths[chain_ids]
        own_rows = rank * tok_dev + part * seg_rows + jnp.arange(seg_rows)
        row_kind = block_kind[own_rows // block_rows]
        rows = row_parts[part]
        out_part, in_part, grad_part, small_part, marks = stream(
            inputs[rows],
            gathered[part],
            marks,
            cotangent[rows],
            seg_kind,
            seg_lens,
            row_kind,
            out_rows_w,
            *weights,
        )
        outs.append(out_part)
        ins.append(in_part)
        grads.append(grad_part)
        smalls.append(small_part)
    layer_out = jnp.concatenate(outs, axis=0)
    input_grad = jnp.concatenate(ins, axis=0)
    grad_qkv, grad_qv, grad_out_w, grad_up, grad_ubias, grad_down = (
        sum(parts[1:], parts[0]) for parts in zip(*grads)
    )
    small = sum(smalls[1:], smalls[0])
    up_total, down_total = dp_sum_low((grad_up, grad_down))
    qkv_t_total, out_total = dp_sum_low((grad_qkv, grad_out_w))
    qkv_total = jnp.swapaxes(qkv_t_total, 2, 3)
    (small_grads,) = exact_sum((small,), "tensor")
    width = small.shape[-1]
    packed = jnp.concatenate(
        [small_grads.reshape(-1, width), grad_ubias.reshape(-1, width), grad_qv.reshape(-1, width)]
    )
    (packed,) = exact_sum((packed,), "dp")
    n_small, n_ubias = small_grads.size // width, grad_ubias.size // width
    small_total = packed[:n_small].reshape(small_grads.shape)
    ubias_total = packed[n_small : n_small + n_ubias].reshape(grad_ubias.shape)
    qv_total = packed[n_small + n_ubias :].reshape(grad_qv.shape)
    return (
        layer_out,
        input_grad,
        qkv_total,
        qv_total,
        out_total,
        small_total[0],
        small_total[1],
        small_total[2],
        up_total,
        ubias_total,
        down_total,
    )


def solution(mesh):
    return jax.shard_map(
        local,
        mesh=mesh,
        in_specs=(
            P(("dp", "tensor"), None),
            P(("dp", "tensor"), None),
            P("dp"),
            P("dp"),
            P(None, None, None, "tensor"),
            P(None, None, "tensor"),
            P(None, "tensor", None),
            P(),
            P(),
            P(),
            P(None, None, "tensor"),
            P(None, "tensor"),
            P(None, "tensor", None),
        ),
        out_specs=(
            P(("dp", "tensor"), None),
            P(("dp", "tensor"), None),
            P(None, None, None, "tensor"),
            P(None, None, "tensor"),
            P(None, "tensor", None),
            P(),
            P(),
            P(),
            P(None, None, "tensor"),
            P(None, "tensor"),
            P(None, "tensor", None),
        ),
        check_vma=False,
    )
```

```python
import jax
import jax.numpy as jnp
from jax import lax
from jax.sharding import PartitionSpec as P

HEAD_DIM = 64
CHAIN = 128
BLOCK_SEQS = 4
STREAMS = 2


EPSILON = 1e-05
SQRT_HALF = 0.7071067811865476
INV_ROOT_TWO_PI = 0.3989422804014327


def norm_forward(row_data, gain_rows, shift_rows):
    mean_row = jnp.mean(row_data, axis=-1, keepdims=True)
    centred = row_data - mean_row
    var_row = jnp.mean(centred * centred, axis=-1, keepdims=True)
    inv_std = lax.rsqrt(var_row + EPSILON)
    unit_rows = centred * inv_std
    return (unit_rows * gain_rows + shift_rows, unit_rows, inv_std)


def norm_backward(grad_rows, gain_rows, unit_rows, inv_std):
    scaled = grad_rows * gain_rows
    mean_first = jnp.mean(scaled, axis=-1, keepdims=True)
    mean_second = jnp.mean(scaled * unit_rows, axis=-1, keepdims=True)
    return inv_std * (scaled - mean_first - unit_rows * mean_second)


def type_sum(kind_hot, values):
    return jnp.einsum("rt,rd->td", kind_hot, values, precision=lax.Precision.HIGHEST)


def gelu_slope(values):
    return 0.5 * (1.0 + lax.erf(values * SQRT_HALF)) + values * INV_ROOT_TWO_PI * jnp.exp(
        -0.5 * values * values
    )


def gather_rows(local_rows):
    return lax.all_gather(local_rows, "tensor", axis=0, tiled=False)


def scatter_sum(seg_parts):
    n_seg, seg_rows, width = seg_parts.shape
    summed = lax.psum_scatter(
        seg_parts.reshape(n_seg * seg_rows, width).astype(jnp.bfloat16),
        "tensor",
        scatter_dimension=0,
        tiled=True,
    )
    return summed.astype(jnp.float32)


def masked(seg_rows, seg_hot):
    return seg_rows[:, None] * seg_hot[:, :, None, None].astype(seg_rows.dtype)


def kind_sums(seg_hot, seg_totals):
    return jnp.einsum(
        "st,se->te", seg_hot, seg_totals, precision=lax.Precision.HIGHEST
    )


def dp_perm(n, bit):
    return [(j, j ^ bit) for j in range(n)]


def dp_sum_low(parts):
    shapes = [p.shape for p in parts]
    n_dp = lax.axis_size("dp")
    idx = lax.axis_index("dp")
    steps = n_dp.bit_length() - 1
    cur = [p.reshape(-1, p.shape[-1]) for p in parts]
    assert 1 << steps == n_dp and all(c.shape[0] % n_dp == 0 for c in cur)
    for b in range(steps):
        upper = ((idx >> b) & 1) == 1
        halves = [(c[: c.shape[0] // 2], c[c.shape[0] // 2 :]) for c in cur]
        sends = tuple(jnp.where(upper, lo, hi).astype(jnp.bfloat16) for lo, hi in halves)
        gots = lax.ppermute(sends, "dp", dp_perm(n_dp, 1 << b))
        cur = [jnp.where(upper, hi, lo) + g.astype(jnp.float32) for (lo, hi), g in zip(halves, gots)]
    cur = [c.astype(jnp.bfloat16) for c in cur]
    for b in reversed(range(steps)):
        upper = ((idx >> b) & 1) == 1
        gots = lax.ppermute(tuple(cur), "dp", dp_perm(n_dp, 1 << b))
        cur = [
            jnp.where(upper, jnp.concatenate([g, c]), jnp.concatenate([c, g]))
            for c, g in zip(cur, gots)
        ]
    return [c.astype(jnp.float32).reshape(shape) for c, shape in zip(cur, shapes)]


def exact_sum(values, axis):
    n_ax = lax.axis_size(axis)
    steps = n_ax.bit_length() - 1
    assert 1 << steps == n_ax
    for b in range(steps):
        values = tuple(
            v + g for v, g in zip(values, lax.ppermute(values, axis, dp_perm(n_ax, 1 << b)))
        )
    return values


def stream(
    inputs,
    input_segs,
    cotangent,
    seg_kind,
    seg_lens,
    row_kind,
    out_rows_w,
    w_qkv,
    qv_bias,
    w_out,
    resid_bias,
    norm_gain,
    norm_shift,
    w_up,
    up_bias,
    w_down,
):
    n_seg, chains = seg_lens.shape
    seg_rows = chains * CHAIN
    heads_here = w_qkv.shape[3] // HEAD_DIM
    score_scale = HEAD_DIM ** (-0.5)
    highest = lax.Precision.HIGHEST
    seg_hot = (seg_kind[:, None] == jnp.arange(2)[None, :]).astype(jnp.float32)
    kind_hot = (row_kind[:, None] == jnp.arange(2)[None, :]).astype(jnp.float32)

    def pick(kind_table):
        return jnp.dot(kind_hot, kind_table.astype(jnp.float32), precision=highest)

    def heads(rows):
        return rows.reshape(n_seg, chains, CHAIN, heads_here, HEAD_DIM)

    key_valid = jnp.arange(CHAIN)[None, None, :] < seg_lens[:, :, None]

    qkv_sel = w_qkv[seg_kind]
    qvb_sel = qv_bias[seg_kind].astype(jnp.float32)
    out_sel = w_out[seg_kind]
    up_sel = w_up[seg_kind]
    ubias_sel = up_bias[seg_kind].astype(jnp.float32)
    down_sel = w_down[seg_kind]

    projected = jnp.einsum(
        "srd,sjde->jsre", input_segs, qkv_sel, preferred_element_type=jnp.float32
    )
    query_rows = (projected[0] + qvb_sel[:, None, 0]).astype(jnp.bfloat16)
    key_rows = projected[1].astype(jnp.bfloat16)
    value_rows = (projected[2] + qvb_sel[:, None, 1]).astype(jnp.bfloat16)

    def probs_of():
        raw_scores = (
            jnp.einsum(
                "scqhd,sckhd->schqk",
                heads(query_rows),
                heads(key_rows),
                preferred_element_type=jnp.float32,
            )
            * score_scale
        )
        return jnp.where(key_valid[:, :, None, None, :], raw_scores, -1e30)

    scores = probs_of()
    row_max = jnp.max(scores, axis=-1, keepdims=True)
    log_total = row_max[..., 0] + jnp.log(jnp.sum(jnp.exp(scores - row_max), axis=-1))
    attn_probs = jnp.exp(scores - log_total[..., None])
    probs_low = attn_probs.astype(jnp.bfloat16)
    mixed = jnp.einsum(
        "schqk,sckhd->scqhd", probs_low, heads(value_rows), preferred_element_type=jnp.float32
    )
    mixed = mixed.reshape(n_seg, seg_rows, -1).astype(jnp.bfloat16)
    mixed_rows = lax.all_to_all(mixed, "tensor", 0, 0, tiled=True)
    attn_rows = jnp.einsum(
        "erc,ecd->rd", mixed_rows, out_rows_w, preferred_element_type=jnp.float32
    )

    hidden_one = inputs.astype(jnp.float32) + attn_rows + pick(resid_bias[:, 0])
    gain_one = pick(norm_gain[:, 0])
    normed, unit_one, inv_one = norm_forward(hidden_one, gain_one, pick(norm_shift[:, 0]))
    normed_low = normed.astype(jnp.bfloat16)
    norm_segs = gather_rows(normed_low)
    pre_act = (
        jnp.einsum("srd,sdf->srf", norm_segs, up_sel, preferred_element_type=jnp.float32)
        + ubias_sel[:, None]
    )
    activ = jax.nn.gelu(pre_act, approximate=False).astype(jnp.bfloat16)
    ffn_parts = jnp.einsum("srf,sfd->srd", activ, down_sel, preferred_element_type=jnp.float32)
    ffn_rows = scatter_sum(ffn_parts)

    hidden_two = normed + ffn_rows + pick(resid_bias[:, 1])
    gain_two = pick(norm_gain[:, 1])
    output_rows, unit_two, inv_two = norm_forward(hidden_two, gain_two, pick(norm_shift[:, 1]))
    layer_out = output_rows.astype(jnp.bfloat16)
    grad_out = cotangent.astype(jnp.float32)
    d_two = norm_backward(grad_out, gain_two, unit_two, inv_two)
    two_segs = gather_rows(d_two.astype(jnp.bfloat16))

    grad_down = jnp.einsum(
        "strf,srd->tfd", masked(activ, seg_hot), two_segs, preferred_element_type=jnp.float32
    )
    d_activ = jnp.einsum(
        "srd,sfd->srf", two_segs, down_sel, preferred_element_type=jnp.float32
    ).astype(jnp.bfloat16)
    d_pre = (d_activ.astype(jnp.float32) * gelu_slope(pre_act)).astype(jnp.bfloat16)
    grad_up = jnp.einsum(
        "strd,srf->tdf", masked(norm_segs, seg_hot), d_pre, preferred_element_type=jnp.float32
    )
    grad_ubias = kind_sums(seg_hot, jnp.sum(d_pre.astype(jnp.float32), axis=1))
    ffn_back = jnp.einsum("srf,sdf->srd", d_pre, up_sel, preferred_element_type=jnp.float32)
    d_normed = scatter_sum(ffn_back) + d_two

    d_one = norm_backward(d_normed, gain_one, unit_one, inv_one)
    gain_grads = jnp.stack(
        [type_sum(kind_hot, d_normed * unit_one), type_sum(kind_hot, grad_out * unit_two)], axis=1
    )
    shift_grads = jnp.stack([type_sum(kind_hot, d_normed), type_sum(kind_hot, grad_out)], axis=1)
    rbias_grads = jnp.stack([type_sum(kind_hot, d_one), type_sum(kind_hot, d_two)], axis=1)
    one_segs = gather_rows(d_one.astype(jnp.bfloat16))

    grad_out_w = jnp.einsum(
        "stre,srd->ted", masked(mixed, seg_hot), one_segs, preferred_element_type=jnp.float32
    )
    d_mixed = jnp.einsum(
        "srd,sed->sre", one_segs, out_sel, preferred_element_type=jnp.float32
    ).astype(jnp.bfloat16)
    d_mixed_heads = heads(d_mixed)
    d_value = jnp.einsum(
        "schqk,scqhd->sckhd", probs_low, d_mixed_heads, preferred_element_type=jnp.float32
    )
    d_value = d_value.reshape(n_seg, seg_rows, -1).astype(jnp.bfloat16)
    d_probs = jnp.einsum(
        "scqhd,sckhd->schqk", d_mixed_heads, heads(value_rows), preferred_element_type=jnp.float32
    )
    prob_dot = jnp.sum(attn_probs * d_probs, axis=-1, keepdims=True)
    d_scores = (attn_probs * (d_probs - prob_dot)).astype(jnp.bfloat16)
    d_query = (
        jnp.einsum(
            "schqk,sckhd->scqhd", d_scores, heads(key_rows), preferred_element_type=jnp.float32
        )
        * score_scale
    )
    d_key = (
        jnp.einsum(
            "schqk,scqhd->sckhd", d_scores, heads(query_rows), preferred_element_type=jnp.float32
        )
        * score_scale
    )
    d_query = d_query.reshape(n_seg, seg_rows, -1).astype(jnp.bfloat16)
    d_key = d_key.reshape(n_seg, seg_rows, -1).astype(jnp.bfloat16)
    d_proj = jnp.stack([d_query, d_key, d_value])
    grad_qkv = jnp.einsum(
        "strd,jsre->tjed", masked(input_segs, seg_hot), d_proj, preferred_element_type=jnp.float32
    )
    grad_qv = jnp.stack(
        [
            kind_sums(seg_hot, jnp.sum(d_query.astype(jnp.float32), axis=1)),
            kind_sums(seg_hot, jnp.sum(d_value.astype(jnp.float32), axis=1)),
        ],
        axis=1,
    )
    qkv_back = jnp.einsum("jsre,sjde->srd", d_proj, qkv_sel, preferred_element_type=jnp.float32)
    input_grad = scatter_sum(qkv_back) + d_one
    small = jnp.stack([rbias_grads, gain_grads, shift_grads])
    return (
        layer_out,
        input_grad,
        (grad_qkv, grad_qv, grad_out_w, grad_up, grad_ubias, grad_down),
        small,
    )


def local(
    inputs,
    cotangent,
    lengths,
    block_kind,
    w_qkv,
    qv_bias,
    w_out,
    resid_bias,
    norm_gain,
    norm_shift,
    w_up,
    up_bias,
    w_down,
):
    tok_dev = inputs.shape[0]
    n_tensor = lax.axis_size("tensor")
    rank = lax.axis_index("tensor")
    block_rows = BLOCK_SEQS * CHAIN
    assert block_rows % tok_dev == 0
    dev_chains = tok_dev // CHAIN
    chains = dev_chains // STREAMS
    seg_rows = chains * CHAIN
    weights = (w_qkv, qv_bias, w_out, resid_bias, norm_gain, norm_shift, w_up, up_bias, w_down)
    peer_kind = block_kind[(jnp.arange(n_tensor) * tok_dev) // block_rows]
    row_parts = [slice(part * seg_rows, (part + 1) * seg_rows) for part in range(STREAMS)]
    gathered = [gather_rows(inputs[rows]) for rows in row_parts]
    out_sel, gathered[0] = lax.optimization_barrier((w_out[peer_kind], gathered[0]))
    out_rows_w = lax.all_to_all(out_sel, "tensor", 0, 0, tiled=True)
    outs, ins, grads, smalls = [], [], [], []
    for part in range(STREAMS):
        first_row = jnp.arange(n_tensor) * tok_dev + part * seg_rows
        seg_kind = block_kind[first_row // block_rows]
        chain_ids = (
            jnp.arange(n_tensor)[:, None] * dev_chains + part * chains + jnp.arange(chains)[None, :]
        )
        seg_lens = lengths[chain_ids]
        own_rows = rank * tok_dev + part * seg_rows + jnp.arange(seg_rows)
        row_kind = block_kind[own_rows // block_rows]
        rows = row_parts[part]
        out_part, in_part, grad_part, small_part = stream(
            inputs[rows],
            gathered[part],
            cotangent[rows],
            seg_kind,
            seg_lens,
            row_kind,
            out_rows_w,
            *weights,
        )
        outs.append(out_part)
        ins.append(in_part)
        grads.append(grad_part)
        smalls.append(small_part)
    layer_out = jnp.concatenate(outs, axis=0)
    input_grad = jnp.concatenate(ins, axis=0)
    grad_qkv, grad_qv, grad_out_w, grad_up, grad_ubias, grad_down = (
        sum(parts[1:], parts[0]) for parts in zip(*grads)
    )
    small = sum(smalls[1:], smalls[0])
    up_total, down_total = dp_sum_low((grad_up, grad_down))
    qkv_t_total, out_total = dp_sum_low((grad_qkv, grad_out_w))
    qkv_total = jnp.swapaxes(qkv_t_total, 2, 3)
    (small_grads,) = exact_sum((small,), "tensor")
    width = small.shape[-1]
    packed = jnp.concatenate(
        [small_grads.reshape(-1, width), grad_ubias.reshape(-1, width), grad_qv.reshape(-1, width)]
    )
    (packed,) = exact_sum((packed,), "dp")
    n_small, n_ubias = small_grads.size // width, grad_ubias.size // width
    small_total = packed[:n_small].reshape(small_grads.shape)
    ubias_total = packed[n_small : n_small + n_ubias].reshape(grad_ubias.shape)
    qv_total = packed[n_small + n_ubias :].reshape(grad_qv.shape)
    return (
        layer_out,
        input_grad,
        qkv_total,
        qv_total,
        out_total,
        small_total[0],
        small_total[1],
        small_total[2],
        up_total,
        ubias_total,
        down_total,
    )


def solution(mesh):
    return jax.shard_map(
        local,
        mesh=mesh,
        in_specs=(
            P(("dp", "tensor"), None),
            P(("dp", "tensor"), None),
            P("dp"),
            P("dp"),
            P(None, None, None, "tensor"),
            P(None, None, "tensor"),
            P(None, "tensor", None),
            P(),
            P(),
            P(),
            P(None, None, "tensor"),
            P(None, "tensor"),
            P(None, "tensor", None),
        ),
        out_specs=(
            P(("dp", "tensor"), None),
            P(("dp", "tensor"), None),
            P(None, None, None, "tensor"),
            P(None, None, "tensor"),
            P(None, "tensor", None),
            P(),
            P(),
            P(),
            P(None, None, "tensor"),
            P(None, "tensor"),
            P(None, "tensor", None),
        ),
        check_vma=False,
    )
```

```python
import jax
import jax.numpy as jnp
from jax import lax
from jax.sharding import PartitionSpec as P

HEAD_DIM = 64
CHAIN = 128
BLOCK_SEQS = 4
STREAMS = 2


EPSILON = 1e-05
SQRT_HALF = 0.7071067811865476
INV_ROOT_TWO_PI = 0.3989422804014327


def norm_forward(row_data, gain_rows, shift_rows):
    mean_row = jnp.mean(row_data, axis=-1, keepdims=True)
    centred = row_data - mean_row
    var_row = jnp.mean(centred * centred, axis=-1, keepdims=True)
    inv_std = lax.rsqrt(var_row + EPSILON)
    unit_rows = centred * inv_std
    return (unit_rows * gain_rows + shift_rows, unit_rows, inv_std)


def norm_backward(grad_rows, gain_rows, unit_rows, inv_std):
    scaled = grad_rows * gain_rows
    mean_first = jnp.mean(scaled, axis=-1, keepdims=True)
    mean_second = jnp.mean(scaled * unit_rows, axis=-1, keepdims=True)
    return inv_std * (scaled - mean_first - unit_rows * mean_second)


def type_sum(kind_hot, values):
    return jnp.einsum("rt,rd->td", kind_hot, values, precision=lax.Precision.HIGHEST)


def gelu_slope(values):
    return 0.5 * (1.0 + lax.erf(values * SQRT_HALF)) + values * INV_ROOT_TWO_PI * jnp.exp(
        -0.5 * values * values
    )


def gather_rows(local_rows):
    return lax.all_gather(local_rows, "tensor", axis=0, tiled=False)


def scatter_sum(seg_parts):
    n_seg, seg_rows, width = seg_parts.shape
    summed = lax.psum_scatter(
        seg_parts.reshape(n_seg * seg_rows, width).astype(jnp.bfloat16),
        "tensor",
        scatter_dimension=0,
        tiled=True,
    )
    return summed.astype(jnp.float32)


def masked(seg_rows, seg_hot):
    return seg_rows[:, None] * seg_hot[:, :, None, None].astype(seg_rows.dtype)


def kind_sums(seg_hot, seg_totals):
    return jnp.einsum(
        "st,se->te", seg_hot, seg_totals, precision=lax.Precision.HIGHEST
    )


def dp_perm(n, bit):
    return [(j, j ^ bit) for j in range(n)]


def dp_sum_low(parts):
    shapes = [p.shape for p in parts]
    n_dp = lax.axis_size("dp")
    idx = lax.axis_index("dp")
    steps = n_dp.bit_length() - 1
    cur = [p.reshape(-1, p.shape[-1]) for p in parts]
    assert 1 << steps == n_dp and all(c.shape[0] % n_dp == 0 for c in cur)
    for b in range(steps):
        upper = ((idx >> b) & 1) == 1
        halves = [(c[: c.shape[0] // 2], c[c.shape[0] // 2 :]) for c in cur]
        sends = tuple(jnp.where(upper, lo, hi).astype(jnp.bfloat16) for lo, hi in halves)
        gots = lax.ppermute(sends, "dp", dp_perm(n_dp, 1 << b))
        cur = [jnp.where(upper, hi, lo) + g.astype(jnp.float32) for (lo, hi), g in zip(halves, gots)]
    cur = [c.astype(jnp.bfloat16) for c in cur]
    for b in reversed(range(steps)):
        upper = ((idx >> b) & 1) == 1
        gots = lax.ppermute(tuple(cur), "dp", dp_perm(n_dp, 1 << b))
        cur = [
            jnp.where(upper, jnp.concatenate([g, c]), jnp.concatenate([c, g]))
            for c, g in zip(cur, gots)
        ]
    return [c.astype(jnp.float32).reshape(shape) for c, shape in zip(cur, shapes)]


def exact_sum(values, axis):
    n_ax = lax.axis_size(axis)
    steps = n_ax.bit_length() - 1
    assert 1 << steps == n_ax
    for b in range(steps):
        values = tuple(
            v + g for v, g in zip(values, lax.ppermute(values, axis, dp_perm(n_ax, 1 << b)))
        )
    return values


def stream(
    inputs,
    after,
    cotangent,
    seg_kind,
    seg_lens,
    row_kind,
    out_rows_w,
    w_qkv,
    qv_bias,
    w_out,
    resid_bias,
    norm_gain,
    norm_shift,
    w_up,
    up_bias,
    w_down,
):
    n_seg, chains = seg_lens.shape
    seg_rows = chains * CHAIN
    heads_here = w_qkv.shape[3] // HEAD_DIM
    score_scale = HEAD_DIM ** (-0.5)
    highest = lax.Precision.HIGHEST
    seg_hot = (seg_kind[:, None] == jnp.arange(2)[None, :]).astype(jnp.float32)
    kind_hot = (row_kind[:, None] == jnp.arange(2)[None, :]).astype(jnp.float32)

    def pick(kind_table):
        return jnp.dot(kind_hot, kind_table.astype(jnp.float32), precision=highest)

    def heads(rows):
        return rows.reshape(n_seg, chains, CHAIN, heads_here, HEAD_DIM)

    key_valid = jnp.arange(CHAIN)[None, None, :] < seg_lens[:, :, None]

    qkv_sel = w_qkv[seg_kind]
    qvb_sel = qv_bias[seg_kind].astype(jnp.float32)
    out_sel = w_out[seg_kind]
    up_sel = w_up[seg_kind]
    ubias_sel = up_bias[seg_kind].astype(jnp.float32)
    down_sel = w_down[seg_kind]

    input_segs = gather_rows(inputs)
    projected = jnp.einsum(
        "srd,sjde->jsre", input_segs, qkv_sel, preferred_element_type=jnp.float32
    )
    query_rows = (projected[0] + qvb_sel[:, None, 0]).astype(jnp.bfloat16)
    key_rows = projected[1].astype(jnp.bfloat16)
    value_rows = (projected[2] + qvb_sel[:, None, 1]).astype(jnp.bfloat16)

    def probs_of():
        raw_scores = (
            jnp.einsum(
                "scqhd,sckhd->schqk",
                heads(query_rows),
                heads(key_rows),
                preferred_element_type=jnp.float32,
            )
            * score_scale
        )
        return jnp.where(key_valid[:, :, None, None, :], raw_scores, -1e30)

    scores = probs_of()
    row_max = jnp.max(scores, axis=-1, keepdims=True)
    log_total = row_max[..., 0] + jnp.log(jnp.sum(jnp.exp(scores - row_max), axis=-1))
    attn_probs = jnp.exp(scores - log_total[..., None])
    probs_low = attn_probs.astype(jnp.bfloat16)
    mixed = jnp.einsum(
        "schqk,sckhd->scqhd", probs_low, heads(value_rows), preferred_element_type=jnp.float32
    )
    mixed = mixed.reshape(n_seg, seg_rows, -1).astype(jnp.bfloat16)
    mixed_rows = lax.all_to_all(mixed, "tensor", 0, 0, tiled=True)
    attn_rows = jnp.einsum(
        "erc,ecd->rd", mixed_rows, out_rows_w, preferred_element_type=jnp.float32
    )

    hidden_one = inputs.astype(jnp.float32) + attn_rows + pick(resid_bias[:, 0])
    gain_one = pick(norm_gain[:, 0])
    normed, unit_one, inv_one = norm_forward(hidden_one, gain_one, pick(norm_shift[:, 0]))
    normed_low = normed.astype(jnp.bfloat16)
    norm_segs = gather_rows(normed_low)
    pre_act = (
        jnp.einsum("srd,sdf->srf", norm_segs, up_sel, preferred_element_type=jnp.float32)
        + ubias_sel[:, None]
    )
    activ = jax.nn.gelu(pre_act, approximate=False).astype(jnp.bfloat16)
    ffn_parts = jnp.einsum("srf,sfd->srd", activ, down_sel, preferred_element_type=jnp.float32)
    ffn_rows = scatter_sum(ffn_parts)

    hidden_two = normed + ffn_rows + pick(resid_bias[:, 1])
    gain_two = pick(norm_gain[:, 1])
    output_rows, unit_two, inv_two = norm_forward(hidden_two, gain_two, pick(norm_shift[:, 1]))
    layer_out = output_rows.astype(jnp.bfloat16)
    grad_out = cotangent.astype(jnp.float32)
    d_two = norm_backward(grad_out, gain_two, unit_two, inv_two)
    two_segs = gather_rows(d_two.astype(jnp.bfloat16))

    grad_down = jnp.einsum(
        "strf,srd->tfd", masked(activ, seg_hot), two_segs, preferred_element_type=jnp.float32
    )
    d_activ = jnp.einsum(
        "srd,sfd->srf", two_segs, down_sel, preferred_element_type=jnp.float32
    ).astype(jnp.bfloat16)
    d_pre = (d_activ.astype(jnp.float32) * gelu_slope(pre_act)).astype(jnp.bfloat16)
    grad_up = jnp.einsum(
        "strd,srf->tdf", masked(norm_segs, seg_hot), d_pre, preferred_element_type=jnp.float32
    )
    grad_ubias = kind_sums(seg_hot, jnp.sum(d_pre.astype(jnp.float32), axis=1))
    ffn_back = jnp.einsum("srf,sdf->srd", d_pre, up_sel, preferred_element_type=jnp.float32)
    d_normed = scatter_sum(ffn_back) + d_two

    d_one = norm_backward(d_normed, gain_one, unit_one, inv_one)
    gain_grads = jnp.stack(
        [type_sum(kind_hot, d_normed * unit_one), type_sum(kind_hot, grad_out * unit_two)], axis=1
    )
    shift_grads = jnp.stack([type_sum(kind_hot, d_normed), type_sum(kind_hot, grad_out)], axis=1)
    rbias_grads = jnp.stack([type_sum(kind_hot, d_one), type_sum(kind_hot, d_two)], axis=1)
    one_segs = gather_rows(d_one.astype(jnp.bfloat16))
    if after is not None:
        one_segs, _ = lax.optimization_barrier((one_segs, after))

    grad_out_w = jnp.einsum(
        "stre,srd->ted", masked(mixed, seg_hot), one_segs, preferred_element_type=jnp.float32
    )
    d_mixed = jnp.einsum(
        "srd,sed->sre", one_segs, out_sel, preferred_element_type=jnp.float32
    ).astype(jnp.bfloat16)
    d_mixed_heads = heads(d_mixed)
    d_value = jnp.einsum(
        "schqk,scqhd->sckhd", probs_low, d_mixed_heads, preferred_element_type=jnp.float32
    )
    d_value = d_value.reshape(n_seg, seg_rows, -1).astype(jnp.bfloat16)
    d_probs = jnp.einsum(
        "scqhd,sckhd->schqk", d_mixed_heads, heads(value_rows), preferred_element_type=jnp.float32
    )
    prob_dot = jnp.sum(attn_probs * d_probs, axis=-1, keepdims=True)
    d_scores = (attn_probs * (d_probs - prob_dot)).astype(jnp.bfloat16)
    d_query = (
        jnp.einsum(
            "schqk,sckhd->scqhd", d_scores, heads(key_rows), preferred_element_type=jnp.float32
        )
        * score_scale
    )
    d_key = (
        jnp.einsum(
            "schqk,scqhd->sckhd", d_scores, heads(query_rows), preferred_element_type=jnp.float32
        )
        * score_scale
    )
    d_query = d_query.reshape(n_seg, seg_rows, -1).astype(jnp.bfloat16)
    d_key = d_key.reshape(n_seg, seg_rows, -1).astype(jnp.bfloat16)
    d_proj = jnp.stack([d_query, d_key, d_value])
    grad_qkv = jnp.einsum(
        "strd,jsre->tjed", masked(input_segs, seg_hot), d_proj, preferred_element_type=jnp.float32
    )
    grad_qv = jnp.stack(
        [
            kind_sums(seg_hot, jnp.sum(d_query.astype(jnp.float32), axis=1)),
            kind_sums(seg_hot, jnp.sum(d_value.astype(jnp.float32), axis=1)),
        ],
        axis=1,
    )
    qkv_back = jnp.einsum("jsre,sjde->srd", d_proj, qkv_sel, preferred_element_type=jnp.float32)
    input_grad = scatter_sum(qkv_back) + d_one
    small = jnp.stack([rbias_grads, gain_grads, shift_grads])
    return (
        layer_out,
        input_grad,
        (grad_qkv, grad_qv, grad_out_w, grad_up, grad_ubias, grad_down),
        small,
        qkv_back,
    )


def local(
    inputs,
    cotangent,
    lengths,
    block_kind,
    w_qkv,
    qv_bias,
    w_out,
    resid_bias,
    norm_gain,
    norm_shift,
    w_up,
    up_bias,
    w_down,
):
    tok_dev = inputs.shape[0]
    n_tensor = lax.axis_size("tensor")
    rank = lax.axis_index("tensor")
    block_rows = BLOCK_SEQS * CHAIN
    assert block_rows % tok_dev == 0
    dev_chains = tok_dev // CHAIN
    chains = dev_chains // STREAMS
    seg_rows = chains * CHAIN
    weights = (w_qkv, qv_bias, w_out, resid_bias, norm_gain, norm_shift, w_up, up_bias, w_down)
    peer_kind = block_kind[(jnp.arange(n_tensor) * tok_dev) // block_rows]
    out_rows_w = lax.all_to_all(w_out[peer_kind], "tensor", 0, 0, tiled=True)
    outs, ins, grads, smalls = [], [], [], []
    mark = None
    for part in range(STREAMS):
        first_row = jnp.arange(n_tensor) * tok_dev + part * seg_rows
        seg_kind = block_kind[first_row // block_rows]
        chain_ids = (
            jnp.arange(n_tensor)[:, None] * dev_chains + part * chains + jnp.arange(chains)[None, :]
        )
        seg_lens = lengths[chain_ids]
        own_rows = rank * tok_dev + part * seg_rows + jnp.arange(seg_rows)
        row_kind = block_kind[own_rows // block_rows]
        rows = slice(part * seg_rows, (part + 1) * seg_rows)
        out_part, in_part, grad_part, small_part, mark = stream(
            inputs[rows], mark, cotangent[rows], seg_kind, seg_lens, row_kind, out_rows_w, *weights
        )
        outs.append(out_part)
        ins.append(in_part)
        grads.append(grad_part)
        smalls.append(small_part)
    layer_out = jnp.concatenate(outs, axis=0)
    input_grad = jnp.concatenate(ins, axis=0)
    grad_qkv, grad_qv, grad_out_w, grad_up, grad_ubias, grad_down = (
        sum(parts[1:], parts[0]) for parts in zip(*grads)
    )
    small = sum(smalls[1:], smalls[0])
    up_total, down_total = dp_sum_low((grad_up, grad_down))
    qkv_t_total, out_total = dp_sum_low((grad_qkv, grad_out_w))
    qkv_total = jnp.swapaxes(qkv_t_total, 2, 3)
    (small_grads,) = exact_sum((small,), "tensor")
    width = small.shape[-1]
    packed = jnp.concatenate(
        [small_grads.reshape(-1, width), grad_ubias.reshape(-1, width), grad_qv.reshape(-1, width)]
    )
    (packed,) = exact_sum((packed,), "dp")
    n_small, n_ubias = small_grads.size // width, grad_ubias.size // width
    small_total = packed[:n_small].reshape(small_grads.shape)
    ubias_total = packed[n_small : n_small + n_ubias].reshape(grad_ubias.shape)
    qv_total = packed[n_small + n_ubias :].reshape(grad_qv.shape)
    return (
        layer_out,
        input_grad,
        qkv_total,
        qv_total,
        out_total,
        small_total[0],
        small_total[1],
        small_total[2],
        up_total,
        ubias_total,
        down_total,
    )


def solution(mesh):
    return jax.shard_map(
        local,
        mesh=mesh,
        in_specs=(
            P(("dp", "tensor"), None),
            P(("dp", "tensor"), None),
            P("dp"),
            P("dp"),
            P(None, None, None, "tensor"),
            P(None, None, "tensor"),
            P(None, "tensor", None),
            P(),
            P(),
            P(),
            P(None, None, "tensor"),
            P(None, "tensor"),
            P(None, "tensor", None),
        ),
        out_specs=(
            P(("dp", "tensor"), None),
            P(("dp", "tensor"), None),
            P(None, None, None, "tensor"),
            P(None, None, "tensor"),
            P(None, "tensor", None),
            P(),
            P(),
            P(),
            P(None, None, "tensor"),
            P(None, "tensor"),
            P(None, "tensor", None),
        ),
        check_vma=False,
    )
```

```python
import jax
import jax.numpy as jnp
from jax import lax
from jax.sharding import PartitionSpec as P

HEAD_DIM = 64
CHAIN = 128
BLOCK_SEQS = 4
STREAMS = 2


EPSILON = 1e-05
SQRT_HALF = 0.7071067811865476
INV_ROOT_TWO_PI = 0.3989422804014327


def norm_forward(row_data, gain_rows, shift_rows):
    mean_row = jnp.mean(row_data, axis=-1, keepdims=True)
    centred = row_data - mean_row
    var_row = jnp.mean(centred * centred, axis=-1, keepdims=True)
    inv_std = lax.rsqrt(var_row + EPSILON)
    unit_rows = centred * inv_std
    return (unit_rows * gain_rows + shift_rows, unit_rows, inv_std)


def norm_backward(grad_rows, gain_rows, unit_rows, inv_std):
    scaled = grad_rows * gain_rows
    mean_first = jnp.mean(scaled, axis=-1, keepdims=True)
    mean_second = jnp.mean(scaled * unit_rows, axis=-1, keepdims=True)
    return inv_std * (scaled - mean_first - unit_rows * mean_second)


def type_sum(kind_hot, values):
    return jnp.einsum("rt,rd->td", kind_hot, values, precision=lax.Precision.HIGHEST)


def gelu_slope(values):
    return 0.5 * (1.0 + lax.erf(values * SQRT_HALF)) + values * INV_ROOT_TWO_PI * jnp.exp(
        -0.5 * values * values
    )


def gather_rows(local_rows):
    return lax.all_gather(local_rows, "tensor", axis=0, tiled=False)


def scatter_sum(seg_parts):
    n_seg, seg_rows, width = seg_parts.shape
    summed = lax.psum_scatter(
        seg_parts.reshape(n_seg * seg_rows, width).astype(jnp.bfloat16),
        "tensor",
        scatter_dimension=0,
        tiled=True,
    )
    return summed.astype(jnp.float32)


def masked(seg_rows, seg_hot):
    return seg_rows[:, None] * seg_hot[:, :, None, None].astype(seg_rows.dtype)


def kind_sums(seg_hot, seg_totals):
    return jnp.einsum(
        "st,se->te", seg_hot, seg_totals, precision=lax.Precision.HIGHEST
    )


def dp_perm(n, bit):
    return [(j, j ^ bit) for j in range(n)]


def dp_sum_low(parts):
    shapes = [p.shape for p in parts]
    n_dp = lax.axis_size("dp")
    idx = lax.axis_index("dp")
    steps = n_dp.bit_length() - 1
    cur = [p.reshape(-1, p.shape[-1]) for p in parts]
    assert 1 << steps == n_dp and all(c.shape[0] % n_dp == 0 for c in cur)
    for b in range(steps):
        upper = ((idx >> b) & 1) == 1
        halves = [(c[: c.shape[0] // 2], c[c.shape[0] // 2 :]) for c in cur]
        sends = tuple(jnp.where(upper, lo, hi).astype(jnp.bfloat16) for lo, hi in halves)
        gots = lax.ppermute(sends, "dp", dp_perm(n_dp, 1 << b))
        cur = [jnp.where(upper, hi, lo) + g.astype(jnp.float32) for (lo, hi), g in zip(halves, gots)]
    cur = [c.astype(jnp.bfloat16) for c in cur]
    for b in reversed(range(steps)):
        upper = ((idx >> b) & 1) == 1
        gots = lax.ppermute(tuple(cur), "dp", dp_perm(n_dp, 1 << b))
        cur = [
            jnp.where(upper, jnp.concatenate([g, c]), jnp.concatenate([c, g]))
            for c, g in zip(cur, gots)
        ]
    return [c.astype(jnp.float32).reshape(shape) for c, shape in zip(cur, shapes)]


def exact_sum(values, axis):
    n_ax = lax.axis_size(axis)
    steps = n_ax.bit_length() - 1
    assert 1 << steps == n_ax
    for b in range(steps):
        values = tuple(
            v + g for v, g in zip(values, lax.ppermute(values, axis, dp_perm(n_ax, 1 << b)))
        )
    return values


def stream(
    inputs,
    after,
    cotangent,
    seg_kind,
    seg_lens,
    row_kind,
    out_rows_w,
    w_qkv,
    qv_bias,
    w_out,
    resid_bias,
    norm_gain,
    norm_shift,
    w_up,
    up_bias,
    w_down,
):
    n_seg, chains = seg_lens.shape
    seg_rows = chains * CHAIN
    heads_here = w_qkv.shape[3] // HEAD_DIM
    score_scale = HEAD_DIM ** (-0.5)
    highest = lax.Precision.HIGHEST
    seg_hot = (seg_kind[:, None] == jnp.arange(2)[None, :]).astype(jnp.float32)
    kind_hot = (row_kind[:, None] == jnp.arange(2)[None, :]).astype(jnp.float32)

    def pick(kind_table):
        return jnp.dot(kind_hot, kind_table.astype(jnp.float32), precision=highest)

    def heads(rows):
        return rows.reshape(n_seg, chains, CHAIN, heads_here, HEAD_DIM)

    key_valid = jnp.arange(CHAIN)[None, None, :] < seg_lens[:, :, None]

    qkv_sel = w_qkv[seg_kind]
    qvb_sel = qv_bias[seg_kind].astype(jnp.float32)
    out_sel = w_out[seg_kind]
    up_sel = w_up[seg_kind]
    ubias_sel = up_bias[seg_kind].astype(jnp.float32)
    down_sel = w_down[seg_kind]

    input_segs = gather_rows(inputs)
    projected = jnp.einsum(
        "srd,sjde->jsre", input_segs, qkv_sel, preferred_element_type=jnp.float32
    )
    query_rows = (projected[0] + qvb_sel[:, None, 0]).astype(jnp.bfloat16)
    key_rows = projected[1].astype(jnp.bfloat16)
    value_rows = (projected[2] + qvb_sel[:, None, 1]).astype(jnp.bfloat16)

    def probs_of():
        raw_scores = (
            jnp.einsum(
                "scqhd,sckhd->schqk",
                heads(query_rows),
                heads(key_rows),
                preferred_element_type=jnp.float32,
            )
            * score_scale
        )
        return jnp.where(key_valid[:, :, None, None, :], raw_scores, -1e30)

    scores = probs_of()
    row_max = jnp.max(scores, axis=-1, keepdims=True)
    log_total = row_max[..., 0] + jnp.log(jnp.sum(jnp.exp(scores - row_max), axis=-1))
    attn_probs = jnp.exp(scores - log_total[..., None])
    probs_low = attn_probs.astype(jnp.bfloat16)
    mixed = jnp.einsum(
        "schqk,sckhd->scqhd", probs_low, heads(value_rows), preferred_element_type=jnp.float32
    )
    mixed = mixed.reshape(n_seg, seg_rows, -1).astype(jnp.bfloat16)
    mixed_rows = lax.all_to_all(mixed, "tensor", 0, 0, tiled=True)
    attn_rows = jnp.einsum(
        "erc,ecd->rd", mixed_rows, out_rows_w, preferred_element_type=jnp.float32
    )

    hidden_one = inputs.astype(jnp.float32) + attn_rows + pick(resid_bias[:, 0])
    gain_one = pick(norm_gain[:, 0])
    normed, unit_one, inv_one = norm_forward(hidden_one, gain_one, pick(norm_shift[:, 0]))
    normed_low = normed.astype(jnp.bfloat16)
    norm_segs = gather_rows(normed_low)
    pre_act = (
        jnp.einsum("srd,sdf->srf", norm_segs, up_sel, preferred_element_type=jnp.float32)
        + ubias_sel[:, None]
    )
    activ = jax.nn.gelu(pre_act, approximate=False).astype(jnp.bfloat16)
    ffn_parts = jnp.einsum("srf,sfd->srd", activ, down_sel, preferred_element_type=jnp.float32)
    ffn_rows = scatter_sum(ffn_parts)

    hidden_two = normed + ffn_rows + pick(resid_bias[:, 1])
    gain_two = pick(norm_gain[:, 1])
    output_rows, unit_two, inv_two = norm_forward(hidden_two, gain_two, pick(norm_shift[:, 1]))
    layer_out = output_rows.astype(jnp.bfloat16)
    grad_out = cotangent.astype(jnp.float32)
    d_two = norm_backward(grad_out, gain_two, unit_two, inv_two)
    two_segs = gather_rows(d_two.astype(jnp.bfloat16))
    if after is not None:
        two_segs, _ = lax.optimization_barrier((two_segs, after[0]))

    grad_down = jnp.einsum(
        "strf,srd->tfd", masked(activ, seg_hot), two_segs, preferred_element_type=jnp.float32
    )
    d_activ = jnp.einsum(
        "srd,sfd->srf", two_segs, down_sel, preferred_element_type=jnp.float32
    ).astype(jnp.bfloat16)
    d_pre = (d_activ.astype(jnp.float32) * gelu_slope(pre_act)).astype(jnp.bfloat16)
    grad_up = jnp.einsum(
        "strd,srf->tdf", masked(norm_segs, seg_hot), d_pre, preferred_element_type=jnp.float32
    )
    grad_ubias = kind_sums(seg_hot, jnp.sum(d_pre.astype(jnp.float32), axis=1))
    ffn_back = jnp.einsum("srf,sdf->srd", d_pre, up_sel, preferred_element_type=jnp.float32)
    d_normed = scatter_sum(ffn_back) + d_two

    d_one = norm_backward(d_normed, gain_one, unit_one, inv_one)
    gain_grads = jnp.stack(
        [type_sum(kind_hot, d_normed * unit_one), type_sum(kind_hot, grad_out * unit_two)], axis=1
    )
    shift_grads = jnp.stack([type_sum(kind_hot, d_normed), type_sum(kind_hot, grad_out)], axis=1)
    rbias_grads = jnp.stack([type_sum(kind_hot, d_one), type_sum(kind_hot, d_two)], axis=1)
    one_segs = gather_rows(d_one.astype(jnp.bfloat16))
    if after is not None:
        one_segs, _ = lax.optimization_barrier((one_segs, after[1]))

    grad_out_w = jnp.einsum(
        "stre,srd->ted", masked(mixed, seg_hot), one_segs, preferred_element_type=jnp.float32
    )
    d_mixed = jnp.einsum(
        "srd,sed->sre", one_segs, out_sel, preferred_element_type=jnp.float32
    ).astype(jnp.bfloat16)
    d_mixed_heads = heads(d_mixed)
    d_value = jnp.einsum(
        "schqk,scqhd->sckhd", probs_low, d_mixed_heads, preferred_element_type=jnp.float32
    )
    d_value = d_value.reshape(n_seg, seg_rows, -1).astype(jnp.bfloat16)
    d_probs = jnp.einsum(
        "scqhd,sckhd->schqk", d_mixed_heads, heads(value_rows), preferred_element_type=jnp.float32
    )
    prob_dot = jnp.sum(attn_probs * d_probs, axis=-1, keepdims=True)
    d_scores = (attn_probs * (d_probs - prob_dot)).astype(jnp.bfloat16)
    d_query = (
        jnp.einsum(
            "schqk,sckhd->scqhd", d_scores, heads(key_rows), preferred_element_type=jnp.float32
        )
        * score_scale
    )
    d_key = (
        jnp.einsum(
            "schqk,scqhd->sckhd", d_scores, heads(query_rows), preferred_element_type=jnp.float32
        )
        * score_scale
    )
    d_query = d_query.reshape(n_seg, seg_rows, -1).astype(jnp.bfloat16)
    d_key = d_key.reshape(n_seg, seg_rows, -1).astype(jnp.bfloat16)
    d_proj = jnp.stack([d_query, d_key, d_value])
    grad_qkv = jnp.einsum(
        "strd,jsre->tjed", masked(input_segs, seg_hot), d_proj, preferred_element_type=jnp.float32
    )
    grad_qv = jnp.stack(
        [
            kind_sums(seg_hot, jnp.sum(d_query.astype(jnp.float32), axis=1)),
            kind_sums(seg_hot, jnp.sum(d_value.astype(jnp.float32), axis=1)),
        ],
        axis=1,
    )
    qkv_back = jnp.einsum("jsre,sjde->srd", d_proj, qkv_sel, preferred_element_type=jnp.float32)
    input_grad = scatter_sum(qkv_back) + d_one
    small = jnp.stack([rbias_grads, gain_grads, shift_grads])
    return (
        layer_out,
        input_grad,
        (grad_qkv, grad_qv, grad_out_w, grad_up, grad_ubias, grad_down),
        small,
        (ffn_back, qkv_back),
    )


def local(
    inputs,
    cotangent,
    lengths,
    block_kind,
    w_qkv,
    qv_bias,
    w_out,
    resid_bias,
    norm_gain,
    norm_shift,
    w_up,
    up_bias,
    w_down,
):
    tok_dev = inputs.shape[0]
    n_tensor = lax.axis_size("tensor")
    rank = lax.axis_index("tensor")
    block_rows = BLOCK_SEQS * CHAIN
    assert block_rows % tok_dev == 0
    dev_chains = tok_dev // CHAIN
    chains = dev_chains // STREAMS
    seg_rows = chains * CHAIN
    weights = (w_qkv, qv_bias, w_out, resid_bias, norm_gain, norm_shift, w_up, up_bias, w_down)
    peer_kind = block_kind[(jnp.arange(n_tensor) * tok_dev) // block_rows]
    out_rows_w = lax.all_to_all(w_out[peer_kind], "tensor", 0, 0, tiled=True)
    outs, ins, grads, smalls = [], [], [], []
    mark = None
    for part in range(STREAMS):
        first_row = jnp.arange(n_tensor) * tok_dev + part * seg_rows
        seg_kind = block_kind[first_row // block_rows]
        chain_ids = (
            jnp.arange(n_tensor)[:, None] * dev_chains + part * chains + jnp.arange(chains)[None, :]
        )
        seg_lens = lengths[chain_ids]
        own_rows = rank * tok_dev + part * seg_rows + jnp.arange(seg_rows)
        row_kind = block_kind[own_rows // block_rows]
        rows = slice(part * seg_rows, (part + 1) * seg_rows)
        out_part, in_part, grad_part, small_part, mark = stream(
            inputs[rows], mark, cotangent[rows], seg_kind, seg_lens, row_kind, out_rows_w, *weights
        )
        outs.append(out_part)
        ins.append(in_part)
        grads.append(grad_part)
        smalls.append(small_part)
    layer_out = jnp.concatenate(outs, axis=0)
    input_grad = jnp.concatenate(ins, axis=0)
    grad_qkv, grad_qv, grad_out_w, grad_up, grad_ubias, grad_down = (
        sum(parts[1:], parts[0]) for parts in zip(*grads)
    )
    small = sum(smalls[1:], smalls[0])
    up_total, down_total = dp_sum_low((grad_up, grad_down))
    qkv_t_total, out_total = dp_sum_low((grad_qkv, grad_out_w))
    qkv_total = jnp.swapaxes(qkv_t_total, 2, 3)
    (small_grads,) = exact_sum((small,), "tensor")
    width = small.shape[-1]
    packed = jnp.concatenate(
        [small_grads.reshape(-1, width), grad_ubias.reshape(-1, width), grad_qv.reshape(-1, width)]
    )
    (packed,) = exact_sum((packed,), "dp")
    n_small, n_ubias = small_grads.size // width, grad_ubias.size // width
    small_total = packed[:n_small].reshape(small_grads.shape)
    ubias_total = packed[n_small : n_small + n_ubias].reshape(grad_ubias.shape)
    qv_total = packed[n_small + n_ubias :].reshape(grad_qv.shape)
    return (
        layer_out,
        input_grad,
        qkv_total,
        qv_total,
        out_total,
        small_total[0],
        small_total[1],
        small_total[2],
        up_total,
        ubias_total,
        down_total,
    )


def solution(mesh):
    return jax.shard_map(
        local,
        mesh=mesh,
        in_specs=(
            P(("dp", "tensor"), None),
            P(("dp", "tensor"), None),
            P("dp"),
            P("dp"),
            P(None, None, None, "tensor"),
            P(None, None, "tensor"),
            P(None, "tensor", None),
            P(),
            P(),
            P(),
            P(None, None, "tensor"),
            P(None, "tensor"),
            P(None, "tensor", None),
        ),
        out_specs=(
            P(("dp", "tensor"), None),
            P(("dp", "tensor"), None),
            P(None, None, None, "tensor"),
            P(None, None, "tensor"),
            P(None, "tensor", None),
            P(),
            P(),
            P(),
            P(None, None, "tensor"),
            P(None, "tensor"),
            P(None, "tensor", None),
        ),
        check_vma=False,
    )
```

```python
import jax
import jax.numpy as jnp
from jax import lax
from jax.sharding import PartitionSpec as P

HEAD_DIM = 64
CHAIN = 128
BLOCK_SEQS = 4
STREAMS = 2


EPSILON = 1e-05
SQRT_HALF = 0.7071067811865476
INV_ROOT_TWO_PI = 0.3989422804014327


def norm_forward(row_data, gain_rows, shift_rows):
    mean_row = jnp.mean(row_data, axis=-1, keepdims=True)
    centred = row_data - mean_row
    var_row = jnp.mean(centred * centred, axis=-1, keepdims=True)
    inv_std = lax.rsqrt(var_row + EPSILON)
    unit_rows = centred * inv_std
    return (unit_rows * gain_rows + shift_rows, unit_rows, inv_std)


def norm_backward(grad_rows, gain_rows, unit_rows, inv_std):
    scaled = grad_rows * gain_rows
    mean_first = jnp.mean(scaled, axis=-1, keepdims=True)
    mean_second = jnp.mean(scaled * unit_rows, axis=-1, keepdims=True)
    return inv_std * (scaled - mean_first - unit_rows * mean_second)


def type_sum(kind_hot, values):
    return jnp.einsum("rt,rd->td", kind_hot, values, precision=lax.Precision.HIGHEST)


def gelu_slope(values):
    return 0.5 * (1.0 + lax.erf(values * SQRT_HALF)) + values * INV_ROOT_TWO_PI * jnp.exp(
        -0.5 * values * values
    )


def gather_rows(local_rows):
    return lax.all_gather(local_rows, "tensor", axis=0, tiled=False)


def scatter_sum(seg_parts):
    n_seg, seg_rows, width = seg_parts.shape
    summed = lax.psum_scatter(
        seg_parts.reshape(n_seg * seg_rows, width).astype(jnp.bfloat16),
        "tensor",
        scatter_dimension=0,
        tiled=True,
    )
    return summed.astype(jnp.float32)


def masked(seg_rows, seg_hot):
    return seg_rows[:, None] * seg_hot[:, :, None, None].astype(seg_rows.dtype)


def kind_sums(seg_hot, seg_totals):
    return jnp.einsum(
        "st,se->te", seg_hot, seg_totals, precision=lax.Precision.HIGHEST
    )


def dp_perm(n, bit):
    return [(j, j ^ bit) for j in range(n)]


def dp_sum_low(parts):
    shapes = [p.shape for p in parts]
    n_dp = lax.axis_size("dp")
    idx = lax.axis_index("dp")
    steps = n_dp.bit_length() - 1
    cur = [p.reshape(-1, p.shape[-1]) for p in parts]
    assert 1 << steps == n_dp and all(c.shape[0] % n_dp == 0 for c in cur)
    for b in range(steps):
        upper = ((idx >> b) & 1) == 1
        halves = [(c[: c.shape[0] // 2], c[c.shape[0] // 2 :]) for c in cur]
        sends = tuple(jnp.where(upper, lo, hi).astype(jnp.bfloat16) for lo, hi in halves)
        gots = lax.ppermute(sends, "dp", dp_perm(n_dp, 1 << b))
        cur = [jnp.where(upper, hi, lo) + g.astype(jnp.float32) for (lo, hi), g in zip(halves, gots)]
    cur = [c.astype(jnp.bfloat16) for c in cur]
    for b in reversed(range(steps)):
        upper = ((idx >> b) & 1) == 1
        gots = lax.ppermute(tuple(cur), "dp", dp_perm(n_dp, 1 << b))
        if b == 0:
            cur = [c.astype(jnp.float32) for c in cur]
            gots = [g.astype(jnp.float32) for g in gots]
        cur = [
            jnp.where(upper, jnp.concatenate([g, c]), jnp.concatenate([c, g]))
            for c, g in zip(cur, gots)
        ]
    return [c.reshape(shape) for c, shape in zip(cur, shapes)]


def exact_sum(values, axis):
    n_ax = lax.axis_size(axis)
    steps = n_ax.bit_length() - 1
    assert 1 << steps == n_ax
    for b in range(steps):
        values = tuple(
            v + g for v, g in zip(values, lax.ppermute(values, axis, dp_perm(n_ax, 1 << b)))
        )
    return values


def stream(
    inputs,
    after,
    cotangent,
    seg_kind,
    seg_lens,
    row_kind,
    out_rows_w,
    w_qkv,
    qv_bias,
    w_out,
    resid_bias,
    norm_gain,
    norm_shift,
    w_up,
    up_bias,
    w_down,
):
    n_seg, chains = seg_lens.shape
    seg_rows = chains * CHAIN
    heads_here = w_qkv.shape[3] // HEAD_DIM
    score_scale = HEAD_DIM ** (-0.5)
    highest = lax.Precision.HIGHEST
    seg_hot = (seg_kind[:, None] == jnp.arange(2)[None, :]).astype(jnp.float32)
    kind_hot = (row_kind[:, None] == jnp.arange(2)[None, :]).astype(jnp.float32)

    def pick(kind_table):
        return jnp.dot(kind_hot, kind_table.astype(jnp.float32), precision=highest)

    def heads(rows):
        return rows.reshape(n_seg, chains, CHAIN, heads_here, HEAD_DIM)

    key_valid = jnp.arange(CHAIN)[None, None, :] < seg_lens[:, :, None]

    qkv_sel = w_qkv[seg_kind]
    qvb_sel = qv_bias[seg_kind].astype(jnp.float32)
    out_sel = w_out[seg_kind]
    up_sel = w_up[seg_kind]
    ubias_sel = up_bias[seg_kind].astype(jnp.float32)
    down_sel = w_down[seg_kind]

    input_segs = gather_rows(inputs)
    projected = jnp.einsum(
        "srd,sjde->jsre", input_segs, qkv_sel, preferred_element_type=jnp.float32
    )
    query_rows = (projected[0] + qvb_sel[:, None, 0]).astype(jnp.bfloat16)
    key_rows = projected[1].astype(jnp.bfloat16)
    value_rows = (projected[2] + qvb_sel[:, None, 1]).astype(jnp.bfloat16)

    def probs_of():
        raw_scores = (
            jnp.einsum(
                "scqhd,sckhd->schqk",
                heads(query_rows),
                heads(key_rows),
                preferred_element_type=jnp.float32,
            )
            * score_scale
        )
        return jnp.where(key_valid[:, :, None, None, :], raw_scores, -1e30)

    scores = probs_of()
    row_max = jnp.max(scores, axis=-1, keepdims=True)
    log_total = row_max[..., 0] + jnp.log(jnp.sum(jnp.exp(scores - row_max), axis=-1))
    attn_probs = jnp.exp(scores - log_total[..., None])
    probs_low = attn_probs.astype(jnp.bfloat16)
    mixed = jnp.einsum(
        "schqk,sckhd->scqhd", probs_low, heads(value_rows), preferred_element_type=jnp.float32
    )
    mixed = mixed.reshape(n_seg, seg_rows, -1).astype(jnp.bfloat16)
    mixed_rows = lax.all_to_all(mixed, "tensor", 0, 0, tiled=True)
    attn_rows = jnp.einsum(
        "erc,ecd->rd", mixed_rows, out_rows_w, preferred_element_type=jnp.float32
    )

    hidden_one = inputs.astype(jnp.float32) + attn_rows + pick(resid_bias[:, 0])
    gain_one = pick(norm_gain[:, 0])
    normed, unit_one, inv_one = norm_forward(hidden_one, gain_one, pick(norm_shift[:, 0]))
    normed_low = normed.astype(jnp.bfloat16)
    norm_segs = gather_rows(normed_low)
    pre_act = (
        jnp.einsum("srd,sdf->srf", norm_segs, up_sel, preferred_element_type=jnp.float32)
        + ubias_sel[:, None]
    )
    activ = jax.nn.gelu(pre_act, approximate=False).astype(jnp.bfloat16)
    ffn_parts = jnp.einsum("srf,sfd->srd", activ, down_sel, preferred_element_type=jnp.float32)
    ffn_rows = scatter_sum(ffn_parts)

    hidden_two = normed + ffn_rows + pick(resid_bias[:, 1])
    gain_two = pick(norm_gain[:, 1])
    output_rows, unit_two, inv_two = norm_forward(hidden_two, gain_two, pick(norm_shift[:, 1]))
    layer_out = output_rows.astype(jnp.bfloat16)
    grad_out = cotangent.astype(jnp.float32)
    d_two = norm_backward(grad_out, gain_two, unit_two, inv_two)
    two_segs = gather_rows(d_two.astype(jnp.bfloat16))

    grad_down = jnp.einsum(
        "strf,srd->tfd", masked(activ, seg_hot), two_segs, preferred_element_type=jnp.float32
    )
    d_activ = jnp.einsum(
        "srd,sfd->srf", two_segs, down_sel, preferred_element_type=jnp.float32
    ).astype(jnp.bfloat16)
    d_pre = (d_activ.astype(jnp.float32) * gelu_slope(pre_act)).astype(jnp.bfloat16)
    grad_up = jnp.einsum(
        "strd,srf->tdf", masked(norm_segs, seg_hot), d_pre, preferred_element_type=jnp.float32
    )
    grad_ubias = kind_sums(seg_hot, jnp.sum(d_pre.astype(jnp.float32), axis=1))
    ffn_back = jnp.einsum("srf,sdf->srd", d_pre, up_sel, preferred_element_type=jnp.float32)
    d_normed = scatter_sum(ffn_back) + d_two

    d_one = norm_backward(d_normed, gain_one, unit_one, inv_one)
    gain_grads = jnp.stack(
        [type_sum(kind_hot, d_normed * unit_one), type_sum(kind_hot, grad_out * unit_two)], axis=1
    )
    shift_grads = jnp.stack([type_sum(kind_hot, d_normed), type_sum(kind_hot, grad_out)], axis=1)
    rbias_grads = jnp.stack([type_sum(kind_hot, d_one), type_sum(kind_hot, d_two)], axis=1)
    one_segs = gather_rows(d_one.astype(jnp.bfloat16))
    if after is not None:
        one_segs, _ = lax.optimization_barrier((one_segs, after))

    grad_out_w = jnp.einsum(
        "stre,srd->ted", masked(mixed, seg_hot), one_segs, preferred_element_type=jnp.float32
    )
    d_mixed = jnp.einsum(
        "srd,sed->sre", one_segs, out_sel, preferred_element_type=jnp.float32
    ).astype(jnp.bfloat16)
    d_mixed_heads = heads(d_mixed)
    d_value = jnp.einsum(
        "schqk,scqhd->sckhd", probs_low, d_mixed_heads, preferred_element_type=jnp.float32
    )
    d_value = d_value.reshape(n_seg, seg_rows, -1).astype(jnp.bfloat16)
    d_probs = jnp.einsum(
        "scqhd,sckhd->schqk", d_mixed_heads, heads(value_rows), preferred_element_type=jnp.float32
    )
    prob_dot = jnp.sum(attn_probs * d_probs, axis=-1, keepdims=True)
    d_scores = (attn_probs * (d_probs - prob_dot)).astype(jnp.bfloat16)
    d_query = (
        jnp.einsum(
            "schqk,sckhd->scqhd", d_scores, heads(key_rows), preferred_element_type=jnp.float32
        )
        * score_scale
    )
    d_key = (
        jnp.einsum(
            "schqk,scqhd->sckhd", d_scores, heads(query_rows), preferred_element_type=jnp.float32
        )
        * score_scale
    )
    d_query = d_query.reshape(n_seg, seg_rows, -1).astype(jnp.bfloat16)
    d_key = d_key.reshape(n_seg, seg_rows, -1).astype(jnp.bfloat16)
    d_proj = jnp.stack([d_query, d_key, d_value])
    grad_qkv = jnp.einsum(
        "strd,jsre->tjed", masked(input_segs, seg_hot), d_proj, preferred_element_type=jnp.float32
    )
    grad_qv = jnp.stack(
        [
            kind_sums(seg_hot, jnp.sum(d_query.astype(jnp.float32), axis=1)),
            kind_sums(seg_hot, jnp.sum(d_value.astype(jnp.float32), axis=1)),
        ],
        axis=1,
    )
    qkv_back = jnp.einsum("jsre,sjde->srd", d_proj, qkv_sel, preferred_element_type=jnp.float32)
    input_grad = scatter_sum(qkv_back) + d_one
    small = jnp.stack([rbias_grads, gain_grads, shift_grads])
    return (
        layer_out,
        input_grad,
        (grad_qkv, grad_qv, grad_out_w, grad_up, grad_ubias, grad_down),
        small,
        qkv_back,
    )


def local(
    inputs,
    cotangent,
    lengths,
    block_kind,
    w_qkv,
    qv_bias,
    w_out,
    resid_bias,
    norm_gain,
    norm_shift,
    w_up,
    up_bias,
    w_down,
):
    tok_dev = inputs.shape[0]
    n_tensor = lax.axis_size("tensor")
    rank = lax.axis_index("tensor")
    block_rows = BLOCK_SEQS * CHAIN
    assert block_rows % tok_dev == 0
    dev_chains = tok_dev // CHAIN
    chains = dev_chains // STREAMS
    seg_rows = chains * CHAIN
    weights = (w_qkv, qv_bias, w_out, resid_bias, norm_gain, norm_shift, w_up, up_bias, w_down)
    peer_kind = block_kind[(jnp.arange(n_tensor) * tok_dev) // block_rows]
    out_rows_w = lax.all_to_all(w_out[peer_kind], "tensor", 0, 0, tiled=True)
    outs, ins, grads, smalls = [], [], [], []
    mark = None
    for part in range(STREAMS):
        first_row = jnp.arange(n_tensor) * tok_dev + part * seg_rows
        seg_kind = block_kind[first_row // block_rows]
        chain_ids = (
            jnp.arange(n_tensor)[:, None] * dev_chains + part * chains + jnp.arange(chains)[None, :]
        )
        seg_lens = lengths[chain_ids]
        own_rows = rank * tok_dev + part * seg_rows + jnp.arange(seg_rows)
        row_kind = block_kind[own_rows // block_rows]
        rows = slice(part * seg_rows, (part + 1) * seg_rows)
        out_part, in_part, grad_part, small_part, mark = stream(
            inputs[rows], mark, cotangent[rows], seg_kind, seg_lens, row_kind, out_rows_w, *weights
        )
        outs.append(out_part)
        ins.append(in_part)
        grads.append(grad_part)
        smalls.append(small_part)
    layer_out = jnp.concatenate(outs, axis=0)
    input_grad = jnp.concatenate(ins, axis=0)
    grad_qkv, grad_qv, grad_out_w, grad_up, grad_ubias, grad_down = (
        sum(parts[1:], parts[0]) for parts in zip(*grads)
    )
    small = sum(smalls[1:], smalls[0])
    up_total, down_total = dp_sum_low((grad_up, grad_down))
    qkv_t_total, out_total = dp_sum_low((grad_qkv, grad_out_w))
    qkv_total = jnp.swapaxes(qkv_t_total, 2, 3)
    (small_grads,) = exact_sum((small,), "tensor")
    width = small.shape[-1]
    packed = jnp.concatenate(
        [small_grads.reshape(-1, width), grad_ubias.reshape(-1, width), grad_qv.reshape(-1, width)]
    )
    (packed,) = exact_sum((packed,), "dp")
    n_small, n_ubias = small_grads.size // width, grad_ubias.size // width
    small_total = packed[:n_small].reshape(small_grads.shape)
    ubias_total = packed[n_small : n_small + n_ubias].reshape(grad_ubias.shape)
    qv_total = packed[n_small + n_ubias :].reshape(grad_qv.shape)
    return (
        layer_out,
        input_grad,
        qkv_total,
        qv_total,
        out_total,
        small_total[0],
        small_total[1],
        small_total[2],
        up_total,
        ubias_total,
        down_total,
    )


def solution(mesh):
    return jax.shard_map(
        local,
        mesh=mesh,
        in_specs=(
            P(("dp", "tensor"), None),
            P(("dp", "tensor"), None),
            P("dp"),
            P("dp"),
            P(None, None, None, "tensor"),
            P(None, None, "tensor"),
            P(None, "tensor", None),
            P(),
            P(),
            P(),
            P(None, None, "tensor"),
            P(None, "tensor"),
            P(None, "tensor", None),
        ),
        out_specs=(
            P(("dp", "tensor"), None),
            P(("dp", "tensor"), None),
            P(None, None, None, "tensor"),
            P(None, None, "tensor"),
            P(None, "tensor", None),
            P(),
            P(),
            P(),
            P(None, None, "tensor"),
            P(None, "tensor"),
            P(None, "tensor", None),
        ),
        check_vma=False,
    )
```
